128 devices in a mesh: tm: 16 (over z, y_lo, core), head: 8 (over y_hi, x).
Axes of the slice: x: 4, y: 4 (y_hi: 2, y_lo: 2; y = y_hi * 2 + y_lo), z: 4, core: 2. Of those that a mesh axis runs over, the one named last changes fastest.
Arguments:
- queries: bfloat16 [16384, 768], P(('tm', 'head')), may hold values from -64 to 64
- keys: bfloat16 [16384, 768], P(('tm', 'head')), may hold values from -4 to 4
- values: bfloat16 [16384, 768], P(('tm', 'head')), may hold values from -6 to 6
- grad_out: bfloat16 [16384, 768], P(('tm', 'head')), may hold values from -6 to 6
- frame_counts: int32 [4], replicated, may hold values from 1 to 8192, 16384 in all
Outputs:
- attended: bfloat16 [16384, 768], P(('tm', 'head'))
- grad_queries: bfloat16 [16384, 768], P(('tm', 'head'))
- grad_keys: bfloat16 [16384, 768], P(('tm', 'head'))
- grad_values: bfloat16 [16384, 768], P(('tm', 'head'))
The draws below stay inside these ranges and needn't reach their ends.
All inputs are finite; a program needn't handle non-finite values.
Results may differ from the reference program's by a relative error of at most 0.029.
Values may be sent and summed in bfloat16 or wider, within the bound.
No kernel may reach another device: no remote copies, remote signals or barrier semaphores. Data moves between devices by JAX's collectives and lax.ppermute only.
A program may use at most 64 MiB of HBM per device.

```python
import math
import jax
import jax.numpy as jnp
import numpy as np
from jax import lax

HEADS = 8
DH = 96
NUTT = 4
TOTAL = 16384
MOST = 8192


def paired_draw(key):
    base = jax.random.fold_in(key, 11)
    key_query, key_keys = jax.random.split(base, 2)
    shape = (TOTAL, HEADS * DH)
    query = jnp.clip(3.0 * jax.random.normal(key_query, shape, jnp.float32), -18.0, 18.0)
    keyset = jnp.clip(jax.random.normal(key_keys, shape, jnp.float32), -4.0, 4.0)
    return (query, keyset)


def draw_queries(key, part):
    return paired_draw(key)[0].astype(jnp.bfloat16)


def draw_keys(key, part):
    return paired_draw(key)[1].astype(jnp.bfloat16)


def shard_levels(own_key, extent, pieces, least, top_value):
    factor_of, own = 1.0, jax.random.fold_in(own_key, 6)
    for position, parts in pieces:
        steps = jnp.exp(jax.random.uniform(jax.random.fold_in(own, position), (parts,), jnp.float32, least / len(pieces), top_value / len(pieces)))
        factor_of = factor_of * jnp.repeat(steps, extent[position] // parts).reshape([-1 if axis == position else 1 for axis in range(len(extent))])
    return factor_of


def profile(count, total, limit, slope):
    weights = [(1 << 20) // math.isqrt(standing ** slope) + 1 for standing in range(2, count + 1)]
    spare, given = total - limit - (count - 1), [1] * (count - 1)
    while spare > 0:
        free = [i for i in range(count - 1) if given[i] < limit]
        mass, left = sum([weights[i] for i in free]), spare
        for i in free:
            extra = min(limit - given[i], max(1, left * weights[i] // mass), spare)
            given[i] = given[i] + extra
            spare = spare - extra
    return np.array([limit] + given)


def ragged(rng, amount, total, most, slope):
    if amount == 2:
        one = jax.random.randint(rng, (), max(1, total - most), min(most, total - 1) + 1)
        return jnp.stack([one, total - one])
    tallies = jnp.asarray(profile(amount, total, most, slope), jnp.int32)
    pairs = (amount - 1) // 2
    giver, sink = tallies[1:1 + 2 * pairs:2], tallies[2:2 + 2 * pairs:2]
    room = jnp.minimum(giver - 1, most - sink)
    moved = jax.random.randint(jax.random.fold_in(rng, 1), (pairs,), 0, 1 << 20) % (room + 1)
    tallies = tallies.at[1:1 + 2 * pairs:2].set(giver - moved).at[2:2 + 2 * pairs:2].set(sink + moved)
    return tallies[jax.random.permutation(jax.random.fold_in(rng, 2), amount)]


def normal_values(stream_key, shape, width, most, cuts=(), held_as=jnp.bfloat16):
    entries = width * jax.random.normal(stream_key, shape, jnp.float32)
    if cuts:
        entries = entries * shard_levels(stream_key, shape, cuts, -0.22, 0.18)
    return jnp.clip(entries, -most, most).astype(held_as)


def setup_inputs(seed: int = 0) -> dict:
    seeds = jax.random.split(jax.random.key(seed), 6)
    return {
        "queries": draw_queries(jax.random.fold_in(seeds[5], 71), 0),
        "keys": draw_keys(jax.random.fold_in(seeds[5], 71), 0),
        "values": normal_values(seeds[2], (TOTAL, HEADS * DH), 1.0, 6.0, ((0, 128),)),
        "grad_out": normal_values(seeds[3], (TOTAL, HEADS * DH), 1.0, 6.0, ((0, 128),)),
        "frame_counts": ragged(seeds[4], NUTT, TOTAL, MOST, 2).astype(jnp.int32),
    }


def segment_of(index, bounds):
    return lax.optimization_barrier(jnp.sum((index[:, None] >= bounds[None, :]).astype(jnp.int32), axis=1))

def reference(queries, keys, values, grad_out, frame_counts):
    scale = 1.0 / math.sqrt(DH)
    bounds = jnp.cumsum(frame_counts).astype(jnp.int32)[:NUTT - 1]
    seg_all = segment_of(jnp.arange(TOTAL, dtype=jnp.int32), bounds)
    block = math.gcd(TOTAL, 1024)
    nblocks = TOTAL // block

    def split_heads(array):
        return array.reshape(TOTAL, HEADS, DH).transpose(1, 0, 2)

    def one_head(arrays):
        query_h, key_h, value_h, grad_h = arrays

        def step(carry, index):
            acc_keys, acc_values = carry
            start = (index * block).astype(jnp.int32)
            query_blk = lax.dynamic_slice_in_dim(query_h, start, block, 0)
            grad_blk = lax.dynamic_slice_in_dim(grad_h, start, block, 0)
            seg_blk = lax.dynamic_slice_in_dim(seg_all, start, block, 0)
            visible = seg_blk[:, None] == seg_all[None, :]
            scores = jnp.dot(query_blk, key_h.T, preferred_element_type=jnp.float32) * scale
            top = lax.optimization_barrier(jnp.max(jnp.where(visible, scores, -1e+30), axis=1))
            forward_low = jnp.where(visible, jnp.exp(scores - top[:, None]), 0.0)
            total = lax.optimization_barrier(jnp.sum(forward_low, axis=1))
            log_total = top + jnp.log(total)
            forward_low = forward_low.astype(jnp.bfloat16)
            attended = (jnp.dot(forward_low, value_h, preferred_element_type=jnp.float32) / total[:, None]).astype(jnp.bfloat16)
            weights = jnp.where(visible, jnp.exp(scores - log_total[:, None]), 0.0)
            weights_low = weights.astype(jnp.bfloat16)
            delta = lax.optimization_barrier(jnp.sum(grad_blk.astype(jnp.float32) * attended.astype(jnp.float32), axis=1))
            dprod = jnp.dot(grad_blk, value_h.T, preferred_element_type=jnp.float32)
            dscore = (weights * (dprod - delta[:, None])).astype(jnp.bfloat16)
            grad_q = (scale * jnp.dot(dscore, key_h, preferred_element_type=jnp.float32)).astype(jnp.bfloat16)
            acc_keys = acc_keys + jnp.dot(dscore.T, query_blk, preferred_element_type=jnp.float32)
            acc_values = acc_values + jnp.dot(weights_low.T, grad_blk, preferred_element_type=jnp.float32)
            return ((acc_keys, acc_values), (attended, grad_q))
        zeros = jnp.zeros((TOTAL, DH), jnp.float32)
        (acc_keys, acc_values), (attended, grad_q) = lax.scan(step, (zeros, zeros), jnp.arange(nblocks, dtype=jnp.int32))
        return (attended.reshape(TOTAL, DH), grad_q.reshape(TOTAL, DH), (scale * acc_keys).astype(jnp.bfloat16), acc_values.astype(jnp.bfloat16))
    results = lax.map(one_head, (split_heads(queries), split_heads(keys), split_heads(values), split_heads(grad_out)))

    def join_heads(array):
        return array.transpose(1, 0, 2).reshape(TOTAL, HEADS * DH)
    return (join_heads(results[0]), join_heads(results[1]), join_heads(results[2]), join_heads(results[3]))
```

```python
import math

import jax
import jax.numpy as jnp
from jax import lax
from jax.experimental import pallas as pl
from jax.experimental.pallas import tpu as pltpu
from jax.sharding import PartitionSpec as P

HEADS = 8
DH = 96
KBLOCK = 512
NEG = -1e30


def segment_of(index, bounds):
    return jnp.sum((index[:, None] >= bounds[None, :]).astype(jnp.int32), axis=1)


def fwd_kernel(rng_ref, segq_ref, q_ref, k_ref, v_ref, g_ref, segk_ref,
               att_ref, lse_ref, delta_ref, m_sc, l_sc, acc_sc, *, scale):
    j = pl.program_id(0)
    lo = rng_ref[0]
    hi = rng_ref[1]

    @pl.when(j == 0)
    def _():
        m_sc[...] = jnp.full(m_sc.shape, NEG, jnp.float32)
        l_sc[...] = jnp.zeros(l_sc.shape, jnp.float32)
        acc_sc[...] = jnp.zeros(acc_sc.shape, jnp.float32)

    @pl.when(lo + j <= hi)
    def _():
        s = lax.dot_general(q_ref[...], k_ref[...], (((1,), (1,)), ((), ())),
                            preferred_element_type=jnp.float32) * scale
        vis = segq_ref[...] == segk_ref[...]
        m_prev = m_sc[...]
        m_new = jnp.maximum(m_prev, jnp.max(jnp.where(vis, s, NEG), axis=1, keepdims=True))
        alpha = jnp.exp(m_prev - m_new)
        p = jnp.where(vis, jnp.exp(s - m_new), 0.0)
        l_sc[...] = l_sc[...] * alpha + jnp.sum(p, axis=1, keepdims=True)
        acc_sc[...] = acc_sc[...] * alpha + jnp.dot(
            p.astype(jnp.bfloat16), v_ref[...], preferred_element_type=jnp.float32)
        m_sc[...] = m_new

    @pl.when(j == pl.num_programs(0) - 1)
    def _():
        total = l_sc[...]
        att = (acc_sc[...] / total).astype(jnp.bfloat16)
        att_ref[...] = att
        lse_ref[...] = m_sc[...] + jnp.log(total)
        delta_ref[...] = jnp.sum(g_ref[...].astype(jnp.float32) * att.astype(jnp.float32),
                                 axis=1, keepdims=True)


def bwd_kernel(rng_ref, segq_ref, q_ref, g_ref, lse_ref, delta_ref, k_ref, v_ref, segk_ref,
               dq_ref, dk_ref, dv_ref, dq_sc, *, scale):
    j = pl.program_id(0)
    lo = rng_ref[0]
    hi = rng_ref[1]
    active = jnp.logical_and(j >= lo, j <= hi)

    @pl.when(j == 0)
    def _():
        dq_sc[...] = jnp.zeros(dq_sc.shape, jnp.float32)

    @pl.when(active)
    def _():
        q = q_ref[...]
        g = g_ref[...]
        k = k_ref[...]
        s = lax.dot_general(q, k, (((1,), (1,)), ((), ())),
                            preferred_element_type=jnp.float32) * scale
        vis = segq_ref[...] == segk_ref[...]
        w = jnp.where(vis, jnp.exp(s - lse_ref[...]), 0.0)
        dp = lax.dot_general(g, v_ref[...], (((1,), (1,)), ((), ())),
                             preferred_element_type=jnp.float32)
        ds = (w * (dp - delta_ref[...])).astype(jnp.bfloat16)
        dq_sc[...] += jnp.dot(ds, k, preferred_element_type=jnp.float32)
        dk_ref[...] = lax.dot_general(ds, q, (((0,), (0,)), ((), ())),
                                      preferred_element_type=jnp.float32).astype(jnp.bfloat16)
        dv_ref[...] = lax.dot_general(w.astype(jnp.bfloat16), g, (((0,), (0,)), ((), ())),
                                      preferred_element_type=jnp.float32).astype(jnp.bfloat16)

    @pl.when(jnp.logical_not(active))
    def _():
        dk_ref[...] = jnp.zeros(dk_ref.shape, dk_ref.dtype)
        dv_ref[...] = jnp.zeros(dv_ref.shape, dv_ref.dtype)

    @pl.when(j == pl.num_programs(0) - 1)
    def _():
        dq_ref[...] = (scale * dq_sc[...]).astype(jnp.bfloat16)


def attention_head(rng, segq, segk, q, k, v, g, scale):
    rows = q.shape[0]
    nkeys = k.shape[0]
    nk = nkeys // KBLOCK
    full = lambda j, r: (0, 0)
    kmap_f = lambda j, r: (jnp.minimum(r[0] + j, r[1]), 0)
    skmap_f = lambda j, r: (0, jnp.minimum(r[0] + j, r[1]))
    fwd = pl.pallas_call(
        lambda *refs: fwd_kernel(*refs, scale=scale),
        grid_spec=pltpu.PrefetchScalarGridSpec(
            num_scalar_prefetch=1,
            grid=(nk,),
            in_specs=[
                pl.BlockSpec((rows, 1), full),
                pl.BlockSpec((rows, DH), full),
                pl.BlockSpec((KBLOCK, DH), kmap_f),
                pl.BlockSpec((KBLOCK, DH), kmap_f),
                pl.BlockSpec((rows, DH), full),
                pl.BlockSpec((1, KBLOCK), skmap_f),
            ],
            out_specs=[
                pl.BlockSpec((rows, DH), full),
                pl.BlockSpec((rows, 1), full),
                pl.BlockSpec((rows, 1), full),
            ],
            scratch_shapes=[
                pltpu.VMEM((rows, 1), jnp.float32),
                pltpu.VMEM((rows, 1), jnp.float32),
                pltpu.VMEM((rows, DH), jnp.float32),
            ],
        ),
        out_shape=[
            jax.ShapeDtypeStruct((rows, DH), jnp.bfloat16),
            jax.ShapeDtypeStruct((rows, 1), jnp.float32),
            jax.ShapeDtypeStruct((rows, 1), jnp.float32),
        ],
        compiler_params=pltpu.CompilerParams(dimension_semantics=("arbitrary",)),
    )
    att, lse, delta = fwd(rng, segq, q, k, v, g, segk)

    kmap_b = lambda j, r: (jnp.minimum(jnp.maximum(j, r[0]), r[1]), 0)
    skmap_b = lambda j, r: (0, jnp.minimum(jnp.maximum(j, r[0]), r[1]))
    omap = lambda j, r: (j, 0)
    bwd = pl.pallas_call(
        lambda *refs: bwd_kernel(*refs, scale=scale),
        grid_spec=pltpu.PrefetchScalarGridSpec(
            num_scalar_prefetch=1,
            grid=(nk,),
            in_specs=[
                pl.BlockSpec((rows, 1), full),
                pl.BlockSpec((rows, DH), full),
                pl.BlockSpec((rows, DH), full),
                pl.BlockSpec((rows, 1), full),
                pl.BlockSpec((rows, 1), full),
                pl.BlockSpec((KBLOCK, DH), kmap_b),
                pl.BlockSpec((KBLOCK, DH), kmap_b),
                pl.BlockSpec((1, KBLOCK), skmap_b),
            ],
            out_specs=[
                pl.BlockSpec((rows, DH), full),
                pl.BlockSpec((KBLOCK, DH), omap),
                pl.BlockSpec((KBLOCK, DH), omap),
            ],
            scratch_shapes=[pltpu.VMEM((rows, DH), jnp.float32)],
        ),
        out_shape=[
            jax.ShapeDtypeStruct((rows, DH), jnp.bfloat16),
            jax.ShapeDtypeStruct((nkeys, DH), jnp.bfloat16),
            jax.ShapeDtypeStruct((nkeys, DH), jnp.bfloat16),
        ],
        compiler_params=pltpu.CompilerParams(dimension_semantics=("arbitrary",)),
    )
    dq, dk, dv = bwd(rng, segq, q, g, lse, delta, k, v, segk)
    return att, dq, dk, dv


def body(queries, keys, values, grad_out, frame_counts):
    heads_here = HEADS // lax.axis_size("head")
    scale = 1.0 / math.sqrt(DH)
    own_q, own_k, own_v, own_g = (
        lax.all_to_all(queries, "head", split_axis=1, concat_axis=0, tiled=True),
        lax.all_to_all(keys, "head", split_axis=1, concat_axis=0, tiled=True),
        lax.all_to_all(values, "head", split_axis=1, concat_axis=0, tiled=True),
        lax.all_to_all(grad_out, "head", split_axis=1, concat_axis=0, tiled=True),
    )
    rows = own_q.shape[0]
    all_k, all_v = (
        lax.all_gather(own_k, "tm", axis=0, tiled=True),
        lax.all_gather(own_v, "tm", axis=0, tiled=True),
    )
    nkeys = all_k.shape[0]
    nk = nkeys // KBLOCK
    bounds = jnp.cumsum(frame_counts)[:-1].astype(jnp.int32)
    offset = lax.axis_index("tm") * rows
    seg_own = segment_of(offset + jnp.arange(rows, dtype=jnp.int32), bounds)
    seg_keys = segment_of(jnp.arange(nkeys, dtype=jnp.int32), bounds)
    starts = jnp.concatenate([jnp.zeros((1,), jnp.int32), bounds])
    ends = jnp.concatenate([bounds, jnp.full((1,), nkeys, jnp.int32)])
    kstart = starts[seg_own[0]]
    kend = ends[seg_own[rows - 1]]
    rng = jnp.clip(jnp.stack([kstart // KBLOCK, (kend - 1) // KBLOCK]), 0, nk - 1).astype(jnp.int32)
    segq = seg_own.reshape(rows, 1)
    segk = seg_keys.reshape(1, nkeys)

    atts, dqs, dks, dvs = [], [], [], []
    for h in range(heads_here):
        cols = slice(h * DH, (h + 1) * DH)
        att, dq, dk, dv = attention_head(
            rng, segq, segk, own_q[:, cols], all_k[:, cols], all_v[:, cols], own_g[:, cols], scale)
        atts.append(att)
        dqs.append(dq)
        dks.append(dk)
        dvs.append(dv)
    attended_flat = jnp.concatenate(atts, axis=1)
    grad_q = jnp.concatenate(dqs, axis=1)
    key_terms = jnp.concatenate(dks, axis=1)
    value_terms = jnp.concatenate(dvs, axis=1)
    dk_sum, dv_sum = (
        lax.psum_scatter(key_terms, "tm", scatter_dimension=0, tiled=True).astype(jnp.float32),
        lax.psum_scatter(value_terms, "tm", scatter_dimension=0, tiled=True).astype(jnp.float32),
    )
    grad_k = (scale * dk_sum).astype(jnp.bfloat16)
    grad_v = dv_sum.astype(jnp.bfloat16)
    return (
        lax.all_to_all(attended_flat, "head", split_axis=0, concat_axis=1, tiled=True),
        lax.all_to_all(grad_q, "head", split_axis=0, concat_axis=1, tiled=True),
        lax.all_to_all(grad_k, "head", split_axis=0, concat_axis=1, tiled=True),
        lax.all_to_all(grad_v, "head", split_axis=0, concat_axis=1, tiled=True),
    )


def solution(mesh):
    placed = (
        P(("tm", "head"), None),
        P(("tm", "head"), None),
        P(("tm", "head"), None),
        P(("tm", "head"), None),
        P(),
    )
    return jax.shard_map(
        body,
        mesh=mesh,
        in_specs=placed,
        out_specs=(
            P(("tm", "head"), None),
            P(("tm", "head"), None),
            P(("tm", "head"), None),
            P(("tm", "head"), None),
        ),
        check_vma=False,
    )
```

```python
import math

import jax
import jax.numpy as jnp
from jax import lax
from jax.experimental import pallas as pl
from jax.experimental.pallas import tpu as pltpu
from jax.sharding import PartitionSpec as P

HEADS = 8
DH = 96
KBLOCK = 512
NEG = -1e30


def segment_of(index, bounds):
    return jnp.sum((index[:, None] >= bounds[None, :]).astype(jnp.int32), axis=1)


def fwd_kernel(rng_ref, segq_ref, q_ref, k_ref, v_ref, g_ref, segk_ref,
               att_ref, lse_ref, delta_ref, m_sc, l_sc, acc_sc, *, scale):
    j = pl.program_id(0)
    lo = rng_ref[0]
    hi = rng_ref[1]

    @pl.when(j == 0)
    def _():
        m_sc[...] = jnp.full(m_sc.shape, NEG, jnp.float32)
        l_sc[...] = jnp.zeros(l_sc.shape, jnp.float32)
        acc_sc[...] = jnp.zeros(acc_sc.shape, jnp.float32)

    @pl.when(lo + j <= hi)
    def _():
        s = lax.dot_general(q_ref[...], k_ref[...], (((1,), (1,)), ((), ())),
                            preferred_element_type=jnp.float32) * scale
        vis = segq_ref[...] == segk_ref[...]
        m_prev = m_sc[...]
        m_new = jnp.maximum(m_prev, jnp.max(jnp.where(vis, s, NEG), axis=1, keepdims=True))
        alpha = jnp.exp(m_prev - m_new)
        p = jnp.where(vis, jnp.exp(s - m_new), 0.0)
        l_sc[...] = l_sc[...] * alpha + jnp.sum(p, axis=1, keepdims=True)
        acc_sc[...] = acc_sc[...] * alpha + jnp.dot(
            p.astype(jnp.bfloat16), v_ref[...], preferred_element_type=jnp.float32)
        m_sc[...] = m_new

    @pl.when(j == pl.num_programs(0) - 1)
    def _():
        total = l_sc[...]
        att = (acc_sc[...] / total).astype(jnp.bfloat16)
        att_ref[...] = att
        lse_ref[...] = m_sc[...] + jnp.log(total)
        delta_ref[...] = jnp.sum(g_ref[...].astype(jnp.float32) * att.astype(jnp.float32),
                                 axis=1, keepdims=True)


def dq_kernel(rng_ref, segq_ref, q_ref, g_ref, lse_ref, delta_ref, k_ref, v_ref, segk_ref,
              dq_ref, dq_sc, *, scale):
    j = pl.program_id(0)
    lo = rng_ref[0]
    hi = rng_ref[1]

    @pl.when(j == 0)
    def _():
        dq_sc[...] = jnp.zeros(dq_sc.shape, jnp.float32)

    @pl.when(lo + j <= hi)
    def _():
        k = k_ref[...]
        s = lax.dot_general(q_ref[...], k, (((1,), (1,)), ((), ())),
                            preferred_element_type=jnp.float32) * scale
        vis = segq_ref[...] == segk_ref[...]
        w = jnp.where(vis, jnp.exp(s - lse_ref[...]), 0.0)
        dp = lax.dot_general(g_ref[...], v_ref[...], (((1,), (1,)), ((), ())),
                             preferred_element_type=jnp.float32)
        ds = (w * (dp - delta_ref[...])).astype(jnp.bfloat16)
        dq_sc[...] += jnp.dot(ds, k, preferred_element_type=jnp.float32)

    @pl.when(j == pl.num_programs(0) - 1)
    def _():
        dq_ref[...] = (scale * dq_sc[...]).astype(jnp.bfloat16)


def dkv_kernel(rng_ref, segk_own_ref, k_ref, v_ref, q_ref, g_ref, lse_ref, delta_ref, segq_ref,
               dk_ref, dv_ref, dk_sc, dv_sc, *, scale):
    i = pl.program_id(0)
    lo = rng_ref[0]
    hi = rng_ref[1]

    @pl.when(i == 0)
    def _():
        dk_sc[...] = jnp.zeros(dk_sc.shape, jnp.float32)
        dv_sc[...] = jnp.zeros(dv_sc.shape, jnp.float32)

    @pl.when(lo + i <= hi)
    def _():
        q = q_ref[...]
        g = g_ref[...]
        st = lax.dot_general(k_ref[...], q, (((1,), (1,)), ((), ())),
                             preferred_element_type=jnp.float32) * scale
        vis = segk_own_ref[...] == segq_ref[...]
        wt = jnp.where(vis, jnp.exp(st - lse_ref[...]), 0.0)
        dpt = lax.dot_general(v_ref[...], g, (((1,), (1,)), ((), ())),
                              preferred_element_type=jnp.float32)
        dst = (wt * (dpt - delta_ref[...])).astype(jnp.bfloat16)
        dk_sc[...] += jnp.dot(dst, q, preferred_element_type=jnp.float32)
        dv_sc[...] += jnp.dot(wt.astype(jnp.bfloat16), g, preferred_element_type=jnp.float32)

    @pl.when(i == pl.num_programs(0) - 1)
    def _():
        dk_ref[...] = (scale * dk_sc[...]).astype(jnp.bfloat16)
        dv_ref[...] = dv_sc[...].astype(jnp.bfloat16)


def block_call(kernel, rng, fixed, streamed, outs, scratch, nblocks):
    full = lambda j, r: (0, 0)
    rowmap = lambda j, r: (jnp.minimum(r[0] + j, r[1]), 0)
    colmap = lambda j, r: (0, jnp.minimum(r[0] + j, r[1]))
    in_specs = [pl.BlockSpec(a.shape, full) for a in fixed]
    for a, blk, by_row in streamed:
        in_specs.append(pl.BlockSpec(blk, rowmap if by_row else colmap))
    return pl.pallas_call(
        kernel,
        grid_spec=pltpu.PrefetchScalarGridSpec(
            num_scalar_prefetch=1,
            grid=(nblocks,),
            in_specs=in_specs,
            out_specs=[pl.BlockSpec(o.shape, full) for o in outs],
            scratch_shapes=scratch,
        ),
        out_shape=outs,
        compiler_params=pltpu.CompilerParams(dimension_semantics=("arbitrary",)),
    )(rng, *fixed, *[a for a, _, _ in streamed])


def body(queries, keys, values, grad_out, frame_counts):
    n_head = lax.axis_size("head")
    heads_here = HEADS // n_head
    scale = 1.0 / math.sqrt(DH)
    rows_in = queries.shape[0]
    stacked = jnp.stack(
        [a.reshape(rows_in, HEADS, DH) for a in (queries, keys, values, grad_out)], axis=2
    ).reshape(rows_in, HEADS * 4 * DH)
    mine = lax.all_to_all(stacked, "head", split_axis=1, concat_axis=0, tiled=True)
    rows = mine.shape[0]
    mine = mine.reshape(rows, heads_here, 4, DH)
    nkeys = rows * lax.axis_size("tm")
    nk = nkeys // KBLOCK
    bounds = jnp.cumsum(frame_counts)[:-1].astype(jnp.int32)
    offset = lax.axis_index("tm") * rows
    seg_own = segment_of(offset + jnp.arange(rows, dtype=jnp.int32), bounds)
    seg_keys = segment_of(jnp.arange(nkeys, dtype=jnp.int32), bounds)
    starts = jnp.concatenate([jnp.zeros((1,), jnp.int32), bounds])
    ends = jnp.concatenate([bounds, jnp.full((1,), nkeys, jnp.int32)])
    kstart = starts[seg_own[0]]
    kend = ends[seg_own[rows - 1]]
    rng = jnp.clip(jnp.stack([kstart // KBLOCK, (kend - 1) // KBLOCK]), 0, nk - 1).astype(jnp.int32)
    segq = seg_own.reshape(rows, 1)
    segk = seg_keys.reshape(1, nkeys)
    f32 = jnp.float32
    bf16 = jnp.bfloat16

    outs_a, outs_b = [], []
    for h in range(heads_here):
        own_q, own_k, own_v, own_g = (mine[:, h, c, :] for c in range(4))
        all_k = lax.all_gather(own_k, "tm", axis=0, tiled=True)
        all_v = lax.all_gather(own_v, "tm", axis=0, tiled=True)
        all_q = lax.all_gather(own_q, "tm", axis=0, tiled=True)
        all_g = lax.all_gather(own_g, "tm", axis=0, tiled=True)
        att, lse, delta = fwd_call(rng, segq, own_q, all_k, all_v, own_g, segk, scale, nk)
        (dq,) = block_call(
            lambda *refs: dq_kernel(*refs, scale=scale), rng,
            [segq, own_q, own_g, lse, delta],
            [(all_k, (KBLOCK, DH), True), (all_v, (KBLOCK, DH), True), (segk, (1, KBLOCK), False)],
            [jax.ShapeDtypeStruct((rows, DH), bf16)],
            [pltpu.VMEM((rows, DH), f32)],
            nk,
        )
        all_lse = lax.all_gather(lse.reshape(1, rows), "tm", axis=1, tiled=True)
        all_delta = lax.all_gather(delta.reshape(1, rows), "tm", axis=1, tiled=True)
        dk, dv = block_call(
            lambda *refs: dkv_kernel(*refs, scale=scale), rng,
            [segq, own_k, own_v],
            [(all_q, (KBLOCK, DH), True), (all_g, (KBLOCK, DH), True),
             (all_lse, (1, KBLOCK), False), (all_delta, (1, KBLOCK), False),
             (segk, (1, KBLOCK), False)],
            [jax.ShapeDtypeStruct((rows, DH), bf16), jax.ShapeDtypeStruct((rows, DH), bf16)],
            [pltpu.VMEM((rows, DH), f32), pltpu.VMEM((rows, DH), f32)],
            nk,
        )
        outs_a.append(jnp.stack([att, dq], axis=1))
        outs_b.append(jnp.stack([dk, dv], axis=1))

    def send_back(parts):
        packed = jnp.stack(parts, axis=1).reshape(rows, heads_here * 2 * DH)
        back = lax.all_to_all(packed, "head", split_axis=0, concat_axis=1, tiled=True)
        back = back.reshape(rows_in, HEADS, 2, DH)
        return back[:, :, 0, :].reshape(rows_in, HEADS * DH), back[:, :, 1, :].reshape(rows_in, HEADS * DH)

    attended, grad_q = send_back(outs_a)
    grad_k, grad_v = send_back(outs_b)
    return attended, grad_q, grad_k, grad_v


def fwd_call(rng, segq, q, k, v, g, segk, scale, nk):
    rows = q.shape[0]
    f32 = jnp.float32
    full = lambda j, r: (0, 0)
    kmap = lambda j, r: (jnp.minimum(r[0] + j, r[1]), 0)
    skmap = lambda j, r: (0, jnp.minimum(r[0] + j, r[1]))
    return pl.pallas_call(
        lambda *refs: fwd_kernel(*refs, scale=scale),
        grid_spec=pltpu.PrefetchScalarGridSpec(
            num_scalar_prefetch=1,
            grid=(nk,),
            in_specs=[
                pl.BlockSpec((rows, 1), full),
                pl.BlockSpec((rows, DH), full),
                pl.BlockSpec((KBLOCK, DH), kmap),
                pl.BlockSpec((KBLOCK, DH), kmap),
                pl.BlockSpec((rows, DH), full),
                pl.BlockSpec((1, KBLOCK), skmap),
            ],
            out_specs=[
                pl.BlockSpec((rows, DH), full),
                pl.BlockSpec((rows, 1), full),
                pl.BlockSpec((rows, 1), full),
            ],
            scratch_shapes=[
                pltpu.VMEM((rows, 1), f32),
                pltpu.VMEM((rows, 1), f32),
                pltpu.VMEM((rows, DH), f32),
            ],
        ),
        out_shape=[
            jax.ShapeDtypeStruct((rows, DH), jnp.bfloat16),
            jax.ShapeDtypeStruct((rows, 1), f32),
            jax.ShapeDtypeStruct((rows, 1), f32),
        ],
        compiler_params=pltpu.CompilerParams(dimension_semantics=("arbitrary",)),
    )(rng, segq, q, k, v, g, segk)


def solution(mesh):
    placed = (
        P(("tm", "head"), None),
        P(("tm", "head"), None),
        P(("tm", "head"), None),
        P(("tm", "head"), None),
        P(),
    )
    return jax.shard_map(
        body,
        mesh=mesh,
        in_specs=placed,
        out_specs=(
            P(("tm", "head"), None),
            P(("tm", "head"), None),
            P(("tm", "head"), None),
            P(("tm", "head"), None),
        ),
        check_vma=False,
    )
```

```python
import math

import jax
import jax.numpy as jnp
from jax import lax
from jax.experimental import pallas as pl
from jax.experimental.pallas import tpu as pltpu
from jax.sharding import PartitionSpec as P

HEADS = 8
DH = 96
KBLOCK = 512
NEG = -1e30
NT = (((1,), (1,)), ((), ()))


def segment_of(index, bounds):
    return jnp.sum((index[:, None] >= bounds[None, :]).astype(jnp.int32), axis=1)


def fwd_kernel(rng_ref, segq_ref, q_ref, g_ref, kv_ref, segk_ref,
               att_ref, lse_ref, delta_ref, m_sc, l_sc, acc_sc, *, scale):
    j = pl.program_id(0)
    lo = rng_ref[0]
    hi = rng_ref[1]

    @pl.when(j == 0)
    def _():
        m_sc[...] = jnp.full(m_sc.shape, NEG, jnp.float32)
        l_sc[...] = jnp.zeros(l_sc.shape, jnp.float32)
        acc_sc[...] = jnp.zeros(acc_sc.shape, jnp.float32)

    @pl.when(lo + j <= hi)
    def _():
        s = jnp.dot(q_ref[...], kv_ref[0], preferred_element_type=jnp.float32) * scale
        vis = segq_ref[...] == segk_ref[...]
        m_prev = m_sc[...]
        m_new = jnp.maximum(m_prev, jnp.max(jnp.where(vis, s, NEG), axis=1, keepdims=True))
        alpha = jnp.exp(m_prev - m_new)
        p = jnp.where(vis, jnp.exp(s - m_new), 0.0)
        l_sc[...] = l_sc[...] * alpha + jnp.sum(p, axis=1, keepdims=True)
        acc_sc[...] = acc_sc[...] * alpha + lax.dot_general(
            p.astype(jnp.bfloat16), kv_ref[1], NT, preferred_element_type=jnp.float32)
        m_sc[...] = m_new

    @pl.when(j == pl.num_programs(0) - 1)
    def _():
        total = l_sc[...]
        att = (acc_sc[...] / total).astype(jnp.bfloat16)
        att_ref[...] = att
        lse_ref[...] = m_sc[...] + jnp.log(total)
        delta_ref[...] = jnp.sum(g_ref[...].astype(jnp.float32) * att.astype(jnp.float32),
                                 axis=1, keepdims=True)


def dq_kernel(rng_ref, segq_ref, q_ref, g_ref, lse_ref, delta_ref, kv_ref, segk_ref,
              dq_ref, dq_sc, *, scale):
    j = pl.program_id(0)
    lo = rng_ref[0]
    hi = rng_ref[1]

    @pl.when(j == 0)
    def _():
        dq_sc[...] = jnp.zeros(dq_sc.shape, jnp.float32)

    @pl.when(lo + j <= hi)
    def _():
        kt = kv_ref[0]
        s = jnp.dot(q_ref[...], kt, preferred_element_type=jnp.float32) * scale
        vis = segq_ref[...] == segk_ref[...]
        w = jnp.where(vis, jnp.exp(s - lse_ref[...]), 0.0)
        dp = jnp.dot(g_ref[...], kv_ref[1], preferred_element_type=jnp.float32)
        ds = (w * (dp - delta_ref[...])).astype(jnp.bfloat16)
        dq_sc[...] += lax.dot_general(ds, kt, NT, preferred_element_type=jnp.float32)

    @pl.when(j == pl.num_programs(0) - 1)
    def _():
        dq_ref[...] = (scale * dq_sc[...]).astype(jnp.bfloat16)


def dkv_kernel(rng_ref, segown_ref, k_ref, v_ref, qg_ref, st_ref, segk_ref,
               dk_ref, dv_ref, dk_sc, dv_sc, *, scale):
    i = pl.program_id(0)
    lo = rng_ref[0]
    hi = rng_ref[1]

    @pl.when(i == 0)
    def _():
        dk_sc[...] = jnp.zeros(dk_sc.shape, jnp.float32)
        dv_sc[...] = jnp.zeros(dv_sc.shape, jnp.float32)

    @pl.when(lo + i <= hi)
    def _():
        qt = qg_ref[0]
        gt = qg_ref[1]
        stats = st_ref[...]
        s_t = jnp.dot(k_ref[...], qt, preferred_element_type=jnp.float32) * scale
        vis = segown_ref[...] == segk_ref[...]
        w_t = jnp.where(vis, jnp.exp(s_t - stats[0:1, :]), 0.0)
        dp_t = jnp.dot(v_ref[...], gt, preferred_element_type=jnp.float32)
        ds_t = (w_t * (dp_t - stats[1:2, :])).astype(jnp.bfloat16)
        dk_sc[...] += lax.dot_general(ds_t, qt, NT, preferred_element_type=jnp.float32)
        dv_sc[...] += lax.dot_general(w_t.astype(jnp.bfloat16), gt, NT,
                                      preferred_element_type=jnp.float32)

    @pl.when(i == pl.num_programs(0) - 1)
    def _():
        dk_ref[...] = (scale * dk_sc[...]).astype(jnp.bfloat16)
        dv_ref[...] = dv_sc[...].astype(jnp.bfloat16)


def block_call(kernel, rng, fixed, streamed, outs, scratch, nblocks, per):
    def fixed_map(nd):
        return lambda j, r: (0,) * nd

    def clamp(j, r):
        return jnp.minimum(r[0] + j, r[1])

    def stream_map(nd):
        def index(j, r):
            b = clamp(j, r)
            return (b // per,) + (0,) * (nd - 2) + (b % per,)
        return index

    in_specs = [pl.BlockSpec(a.shape, fixed_map(a.ndim)) for a in fixed]
    for a, blk in streamed:
        in_specs.append(pl.BlockSpec(blk, stream_map(a.ndim)))
    return pl.pallas_call(
        kernel,
        grid_spec=pltpu.PrefetchScalarGridSpec(
            num_scalar_prefetch=1,
            grid=(nblocks,),
            in_specs=in_specs,
            out_specs=[pl.BlockSpec(o.shape, fixed_map(len(o.shape))) for o in outs],
            scratch_shapes=scratch,
        ),
        out_shape=outs,
        compiler_params=pltpu.CompilerParams(dimension_semantics=("arbitrary",)),
    )(rng, *fixed, *[a for a, _ in streamed])


def body(queries, keys, values, grad_out, frame_counts):
    n_head = lax.axis_size("head")
    n_tm = lax.axis_size("tm")
    heads_here = HEADS // n_head
    scale = 1.0 / math.sqrt(DH)
    rows_in = queries.shape[0]
    stacked = jnp.stack(
        [a.reshape(rows_in, HEADS, DH) for a in (queries, keys, values, grad_out)], axis=2
    ).reshape(rows_in, HEADS * 4 * DH)
    mine = lax.all_to_all(stacked, "head", split_axis=1, concat_axis=0, tiled=True)
    rows = mine.shape[0]
    mine = mine.reshape(rows, heads_here, 4, DH)
    per = rows // KBLOCK
    nkeys = rows * n_tm
    nk = nkeys // KBLOCK
    bounds = jnp.cumsum(frame_counts)[:-1].astype(jnp.int32)
    offset = lax.axis_index("tm") * rows
    seg_own = segment_of(offset + jnp.arange(rows, dtype=jnp.int32), bounds)
    seg_keys = segment_of(jnp.arange(nkeys, dtype=jnp.int32), bounds)
    starts = jnp.concatenate([jnp.zeros((1,), jnp.int32), bounds])
    ends = jnp.concatenate([bounds, jnp.full((1,), nkeys, jnp.int32)])
    kstart = starts[seg_own[0]]
    kend = ends[seg_own[rows - 1]]
    rng = jnp.clip(jnp.stack([kstart // KBLOCK, (kend - 1) // KBLOCK]), 0, nk - 1).astype(jnp.int32)
    segq = seg_own.reshape(rows, 1)
    segk = seg_keys.reshape(n_tm, 1, rows)
    f32 = jnp.float32
    bf16 = jnp.bfloat16

    outs_a, outs_b = [], []
    for h in range(heads_here):
        own_q, own_k, own_v, own_g = (mine[:, h, c, :] for c in range(4))
        kv_t = jnp.stack([own_k.T, own_v.T])[None]
        qg_t = jnp.stack([own_q.T, own_g.T])[None]
        all_kv = lax.all_gather(kv_t, "tm", axis=0, tiled=True)
        all_qg = lax.all_gather(qg_t, "tm", axis=0, tiled=True)
        att, lse, delta = block_call(
            lambda *refs: fwd_kernel(*refs, scale=scale), rng,
            [segq, own_q, own_g],
            [(all_kv, (None, 2, DH, KBLOCK)), (segk, (None, 1, KBLOCK))],
            [jax.ShapeDtypeStruct((rows, DH), bf16), jax.ShapeDtypeStruct((rows, 1), f32),
             jax.ShapeDtypeStruct((rows, 1), f32)],
            [pltpu.VMEM((rows, 1), f32), pltpu.VMEM((rows, 1), f32), pltpu.VMEM((rows, DH), f32)],
            nk, per,
        )
        (dq,) = block_call(
            lambda *refs: dq_kernel(*refs, scale=scale), rng,
            [segq, own_q, own_g, lse, delta],
            [(all_kv, (None, 2, DH, KBLOCK)), (segk, (None, 1, KBLOCK))],
            [jax.ShapeDtypeStruct((rows, DH), bf16)],
            [pltpu.VMEM((rows, DH), f32)],
            nk, per,
        )
        stats = jnp.stack([lse.reshape(rows), delta.reshape(rows)])[None]
        all_stats = lax.all_gather(stats, "tm", axis=0, tiled=True)
        dk, dv = block_call(
            lambda *refs: dkv_kernel(*refs, scale=scale), rng,
            [segq, own_k, own_v],
            [(all_qg, (None, 2, DH, KBLOCK)), (all_stats, (None, 2, KBLOCK)),
             (segk, (None, 1, KBLOCK))],
            [jax.ShapeDtypeStruct((rows, DH), bf16), jax.ShapeDtypeStruct((rows, DH), bf16)],
            [pltpu.VMEM((rows, DH), f32), pltpu.VMEM((rows, DH), f32)],
            nk, per,
        )
        outs_a.append(jnp.stack([att, dq], axis=1))
        outs_b.append(jnp.stack([dk, dv], axis=1))

    def send_back(parts):
        packed = jnp.stack(parts, axis=1).reshape(rows, heads_here * 2 * DH)
        back = lax.all_to_all(packed, "head", split_axis=0, concat_axis=1, tiled=True)
        back = back.reshape(rows_in, HEADS, 2, DH)
        return back[:, :, 0, :].reshape(rows_in, HEADS * DH), back[:, :, 1, :].reshape(rows_in, HEADS * DH)

    attended, grad_q = send_back(outs_a)
    grad_k, grad_v = send_back(outs_b)
    return attended, grad_q, grad_k, grad_v


def solution(mesh):
    placed = (
        P(("tm", "head"), None),
        P(("tm", "head"), None),
        P(("tm", "head"), None),
        P(("tm", "head"), None),
        P(),
    )
    return jax.shard_map(
        body,
        mesh=mesh,
        in_specs=placed,
        out_specs=(
            P(("tm", "head"), None),
            P(("tm", "head"), None),
            P(("tm", "head"), None),
            P(("tm", "head"), None),
        ),
        check_vma=False,
    )
```

```python
import math

import jax
import jax.numpy as jnp
from jax import lax
from jax.experimental import pallas as pl
from jax.experimental.pallas import tpu as pltpu
from jax.sharding import PartitionSpec as P

HEADS = 8
DH = 96
KBLOCK = 512
NEG = -1e30
NT = (((1,), (1,)), ((), ()))


def segment_of(index, bounds):
    return jnp.sum((index[:, None] >= bounds[None, :]).astype(jnp.int32), axis=1)


def fwd_kernel(rng_ref, segq_ref, q_ref, g_ref, kv_ref, segk_ref,
               att_ref, lse_ref, delta_ref, m_sc, l_sc, acc_sc, k_sc, v_sc, *, scale):
    j = pl.program_id(0)
    lo = rng_ref[0]
    hi = rng_ref[1]

    @pl.when(j == 0)
    def _():
        m_sc[...] = jnp.full(m_sc.shape, NEG, jnp.float32)
        l_sc[...] = jnp.zeros(l_sc.shape, jnp.float32)
        acc_sc[...] = jnp.zeros(acc_sc.shape, jnp.float32)

    @pl.when(lo + j <= hi)
    def _():
        k_sc[...] = kv_ref[0].T
        v_sc[...] = kv_ref[1].T
        k = k_sc[...]
        v = v_sc[...]
        s = lax.dot_general(q_ref[...], k, NT, preferred_element_type=jnp.float32) * scale
        vis = segq_ref[...] == segk_ref[...]
        m_prev = m_sc[...]
        m_new = jnp.maximum(m_prev, jnp.max(jnp.where(vis, s, NEG), axis=1, keepdims=True))
        alpha = jnp.exp(m_prev - m_new)
        p = jnp.where(vis, jnp.exp(s - m_new), 0.0)
        l_sc[...] = l_sc[...] * alpha + jnp.sum(p, axis=1, keepdims=True)
        acc_sc[...] = acc_sc[...] * alpha + jnp.dot(
            p.astype(jnp.bfloat16), v, preferred_element_type=jnp.float32)
        m_sc[...] = m_new

    @pl.when(j == pl.num_programs(0) - 1)
    def _():
        total = l_sc[...]
        att = (acc_sc[...] / total).astype(jnp.bfloat16)
        att_ref[...] = att
        lse_ref[...] = m_sc[...] + jnp.log(total)
        delta_ref[...] = jnp.sum(g_ref[...].astype(jnp.float32) * att.astype(jnp.float32),
                                 axis=1, keepdims=True)


def dq_kernel(rng_ref, segq_ref, q_ref, g_ref, lse_ref, delta_ref, kv_ref, segk_ref,
              dq_ref, dq_sc, k_sc, v_sc, *, scale):
    j = pl.program_id(0)
    lo = rng_ref[0]
    hi = rng_ref[1]

    @pl.when(j == 0)
    def _():
        dq_sc[...] = jnp.zeros(dq_sc.shape, jnp.float32)

    @pl.when(lo + j <= hi)
    def _():
        k_sc[...] = kv_ref[0].T
        v_sc[...] = kv_ref[1].T
        k = k_sc[...]
        v = v_sc[...]
        s = lax.dot_general(q_ref[...], k, NT, preferred_element_type=jnp.float32) * scale
        vis = segq_ref[...] == segk_ref[...]
        w = jnp.where(vis, jnp.exp(s - lse_ref[...]), 0.0)
        dp = lax.dot_general(g_ref[...], v, NT, preferred_element_type=jnp.float32)
        ds = (w * (dp - delta_ref[...])).astype(jnp.bfloat16)
        dq_sc[...] += jnp.dot(ds, k, preferred_element_type=jnp.float32)

    @pl.when(j == pl.num_programs(0) - 1)
    def _():
        dq_ref[...] = (scale * dq_sc[...]).astype(jnp.bfloat16)


def dkv_kernel(rng_ref, segown_ref, k_ref, v_ref, qg_ref, st_ref, segk_ref,
               dk_ref, dv_ref, dk_sc, dv_sc, q_sc, g_sc, *, scale):
    i = pl.program_id(0)
    lo = rng_ref[0]
    hi = rng_ref[1]

    @pl.when(i == 0)
    def _():
        dk_sc[...] = jnp.zeros(dk_sc.shape, jnp.float32)
        dv_sc[...] = jnp.zeros(dv_sc.shape, jnp.float32)

    @pl.when(lo + i <= hi)
    def _():
        q_sc[...] = qg_ref[0].T
        g_sc[...] = qg_ref[1].T
        q = q_sc[...]
        g = g_sc[...]
        stats = st_ref[...]
        s_t = lax.dot_general(k_ref[...], q, NT, preferred_element_type=jnp.float32) * scale
        vis = segown_ref[...] == segk_ref[...]
        w_t = jnp.where(vis, jnp.exp(s_t - stats[0:1, :]), 0.0)
        dp_t = lax.dot_general(v_ref[...], g, NT, preferred_element_type=jnp.float32)
        ds_t = (w_t * (dp_t - stats[1:2, :])).astype(jnp.bfloat16)
        dk_sc[...] += jnp.dot(ds_t, q, preferred_element_type=jnp.float32)
        dv_sc[...] += jnp.dot(w_t.astype(jnp.bfloat16), g, preferred_element_type=jnp.float32)

    @pl.when(i == pl.num_programs(0) - 1)
    def _():
        dk_ref[...] = (scale * dk_sc[...]).astype(jnp.bfloat16)
        dv_ref[...] = dv_sc[...].astype(jnp.bfloat16)


def block_call(kernel, rng, fixed, streamed, outs, scratch, nblocks, per):
    def fixed_map(nd):
        return lambda j, r: (0,) * nd

    def clamp(j, r):
        return jnp.minimum(r[0] + j, r[1])

    def stream_map(nd):
        def index(j, r):
            b = clamp(j, r)
            return (b // per,) + (0,) * (nd - 2) + (b % per,)
        return index

    in_specs = [pl.BlockSpec(a.shape, fixed_map(a.ndim)) for a in fixed]
    for a, blk in streamed:
        in_specs.append(pl.BlockSpec(blk, stream_map(a.ndim)))
    return pl.pallas_call(
        kernel,
        grid_spec=pltpu.PrefetchScalarGridSpec(
            num_scalar_prefetch=1,
            grid=(nblocks,),
            in_specs=in_specs,
            out_specs=[pl.BlockSpec(o.shape, fixed_map(len(o.shape))) for o in outs],
            scratch_shapes=scratch,
        ),
        out_shape=outs,
        compiler_params=pltpu.CompilerParams(dimension_semantics=("arbitrary",)),
    )(rng, *fixed, *[a for a, _ in streamed])


def body(queries, keys, values, grad_out, frame_counts):
    n_head = lax.axis_size("head")
    n_tm = lax.axis_size("tm")
    heads_here = HEADS // n_head
    scale = 1.0 / math.sqrt(DH)
    rows_in = queries.shape[0]
    stacked = jnp.stack(
        [a.reshape(rows_in, HEADS, DH) for a in (queries, keys, values, grad_out)], axis=2
    ).reshape(rows_in, HEADS * 4 * DH)
    mine = lax.all_to_all(stacked, "head", split_axis=1, concat_axis=0, tiled=True)
    rows = mine.shape[0]
    mine = mine.reshape(rows, heads_here, 4, DH)
    per = rows // KBLOCK
    nkeys = rows * n_tm
    nk = nkeys // KBLOCK
    bounds = jnp.cumsum(frame_counts)[:-1].astype(jnp.int32)
    offset = lax.axis_index("tm") * rows
    seg_own = segment_of(offset + jnp.arange(rows, dtype=jnp.int32), bounds)
    seg_keys = segment_of(jnp.arange(nkeys, dtype=jnp.int32), bounds)
    starts = jnp.concatenate([jnp.zeros((1,), jnp.int32), bounds])
    ends = jnp.concatenate([bounds, jnp.full((1,), nkeys, jnp.int32)])
    kstart = starts[seg_own[0]]
    kend = ends[seg_own[rows - 1]]
    rng = jnp.clip(jnp.stack([kstart // KBLOCK, (kend - 1) // KBLOCK]), 0, nk - 1).astype(jnp.int32)
    segq = seg_own.reshape(rows, 1)
    segk = seg_keys.reshape(n_tm, 1, rows)
    f32 = jnp.float32
    bf16 = jnp.bfloat16

    outs_a, outs_b = [], []
    for h in range(heads_here):
        own_q, own_k, own_v, own_g = (mine[:, h, c, :] for c in range(4))
        kv_t = jnp.stack([own_k.T, own_v.T])[None]
        qg_t = jnp.stack([own_q.T, own_g.T])[None]
        all_kv = lax.all_gather(kv_t, "tm", axis=0, tiled=True)
        all_qg = lax.all_gather(qg_t, "tm", axis=0, tiled=True)
        att, lse, delta = block_call(
            lambda *refs: fwd_kernel(*refs, scale=scale), rng,
            [segq, own_q, own_g],
            [(all_kv, (None, 2, DH, KBLOCK)), (segk, (None, 1, KBLOCK))],
            [jax.ShapeDtypeStruct((rows, DH), bf16), jax.ShapeDtypeStruct((rows, 1), f32),
             jax.ShapeDtypeStruct((rows, 1), f32)],
            [pltpu.VMEM((rows, 1), f32), pltpu.VMEM((rows, 1), f32), pltpu.VMEM((rows, DH), f32),
             pltpu.VMEM((KBLOCK, DH), bf16), pltpu.VMEM((KBLOCK, DH), bf16)],
            nk, per,
        )
        (dq,) = block_call(
            lambda *refs: dq_kernel(*refs, scale=scale), rng,
            [segq, own_q, own_g, lse, delta],
            [(all_kv, (None, 2, DH, KBLOCK)), (segk, (None, 1, KBLOCK))],
            [jax.ShapeDtypeStruct((rows, DH), bf16)],
            [pltpu.VMEM((rows, DH), f32), pltpu.VMEM((KBLOCK, DH), bf16), pltpu.VMEM((KBLOCK, DH), bf16)],
            nk, per,
        )
        stats = jnp.stack([lse.reshape(rows), delta.reshape(rows)])[None]
        all_stats = lax.all_gather(stats, "tm", axis=0, tiled=True)
        dk, dv = block_call(
            lambda *refs: dkv_kernel(*refs, scale=scale), rng,
            [segq, own_k, own_v],
            [(all_qg, (None, 2, DH, KBLOCK)), (all_stats, (None, 2, KBLOCK)),
             (segk, (None, 1, KBLOCK))],
            [jax.ShapeDtypeStruct((rows, DH), bf16), jax.ShapeDtypeStruct((rows, DH), bf16)],
            [pltpu.VMEM((rows, DH), f32), pltpu.VMEM((rows, DH), f32), pltpu.VMEM((KBLOCK, DH), bf16), pltpu.VMEM((KBLOCK, DH), bf16)],
            nk, per,
        )
        outs_a.append(jnp.stack([att, dq], axis=1))
        outs_b.append(jnp.stack([dk, dv], axis=1))

    def send_back(parts):
        packed = jnp.stack(parts, axis=1).reshape(rows, heads_here * 2 * DH)
        back = lax.all_to_all(packed, "head", split_axis=0, concat_axis=1, tiled=True)
        back = back.reshape(rows_in, HEADS, 2, DH)
        return back[:, :, 0, :].reshape(rows_in, HEADS * DH), back[:, :, 1, :].reshape(rows_in, HEADS * DH)

    attended, grad_q = send_back(outs_a)
    grad_k, grad_v = send_back(outs_b)
    return attended, grad_q, grad_k, grad_v


def solution(mesh):
    placed = (
        P(("tm", "head"), None),
        P(("tm", "head"), None),
        P(("tm", "head"), None),
        P(("tm", "head"), None),
        P(),
    )
    return jax.shard_map(
        body,
        mesh=mesh,
        in_specs=placed,
        out_specs=(
            P(("tm", "head"), None),
            P(("tm", "head"), None),
            P(("tm", "head"), None),
            P(("tm", "head"), None),
        ),
        check_vma=False,
    )
```

```python
import math

import jax
import jax.numpy as jnp
from jax import lax
from jax.experimental import pallas as pl
from jax.experimental.pallas import tpu as pltpu
from jax.sharding import PartitionSpec as P

HEADS = 8
DH = 96
KBLOCK = 512
NEG = -1e30
STAT_ROWS = 48
NT = (((1,), (1,)), ((), ()))


def segment_of(index, bounds):
    return jnp.sum((index[:, None] >= bounds[None, :]).astype(jnp.int32), axis=1)


def fwd_kernel(rng_ref, segq_ref, q_ref, g_ref, kv_ref, segk_ref,
               att_ref, lse_ref, delta_ref, m_sc, l_sc, acc_sc, k_sc, v_sc, *, scale):
    j = pl.program_id(0)
    lo = rng_ref[0]
    hi = rng_ref[1]

    @pl.when(j == 0)
    def _():
        m_sc[...] = jnp.full(m_sc.shape, NEG, jnp.float32)
        l_sc[...] = jnp.zeros(l_sc.shape, jnp.float32)
        acc_sc[...] = jnp.zeros(acc_sc.shape, jnp.float32)

    @pl.when(lo + j <= hi)
    def _():
        k_sc[...] = kv_ref[0].T
        v_sc[...] = kv_ref[1].T
        k = k_sc[...]
        v = v_sc[...]
        s = lax.dot_general(q_ref[...], k, NT, preferred_element_type=jnp.float32) * scale
        vis = segq_ref[...] == segk_ref[...]
        m_prev = m_sc[...]
        m_new = jnp.maximum(m_prev, jnp.max(jnp.where(vis, s, NEG), axis=1, keepdims=True))
        alpha = jnp.exp(m_prev - m_new)
        p = jnp.where(vis, jnp.exp(s - m_new), 0.0)
        l_sc[...] = l_sc[...] * alpha + jnp.sum(p, axis=1, keepdims=True)
        acc_sc[...] = acc_sc[...] * alpha + jnp.dot(
            p.astype(jnp.bfloat16), v, preferred_element_type=jnp.float32)
        m_sc[...] = m_new

    @pl.when(j == pl.num_programs(0) - 1)
    def _():
        total = l_sc[...]
        att = (acc_sc[...] / total).astype(jnp.bfloat16)
        att_ref[...] = att
        lse_ref[...] = m_sc[...] + jnp.log(total)
        delta_ref[...] = jnp.sum(g_ref[...].astype(jnp.float32) * att.astype(jnp.float32),
                                 axis=1, keepdims=True)


def dq_kernel(rng_ref, segq_ref, q_ref, g_ref, lse_ref, delta_ref, kv_ref, segk_ref,
              dq_ref, dq_sc, k_sc, v_sc, *, scale):
    j = pl.program_id(0)
    lo = rng_ref[0]
    hi = rng_ref[1]

    @pl.when(j == 0)
    def _():
        dq_sc[...] = jnp.zeros(dq_sc.shape, jnp.float32)

    @pl.when(lo + j <= hi)
    def _():
        k_sc[...] = kv_ref[0].T
        v_sc[...] = kv_ref[1].T
        k = k_sc[...]
        v = v_sc[...]
        s = lax.dot_general(q_ref[...], k, NT, preferred_element_type=jnp.float32) * scale
        vis = segq_ref[...] == segk_ref[...]
        w = jnp.where(vis, jnp.exp(s - lse_ref[...]), 0.0)
        dp = lax.dot_general(g_ref[...], v, NT, preferred_element_type=jnp.float32)
        ds = (w * (dp - delta_ref[...])).astype(jnp.bfloat16)
        dq_sc[...] += jnp.dot(ds, k, preferred_element_type=jnp.float32)

    @pl.when(j == pl.num_programs(0) - 1)
    def _():
        dq_ref[...] = (scale * dq_sc[...]).astype(jnp.bfloat16)


def dkv_kernel(rng_ref, segown_ref, k_ref, v_ref, qg_ref, st_ref, segk_ref,
               dk_ref, dv_ref, dk_sc, dv_sc, q_sc, g_sc, *, scale):
    i = pl.program_id(0)
    lo = rng_ref[0]
    hi = rng_ref[1]

    @pl.when(i == 0)
    def _():
        dk_sc[...] = jnp.zeros(dk_sc.shape, jnp.float32)
        dv_sc[...] = jnp.zeros(dv_sc.shape, jnp.float32)

    @pl.when(lo + i <= hi)
    def _():
        q_sc[...] = qg_ref[0].T
        g_sc[...] = qg_ref[1].T
        q = q_sc[...]
        g = g_sc[...]
        parts = st_ref[...].astype(jnp.float32)
        stats = (parts[0:2, :] + parts[2:4, :]) + parts[4:6, :]
        s_t = lax.dot_general(k_ref[...], q, NT, preferred_element_type=jnp.float32) * scale
        vis = segown_ref[...] == segk_ref[...]
        w_t = jnp.where(vis, jnp.exp(s_t - stats[0:1, :]), 0.0)
        dp_t = lax.dot_general(v_ref[...], g, NT, preferred_element_type=jnp.float32)
        ds_t = (w_t * (dp_t - stats[1:2, :])).astype(jnp.bfloat16)
        dk_sc[...] += jnp.dot(ds_t, q, preferred_element_type=jnp.float32)
        dv_sc[...] += jnp.dot(w_t.astype(jnp.bfloat16), g, preferred_element_type=jnp.float32)

    @pl.when(i == pl.num_programs(0) - 1)
    def _():
        dk_ref[...] = (scale * dk_sc[...]).astype(jnp.bfloat16)
        dv_ref[...] = dv_sc[...].astype(jnp.bfloat16)


def block_call(kernel, rng, fixed, streamed, outs, scratch, nblocks, per):
    def fixed_map(nd):
        return lambda j, r: (0,) * nd

    def clamp(j, r):
        return jnp.minimum(r[0] + j, r[1])

    def stream_map(nd):
        def index(j, r):
            b = clamp(j, r)
            return (b // per,) + (0,) * (nd - 2) + (b % per,)
        return index

    in_specs = [pl.BlockSpec(a.shape, fixed_map(a.ndim)) for a in fixed]
    for a, blk in streamed:
        in_specs.append(pl.BlockSpec(blk, stream_map(a.ndim)))
    return pl.pallas_call(
        kernel,
        grid_spec=pltpu.PrefetchScalarGridSpec(
            num_scalar_prefetch=1,
            grid=(nblocks,),
            in_specs=in_specs,
            out_specs=[pl.BlockSpec(o.shape, fixed_map(len(o.shape))) for o in outs],
            scratch_shapes=scratch,
        ),
        out_shape=outs,
        compiler_params=pltpu.CompilerParams(dimension_semantics=("arbitrary",)),
    )(rng, *fixed, *[a for a, _ in streamed])


def body(queries, keys, values, grad_out, frame_counts):
    n_head = lax.axis_size("head")
    n_tm = lax.axis_size("tm")
    heads_here = HEADS // n_head
    scale = 1.0 / math.sqrt(DH)
    rows_in = queries.shape[0]
    stacked = jnp.stack(
        [a.reshape(rows_in, HEADS, DH) for a in (queries, keys, values, grad_out)], axis=2
    ).reshape(rows_in, HEADS * 4 * DH)
    mine = lax.all_to_all(stacked, "head", split_axis=1, concat_axis=0, tiled=True)
    rows = mine.shape[0]
    mine = mine.reshape(rows, heads_here, 4, DH)
    per = rows // KBLOCK
    nkeys = rows * n_tm
    nk = nkeys // KBLOCK
    bounds = jnp.cumsum(frame_counts)[:-1].astype(jnp.int32)
    offset = lax.axis_index("tm") * rows
    seg_own = segment_of(offset + jnp.arange(rows, dtype=jnp.int32), bounds)
    seg_keys = segment_of(jnp.arange(nkeys, dtype=jnp.int32), bounds)
    starts = jnp.concatenate([jnp.zeros((1,), jnp.int32), bounds])
    ends = jnp.concatenate([bounds, jnp.full((1,), nkeys, jnp.int32)])
    kstart = starts[seg_own[0]]
    kend = ends[seg_own[rows - 1]]
    rng = jnp.clip(jnp.stack([kstart // KBLOCK, (kend - 1) // KBLOCK]), 0, nk - 1).astype(jnp.int32)
    segq = seg_own.reshape(rows, 1)
    segk = seg_keys.reshape(n_tm, 1, rows)
    f32 = jnp.float32
    bf16 = jnp.bfloat16

    outs_a, outs_b = [], []
    for h in range(heads_here):
        own_q, own_k, own_v, own_g = (mine[:, h, c, :] for c in range(4))
        kv_t = jnp.stack([own_k.T, own_v.T])[None]
        qg_t = jnp.stack([own_q.T, own_g.T])[None]
        all_kv = lax.all_gather(kv_t, "tm", axis=0, tiled=True)
        all_qg = lax.all_gather(qg_t, "tm", axis=0, tiled=True)
        att, lse, delta = block_call(
            lambda *refs: fwd_kernel(*refs, scale=scale), rng,
            [segq, own_q, own_g],
            [(all_kv, (None, 2, DH, KBLOCK)), (segk, (None, 1, KBLOCK))],
            [jax.ShapeDtypeStruct((rows, DH), bf16), jax.ShapeDtypeStruct((rows, 1), f32),
             jax.ShapeDtypeStruct((rows, 1), f32)],
            [pltpu.VMEM((rows, 1), f32), pltpu.VMEM((rows, 1), f32), pltpu.VMEM((rows, DH), f32),
             pltpu.VMEM((KBLOCK, DH), bf16), pltpu.VMEM((KBLOCK, DH), bf16)],
            nk, per,
        )
        (dq,) = block_call(
            lambda *refs: dq_kernel(*refs, scale=scale), rng,
            [segq, own_q, own_g, lse, delta],
            [(all_kv, (None, 2, DH, KBLOCK)), (segk, (None, 1, KBLOCK))],
            [jax.ShapeDtypeStruct((rows, DH), bf16)],
            [pltpu.VMEM((rows, DH), f32), pltpu.VMEM((KBLOCK, DH), bf16), pltpu.VMEM((KBLOCK, DH), bf16)],
            nk, per,
        )
        stats = jnp.stack([lse.reshape(rows), delta.reshape(rows)])
        hi_part = lax.reduce_precision(stats, exponent_bits=8, mantissa_bits=7)
        rest = stats - hi_part
        mid_part = lax.reduce_precision(rest, exponent_bits=8, mantissa_bits=7)
        lo_part = rest - mid_part
        split = jnp.pad(jnp.concatenate([hi_part, mid_part, lo_part]), ((0, STAT_ROWS - 6), (0, 0))).astype(bf16)[None]
        all_stats = lax.all_gather(split, "tm", axis=0, tiled=True)
        dk, dv = block_call(
            lambda *refs: dkv_kernel(*refs, scale=scale), rng,
            [segq, own_k, own_v],
            [(all_qg, (None, 2, DH, KBLOCK)), (all_stats, (None, STAT_ROWS, KBLOCK)),
             (segk, (None, 1, KBLOCK))],
            [jax.ShapeDtypeStruct((rows, DH), bf16), jax.ShapeDtypeStruct((rows, DH), bf16)],
            [pltpu.VMEM((rows, DH), f32), pltpu.VMEM((rows, DH), f32), pltpu.VMEM((KBLOCK, DH), bf16), pltpu.VMEM((KBLOCK, DH), bf16)],
            nk, per,
        )
        outs_a.append(jnp.stack([att, dq], axis=1))
        outs_b.append(jnp.stack([dk, dv], axis=1))

    def send_back(parts):
        packed = jnp.stack(parts, axis=1).reshape(rows, heads_here * 2 * DH)
        back = lax.all_to_all(packed, "head", split_axis=0, concat_axis=1, tiled=True)
        back = back.reshape(rows_in, HEADS, 2, DH)
        return back[:, :, 0, :].reshape(rows_in, HEADS * DH), back[:, :, 1, :].reshape(rows_in, HEADS * DH)

    attended, grad_q = send_back(outs_a)
    grad_k, grad_v = send_back(outs_b)
    return attended, grad_q, grad_k, grad_v


def solution(mesh):
    placed = (
        P(("tm", "head"), None),
        P(("tm", "head"), None),
        P(("tm", "head"), None),
        P(("tm", "head"), None),
        P(),
    )
    return jax.shard_map(
        body,
        mesh=mesh,
        in_specs=placed,
        out_specs=(
            P(("tm", "head"), None),
            P(("tm", "head"), None),
            P(("tm", "head"), None),
            P(("tm", "head"), None),
        ),
        check_vma=False,
    )
```

```python
import math

import jax
import jax.numpy as jnp
from jax import lax
from jax.experimental import pallas as pl
from jax.experimental.pallas import tpu as pltpu
from jax.sharding import PartitionSpec as P

HEADS = 8
DH = 96
KBLOCK = 512
NEG = -1e30
STAT_ROWS = 48
NT = (((1,), (1,)), ((), ()))


def segment_of(index, bounds):
    return jnp.sum((index[:, None] >= bounds[None, :]).astype(jnp.int32), axis=1)


def fwd_kernel(rng_ref, segq_ref, q_ref, g_ref, kv_ref, segk_ref,
               att_ref, lse_ref, delta_ref, m_sc, l_sc, acc_sc, k_sc, v_sc, *, scale):
    j = pl.program_id(0)
    lo = rng_ref[0]
    hi = rng_ref[1]

    @pl.when(j == 0)
    def _():
        m_sc[...] = jnp.full(m_sc.shape, NEG, jnp.float32)
        l_sc[...] = jnp.zeros(l_sc.shape, jnp.float32)
        acc_sc[...] = jnp.zeros(acc_sc.shape, jnp.float32)

    b = jnp.minimum(lo + j, hi)
    active = lo + j <= hi
    full = rng_ref[2 + b] == 1

    def step(masked):
        k_sc[...] = kv_ref[0].T
        v_sc[...] = kv_ref[1].T
        k = k_sc[...]
        v = v_sc[...]
        s = lax.dot_general(q_ref[...], k, NT, preferred_element_type=jnp.float32) * scale
        m_prev = m_sc[...]
        if masked:
            vis = segq_ref[...] == segk_ref[...]
            m_new = jnp.maximum(m_prev, jnp.max(jnp.where(vis, s, NEG), axis=1, keepdims=True))
            p = jnp.where(vis, jnp.exp(s - m_new), 0.0)
        else:
            m_new = jnp.maximum(m_prev, jnp.max(s, axis=1, keepdims=True))
            p = jnp.exp(s - m_new)
        alpha = jnp.exp(m_prev - m_new)
        l_sc[...] = l_sc[...] * alpha + jnp.sum(p, axis=1, keepdims=True)
        acc_sc[...] = acc_sc[...] * alpha + jnp.dot(
            p.astype(jnp.bfloat16), v, preferred_element_type=jnp.float32)
        m_sc[...] = m_new

    pl.when(jnp.logical_and(active, full))(lambda: step(False))
    pl.when(jnp.logical_and(active, jnp.logical_not(full)))(lambda: step(True))

    @pl.when(j == pl.num_programs(0) - 1)
    def _():
        total = l_sc[...]
        att = (acc_sc[...] / total).astype(jnp.bfloat16)
        att_ref[...] = att
        lse_ref[...] = m_sc[...] + jnp.log(total)
        delta_ref[...] = jnp.sum(g_ref[...].astype(jnp.float32) * att.astype(jnp.float32),
                                 axis=1, keepdims=True)


def dq_kernel(rng_ref, segq_ref, q_ref, g_ref, lse_ref, delta_ref, kv_ref, segk_ref,
              dq_ref, dq_sc, k_sc, v_sc, *, scale):
    j = pl.program_id(0)
    lo = rng_ref[0]
    hi = rng_ref[1]

    @pl.when(j == 0)
    def _():
        dq_sc[...] = jnp.zeros(dq_sc.shape, jnp.float32)

    b = jnp.minimum(lo + j, hi)
    active = lo + j <= hi
    full = rng_ref[2 + b] == 1

    def step(masked):
        k_sc[...] = kv_ref[0].T
        v_sc[...] = kv_ref[1].T
        k = k_sc[...]
        v = v_sc[...]
        s = lax.dot_general(q_ref[...], k, NT, preferred_element_type=jnp.float32) * scale
        w = jnp.exp(s - lse_ref[...])
        if masked:
            w = jnp.where(segq_ref[...] == segk_ref[...], w, 0.0)
        dp = lax.dot_general(g_ref[...], v, NT, preferred_element_type=jnp.float32)
        ds = (w * (dp - delta_ref[...])).astype(jnp.bfloat16)
        dq_sc[...] += jnp.dot(ds, k, preferred_element_type=jnp.float32)

    pl.when(jnp.logical_and(active, full))(lambda: step(False))
    pl.when(jnp.logical_and(active, jnp.logical_not(full)))(lambda: step(True))

    @pl.when(j == pl.num_programs(0) - 1)
    def _():
        dq_ref[...] = (scale * dq_sc[...]).astype(jnp.bfloat16)


def dkv_kernel(rng_ref, segown_ref, k_ref, v_ref, qg_ref, st_ref, segk_ref,
               dk_ref, dv_ref, dk_sc, dv_sc, q_sc, g_sc, *, scale):
    i = pl.program_id(0)
    lo = rng_ref[0]
    hi = rng_ref[1]

    @pl.when(i == 0)
    def _():
        dk_sc[...] = jnp.zeros(dk_sc.shape, jnp.float32)
        dv_sc[...] = jnp.zeros(dv_sc.shape, jnp.float32)

    b = jnp.minimum(lo + i, hi)
    active = lo + i <= hi
    full = rng_ref[2 + b] == 1

    def step(masked):
        q_sc[...] = qg_ref[0].T
        g_sc[...] = qg_ref[1].T
        q = q_sc[...]
        g = g_sc[...]
        parts = st_ref[...].astype(jnp.float32)
        stats = (parts[0:2, :] + parts[2:4, :]) + parts[4:6, :]
        s_t = lax.dot_general(k_ref[...], q, NT, preferred_element_type=jnp.float32) * scale
        w_t = jnp.exp(s_t - stats[0:1, :])
        if masked:
            w_t = jnp.where(segown_ref[...] == segk_ref[...], w_t, 0.0)
        dp_t = lax.dot_general(v_ref[...], g, NT, preferred_element_type=jnp.float32)
        ds_t = (w_t * (dp_t - stats[1:2, :])).astype(jnp.bfloat16)
        dk_sc[...] += jnp.dot(ds_t, q, preferred_element_type=jnp.float32)
        dv_sc[...] += jnp.dot(w_t.astype(jnp.bfloat16), g, preferred_element_type=jnp.float32)

    pl.when(jnp.logical_and(active, full))(lambda: step(False))
    pl.when(jnp.logical_and(active, jnp.logical_not(full)))(lambda: step(True))

    @pl.when(i == pl.num_programs(0) - 1)
    def _():
        dk_ref[...] = (scale * dk_sc[...]).astype(jnp.bfloat16)
        dv_ref[...] = dv_sc[...].astype(jnp.bfloat16)


def block_call(kernel, rng, fixed, streamed, outs, scratch, nblocks, per):
    def fixed_map(nd):
        return lambda j, r: (0,) * nd

    def clamp(j, r):
        return jnp.minimum(r[0] + j, r[1])

    def stream_map(nd):
        def index(j, r):
            b = clamp(j, r)
            return (b // per,) + (0,) * (nd - 2) + (b % per,)
        return index

    in_specs = [pl.BlockSpec(a.shape, fixed_map(a.ndim)) for a in fixed]
    for a, blk in streamed:
        in_specs.append(pl.BlockSpec(blk, stream_map(a.ndim)))
    return pl.pallas_call(
        kernel,
        grid_spec=pltpu.PrefetchScalarGridSpec(
            num_scalar_prefetch=1,
            grid=(nblocks,),
            in_specs=in_specs,
            out_specs=[pl.BlockSpec(o.shape, fixed_map(len(o.shape))) for o in outs],
            scratch_shapes=scratch,
        ),
        out_shape=outs,
        compiler_params=pltpu.CompilerParams(dimension_semantics=("arbitrary",)),
    )(rng, *fixed, *[a for a, _ in streamed])


def body(queries, keys, values, grad_out, frame_counts):
    n_head = lax.axis_size("head")
    n_tm = lax.axis_size("tm")
    heads_here = HEADS // n_head
    scale = 1.0 / math.sqrt(DH)
    rows_in = queries.shape[0]
    stacked = jnp.stack(
        [a.reshape(rows_in, HEADS, DH) for a in (queries, keys, values, grad_out)], axis=2
    ).reshape(rows_in, HEADS * 4 * DH)
    mine = lax.all_to_all(stacked, "head", split_axis=1, concat_axis=0, tiled=True)
    rows = mine.shape[0]
    mine = mine.reshape(rows, heads_here, 4, DH)
    per = rows // KBLOCK
    nkeys = rows * n_tm
    nk = nkeys // KBLOCK
    bounds = jnp.cumsum(frame_counts)[:-1].astype(jnp.int32)
    offset = lax.axis_index("tm") * rows
    seg_own = segment_of(offset + jnp.arange(rows, dtype=jnp.int32), bounds)
    seg_keys = segment_of(jnp.arange(nkeys, dtype=jnp.int32), bounds)
    starts = jnp.concatenate([jnp.zeros((1,), jnp.int32), bounds])
    ends = jnp.concatenate([bounds, jnp.full((1,), nkeys, jnp.int32)])
    kstart = starts[seg_own[0]]
    kend = ends[seg_own[rows - 1]]
    lohi = jnp.clip(jnp.stack([kstart // KBLOCK, (kend - 1) // KBLOCK]), 0, nk - 1).astype(jnp.int32)
    seg_blocks = seg_keys.reshape(nk, KBLOCK)
    one_seg = jnp.logical_and(seg_own[0] == seg_own[rows - 1],
                              jnp.logical_and(seg_blocks[:, 0] == seg_own[0],
                                              seg_blocks[:, KBLOCK - 1] == seg_own[0]))
    rng = jnp.concatenate([lohi, one_seg.astype(jnp.int32)])
    segq = seg_own.reshape(rows, 1)
    segk = seg_keys.reshape(n_tm, 1, rows)
    f32 = jnp.float32
    bf16 = jnp.bfloat16

    outs_a, outs_b = [], []
    for h in range(heads_here):
        own_q, own_k, own_v, own_g = (mine[:, h, c, :] for c in range(4))
        kv_t = jnp.stack([own_k.T, own_v.T])[None]
        qg_t = jnp.stack([own_q.T, own_g.T])[None]
        all_kv = lax.all_gather(kv_t, "tm", axis=0, tiled=True)
        all_qg = lax.all_gather(qg_t, "tm", axis=0, tiled=True)
        att, lse, delta = block_call(
            lambda *refs: fwd_kernel(*refs, scale=scale), rng,
            [segq, own_q, own_g],
            [(all_kv, (None, 2, DH, KBLOCK)), (segk, (None, 1, KBLOCK))],
            [jax.ShapeDtypeStruct((rows, DH), bf16), jax.ShapeDtypeStruct((rows, 1), f32),
             jax.ShapeDtypeStruct((rows, 1), f32)],
            [pltpu.VMEM((rows, 1), f32), pltpu.VMEM((rows, 1), f32), pltpu.VMEM((rows, DH), f32),
             pltpu.VMEM((KBLOCK, DH), bf16), pltpu.VMEM((KBLOCK, DH), bf16)],
            nk, per,
        )
        (dq,) = block_call(
            lambda *refs: dq_kernel(*refs, scale=scale), rng,
            [segq, own_q, own_g, lse, delta],
            [(all_kv, (None, 2, DH, KBLOCK)), (segk, (None, 1, KBLOCK))],
            [jax.ShapeDtypeStruct((rows, DH), bf16)],
            [pltpu.VMEM((rows, DH), f32), pltpu.VMEM((KBLOCK, DH), bf16), pltpu.VMEM((KBLOCK, DH), bf16)],
            nk, per,
        )
        stats = jnp.stack([lse.reshape(rows), delta.reshape(rows)])
        hi_part = lax.reduce_precision(stats, exponent_bits=8, mantissa_bits=7)
        rest = stats - hi_part
        mid_part = lax.reduce_precision(rest, exponent_bits=8, mantissa_bits=7)
        lo_part = rest - mid_part
        split = jnp.pad(jnp.concatenate([hi_part, mid_part, lo_part]), ((0, STAT_ROWS - 6), (0, 0))).astype(bf16)[None]
        all_stats = lax.all_gather(split, "tm", axis=0, tiled=True)
        dk, dv = block_call(
            lambda *refs: dkv_kernel(*refs, scale=scale), rng,
            [segq, own_k, own_v],
            [(all_qg, (None, 2, DH, KBLOCK)), (all_stats, (None, STAT_ROWS, KBLOCK)),
             (segk, (None, 1, KBLOCK))],
            [jax.ShapeDtypeStruct((rows, DH), bf16), jax.ShapeDtypeStruct((rows, DH), bf16)],
            [pltpu.VMEM((rows, DH), f32), pltpu.VMEM((rows, DH), f32), pltpu.VMEM((KBLOCK, DH), bf16), pltpu.VMEM((KBLOCK, DH), bf16)],
            nk, per,
        )
        outs_a.append(jnp.stack([att, dq], axis=1))
        outs_b.append(jnp.stack([dk, dv], axis=1))

    def send_back(parts):
        packed = jnp.stack(parts, axis=1).reshape(rows, heads_here * 2 * DH)
        back = lax.all_to_all(packed, "head", split_axis=0, concat_axis=1, tiled=True)
        back = back.reshape(rows_in, HEADS, 2, DH)
        return back[:, :, 0, :].reshape(rows_in, HEADS * DH), back[:, :, 1, :].reshape(rows_in, HEADS * DH)

    attended, grad_q = send_back(outs_a)
    grad_k, grad_v = send_back(outs_b)
    return attended, grad_q, grad_k, grad_v


def solution(mesh):
    placed = (
        P(("tm", "head"), None),
        P(("tm", "head"), None),
        P(("tm", "head"), None),
        P(("tm", "head"), None),
        P(),
    )
    return jax.shard_map(
        body,
        mesh=mesh,
        in_specs=placed,
        out_specs=(
            P(("tm", "head"), None),
            P(("tm", "head"), None),
            P(("tm", "head"), None),
            P(("tm", "head"), None),
        ),
        check_vma=False,
    )
```

```python
import math

import jax
import jax.numpy as jnp
from jax import lax
from jax.experimental import pallas as pl
from jax.experimental.pallas import tpu as pltpu
from jax.sharding import PartitionSpec as P

HEADS = 8
DH = 96
KBLOCK = 1024
NEG = -1e30
STAT_ROWS = 48
NT = (((1,), (1,)), ((), ()))


def segment_of(index, bounds):
    return jnp.sum((index[:, None] >= bounds[None, :]).astype(jnp.int32), axis=1)


def fwd_kernel(rng_ref, segq_ref, q_ref, g_ref, kv_ref, segk_ref,
               att_ref, lse_ref, delta_ref, m_sc, l_sc, acc_sc, k_sc, v_sc, *, scale):
    j = pl.program_id(0)
    lo = rng_ref[0]
    hi = rng_ref[1]

    @pl.when(j == 0)
    def _():
        m_sc[...] = jnp.full(m_sc.shape, NEG, jnp.float32)
        l_sc[...] = jnp.zeros(l_sc.shape, jnp.float32)
        acc_sc[...] = jnp.zeros(acc_sc.shape, jnp.float32)

    @pl.when(lo + j <= hi)
    def _():
        k_sc[...] = kv_ref[0].T
        v_sc[...] = kv_ref[1].T
        k = k_sc[...]
        v = v_sc[...]
        s = lax.dot_general(q_ref[...], k, NT, preferred_element_type=jnp.float32) * scale
        vis = segq_ref[...] == segk_ref[...]
        m_prev = m_sc[...]
        m_new = jnp.maximum(m_prev, jnp.max(jnp.where(vis, s, NEG), axis=1, keepdims=True))
        alpha = jnp.exp(m_prev - m_new)
        p = jnp.where(vis, jnp.exp(s - m_new), 0.0)
        l_sc[...] = l_sc[...] * alpha + jnp.sum(p, axis=1, keepdims=True)
        acc_sc[...] = acc_sc[...] * alpha + jnp.dot(
            p.astype(jnp.bfloat16), v, preferred_element_type=jnp.float32)
        m_sc[...] = m_new

    @pl.when(j == pl.num_programs(0) - 1)
    def _():
        total = l_sc[...]
        att = (acc_sc[...] / total).astype(jnp.bfloat16)
        att_ref[...] = att
        lse_ref[...] = m_sc[...] + jnp.log(total)
        delta_ref[...] = jnp.sum(g_ref[...].astype(jnp.float32) * att.astype(jnp.float32),
                                 axis=1, keepdims=True)


def dq_kernel(rng_ref, segq_ref, q_ref, g_ref, lse_ref, delta_ref, kv_ref, segk_ref,
              dq_ref, dq_sc, k_sc, v_sc, *, scale):
    j = pl.program_id(0)
    lo = rng_ref[0]
    hi = rng_ref[1]

    @pl.when(j == 0)
    def _():
        dq_sc[...] = jnp.zeros(dq_sc.shape, jnp.float32)

    @pl.when(lo + j <= hi)
    def _():
        k_sc[...] = kv_ref[0].T
        v_sc[...] = kv_ref[1].T
        k = k_sc[...]
        v = v_sc[...]
        s = lax.dot_general(q_ref[...], k, NT, preferred_element_type=jnp.float32) * scale
        vis = segq_ref[...] == segk_ref[...]
        w = jnp.where(vis, jnp.exp(s - lse_ref[...]), 0.0)
        dp = lax.dot_general(g_ref[...], v, NT, preferred_element_type=jnp.float32)
        ds = (w * (dp - delta_ref[...])).astype(jnp.bfloat16)
        dq_sc[...] += jnp.dot(ds, k, preferred_element_type=jnp.float32)

    @pl.when(j == pl.num_programs(0) - 1)
    def _():
        dq_ref[...] = (scale * dq_sc[...]).astype(jnp.bfloat16)


def dkv_kernel(rng_ref, segown_ref, k_ref, v_ref, qg_ref, st_ref, segk_ref,
               dk_ref, dv_ref, dk_sc, dv_sc, q_sc, g_sc, *, scale):
    i = pl.program_id(0)
    lo = rng_ref[0]
    hi = rng_ref[1]

    @pl.when(i == 0)
    def _():
        dk_sc[...] = jnp.zeros(dk_sc.shape, jnp.float32)
        dv_sc[...] = jnp.zeros(dv_sc.shape, jnp.float32)

    @pl.when(lo + i <= hi)
    def _():
        q_sc[...] = qg_ref[0].T
        g_sc[...] = qg_ref[1].T
        q = q_sc[...]
        g = g_sc[...]
        parts = st_ref[...].astype(jnp.float32)
        stats = (parts[0:2, :] + parts[2:4, :]) + parts[4:6, :]
        s_t = lax.dot_general(k_ref[...], q, NT, preferred_element_type=jnp.float32) * scale
        vis = segown_ref[...] == segk_ref[...]
        w_t = jnp.where(vis, jnp.exp(s_t - stats[0:1, :]), 0.0)
        dp_t = lax.dot_general(v_ref[...], g, NT, preferred_element_type=jnp.float32)
        ds_t = (w_t * (dp_t - stats[1:2, :])).astype(jnp.bfloat16)
        dk_sc[...] += jnp.dot(ds_t, q, preferred_element_type=jnp.float32)
        dv_sc[...] += jnp.dot(w_t.astype(jnp.bfloat16), g, preferred_element_type=jnp.float32)

    @pl.when(i == pl.num_programs(0) - 1)
    def _():
        dk_ref[...] = (scale * dk_sc[...]).astype(jnp.bfloat16)
        dv_ref[...] = dv_sc[...].astype(jnp.bfloat16)


def block_call(kernel, rng, fixed, streamed, outs, scratch, nblocks, per):
    def fixed_map(nd):
        return lambda j, r: (0,) * nd

    def clamp(j, r):
        return jnp.minimum(r[0] + j, r[1])

    def stream_map(nd):
        def index(j, r):
            b = clamp(j, r)
            return (b // per,) + (0,) * (nd - 2) + (b % per,)
        return index

    in_specs = [pl.BlockSpec(a.shape, fixed_map(a.ndim)) for a in fixed]
    for a, blk in streamed:
        in_specs.append(pl.BlockSpec(blk, stream_map(a.ndim)))
    return pl.pallas_call(
        kernel,
        grid_spec=pltpu.PrefetchScalarGridSpec(
            num_scalar_prefetch=1,
            grid=(nblocks,),
            in_specs=in_specs,
            out_specs=[pl.BlockSpec(o.shape, fixed_map(len(o.shape))) for o in outs],
            scratch_shapes=scratch,
        ),
        out_shape=outs,
        compiler_params=pltpu.CompilerParams(dimension_semantics=("arbitrary",)),
    )(rng, *fixed, *[a for a, _ in streamed])


def body(queries, keys, values, grad_out, frame_counts):
    n_head = lax.axis_size("head")
    n_tm = lax.axis_size("tm")
    heads_here = HEADS // n_head
    scale = 1.0 / math.sqrt(DH)
    rows_in = queries.shape[0]
    stacked = jnp.stack(
        [a.reshape(rows_in, HEADS, DH) for a in (queries, keys, values, grad_out)], axis=2
    ).reshape(rows_in, HEADS * 4 * DH)
    mine = lax.all_to_all(stacked, "head", split_axis=1, concat_axis=0, tiled=True)
    rows = mine.shape[0]
    mine = mine.reshape(rows, heads_here, 4, DH)
    per = rows // KBLOCK
    nkeys = rows * n_tm
    nk = nkeys // KBLOCK
    bounds = jnp.cumsum(frame_counts)[:-1].astype(jnp.int32)
    offset = lax.axis_index("tm") * rows
    seg_own = segment_of(offset + jnp.arange(rows, dtype=jnp.int32), bounds)
    seg_keys = segment_of(jnp.arange(nkeys, dtype=jnp.int32), bounds)
    starts = jnp.concatenate([jnp.zeros((1,), jnp.int32), bounds])
    ends = jnp.concatenate([bounds, jnp.full((1,), nkeys, jnp.int32)])
    kstart = starts[seg_own[0]]
    kend = ends[seg_own[rows - 1]]
    rng = jnp.clip(jnp.stack([kstart // KBLOCK, (kend - 1) // KBLOCK]), 0, nk - 1).astype(jnp.int32)
    segq = seg_own.reshape(rows, 1)
    segk = seg_keys.reshape(n_tm, 1, rows)
    f32 = jnp.float32
    bf16 = jnp.bfloat16

    outs_a, outs_b = [], []
    for h in range(heads_here):
        own_q, own_k, own_v, own_g = (mine[:, h, c, :] for c in range(4))
        kv_t = jnp.stack([own_k.T, own_v.T])[None]
        qg_t = jnp.stack([own_q.T, own_g.T])[None]
        all_kv = lax.all_gather(kv_t, "tm", axis=0, tiled=True)
        all_qg = lax.all_gather(qg_t, "tm", axis=0, tiled=True)
        att, lse, delta = block_call(
            lambda *refs: fwd_kernel(*refs, scale=scale), rng,
            [segq, own_q, own_g],
            [(all_kv, (None, 2, DH, KBLOCK)), (segk, (None, 1, KBLOCK))],
            [jax.ShapeDtypeStruct((rows, DH), bf16), jax.ShapeDtypeStruct((rows, 1), f32),
             jax.ShapeDtypeStruct((rows, 1), f32)],
            [pltpu.VMEM((rows, 1), f32), pltpu.VMEM((rows, 1), f32), pltpu.VMEM((rows, DH), f32),
             pltpu.VMEM((KBLOCK, DH), bf16), pltpu.VMEM((KBLOCK, DH), bf16)],
            nk, per,
        )
        (dq,) = block_call(
            lambda *refs: dq_kernel(*refs, scale=scale), rng,
            [segq, own_q, own_g, lse, delta],
            [(all_kv, (None, 2, DH, KBLOCK)), (segk, (None, 1, KBLOCK))],
            [jax.ShapeDtypeStruct((rows, DH), bf16)],
            [pltpu.VMEM((rows, DH), f32), pltpu.VMEM((KBLOCK, DH), bf16), pltpu.VMEM((KBLOCK, DH), bf16)],
            nk, per,
        )
        stats = jnp.stack([lse.reshape(rows), delta.reshape(rows)])
        hi_part = lax.reduce_precision(stats, exponent_bits=8, mantissa_bits=7)
        rest = stats - hi_part
        mid_part = lax.reduce_precision(rest, exponent_bits=8, mantissa_bits=7)
        lo_part = rest - mid_part
        split = jnp.pad(jnp.concatenate([hi_part, mid_part, lo_part]), ((0, STAT_ROWS - 6), (0, 0))).astype(bf16)[None]
        all_stats = lax.all_gather(split, "tm", axis=0, tiled=True)
        dk, dv = block_call(
            lambda *refs: dkv_kernel(*refs, scale=scale), rng,
            [segq, own_k, own_v],
            [(all_qg, (None, 2, DH, KBLOCK)), (all_stats, (None, STAT_ROWS, KBLOCK)),
             (segk, (None, 1, KBLOCK))],
            [jax.ShapeDtypeStruct((rows, DH), bf16), jax.ShapeDtypeStruct((rows, DH), bf16)],
            [pltpu.VMEM((rows, DH), f32), pltpu.VMEM((rows, DH), f32), pltpu.VMEM((KBLOCK, DH), bf16), pltpu.VMEM((KBLOCK, DH), bf16)],
            nk, per,
        )
        outs_a.append(jnp.stack([att, dq], axis=1))
        outs_b.append(jnp.stack([dk, dv], axis=1))

    def send_back(parts):
        packed = jnp.stack(parts, axis=1).reshape(rows, heads_here * 2 * DH)
        back = lax.all_to_all(packed, "head", split_axis=0, concat_axis=1, tiled=True)
        back = back.reshape(rows_in, HEADS, 2, DH)
        return back[:, :, 0, :].reshape(rows_in, HEADS * DH), back[:, :, 1, :].reshape(rows_in, HEADS * DH)

    attended, grad_q = send_back(outs_a)
    grad_k, grad_v = send_back(outs_b)
    return attended, grad_q, grad_k, grad_v


def solution(mesh):
    placed = (
        P(("tm", "head"), None),
        P(("tm", "head"), None),
        P(("tm", "head"), None),
        P(("tm", "head"), None),
        P(),
    )
    return jax.shard_map(
        body,
        mesh=mesh,
        in_specs=placed,
        out_specs=(
            P(("tm", "head"), None),
            P(("tm", "head"), None),
            P(("tm", "head"), None),
            P(("tm", "head"), None),
        ),
        check_vma=False,
    )
```

```python
import math

import jax
import jax.numpy as jnp
from jax import lax
from jax.experimental import pallas as pl
from jax.experimental.pallas import tpu as pltpu
from jax.sharding import PartitionSpec as P

HEADS = 8
DH = 96
KBLOCK = 1024
NEG = -1e30
STAT_ROWS = 48
NT = (((1,), (1,)), ((), ()))


def segment_of(index, bounds):
    return jnp.sum((index[:, None] >= bounds[None, :]).astype(jnp.int32), axis=1)


def fwd_kernel(rng_ref, segq_ref, q_ref, g_ref, kv_ref, segk_ref,
               att_ref, lse_ref, delta_ref, m_sc, l_sc, acc_sc, k_sc, v_sc, *, scale):
    j = pl.program_id(0)
    lo = rng_ref[0]
    hi = rng_ref[1]

    @pl.when(j == 0)
    def _():
        m_sc[...] = jnp.full(m_sc.shape, NEG, jnp.float32)
        l_sc[...] = jnp.zeros(l_sc.shape, jnp.float32)
        acc_sc[...] = jnp.zeros(acc_sc.shape, jnp.float32)

    @pl.when(lo + j <= hi)
    def _():
        k_sc[...] = kv_ref[0].T
        v_sc[...] = kv_ref[1].T
        k = k_sc[...]
        v = v_sc[...]
        s = lax.dot_general(q_ref[...], k, NT, preferred_element_type=jnp.float32) * scale
        vis = segq_ref[...] == segk_ref[...]
        m_prev = m_sc[...]
        m_new = jnp.maximum(m_prev, jnp.max(jnp.where(vis, s, NEG), axis=1, keepdims=True))
        alpha = jnp.exp(m_prev - m_new)
        p = jnp.where(vis, jnp.exp(s - m_new), 0.0)
        l_sc[...] = l_sc[...] * alpha + jnp.sum(p, axis=1, keepdims=True)
        acc_sc[...] = acc_sc[...] * alpha + jnp.dot(
            p.astype(jnp.bfloat16), v, preferred_element_type=jnp.float32)
        m_sc[...] = m_new

    @pl.when(j == pl.num_programs(0) - 1)
    def _():
        total = l_sc[...]
        att = (acc_sc[...] / total).astype(jnp.bfloat16)
        att_ref[...] = att
        lse_ref[...] = m_sc[...] + jnp.log(total)
        delta_ref[...] = jnp.sum(g_ref[...].astype(jnp.float32) * att.astype(jnp.float32),
                                 axis=1, keepdims=True)


def dq_kernel(rng_ref, segq_ref, q_ref, g_ref, lse_ref, delta_ref, kv_ref, segk_ref,
              dq_ref, dq_sc, k_sc, v_sc, *, scale):
    j = pl.program_id(0)
    lo = rng_ref[0]
    hi = rng_ref[1]

    @pl.when(j == 0)
    def _():
        dq_sc[...] = jnp.zeros(dq_sc.shape, jnp.float32)

    @pl.when(lo + j <= hi)
    def _():
        k_sc[...] = kv_ref[0].T
        v_sc[...] = kv_ref[1].T
        k = k_sc[...]
        v = v_sc[...]
        s = lax.dot_general(q_ref[...], k, NT, preferred_element_type=jnp.float32) * scale
        vis = segq_ref[...] == segk_ref[...]
        w = jnp.where(vis, jnp.exp(s - lse_ref[...]), 0.0)
        dp = lax.dot_general(g_ref[...], v, NT, preferred_element_type=jnp.float32)
        ds = (w * (dp - delta_ref[...])).astype(jnp.bfloat16)
        dq_sc[...] += jnp.dot(ds, k, preferred_element_type=jnp.float32)

    @pl.when(j == pl.num_programs(0) - 1)
    def _():
        dq_ref[...] = (scale * dq_sc[...]).astype(jnp.bfloat16)


def dkv_kernel(rng_ref, segown_ref, k_ref, v_ref, qg_ref, st_ref, segk_ref,
               dk_ref, dv_ref, dk_sc, dv_sc, q_sc, g_sc, *, scale):
    i = pl.program_id(0)
    lo = rng_ref[0]
    hi = rng_ref[1]

    @pl.when(i == 0)
    def _():
        dk_sc[...] = jnp.zeros(dk_sc.shape, jnp.float32)
        dv_sc[...] = jnp.zeros(dv_sc.shape, jnp.float32)

    @pl.when(lo + i <= hi)
    def _():
        q_sc[...] = qg_ref[0].T
        g_sc[...] = qg_ref[1].T
        q = q_sc[...]
        g = g_sc[...]
        parts = st_ref[...].astype(jnp.float32)
        stats = (parts[0:2, :] + parts[2:4, :]) + parts[4:6, :]
        s_t = lax.dot_general(k_ref[...], q, NT, preferred_element_type=jnp.float32) * scale
        vis = segown_ref[...] == segk_ref[...]
        w_t = jnp.where(vis, jnp.exp(s_t - stats[0:1, :]), 0.0)
        dp_t = lax.dot_general(v_ref[...], g, NT, preferred_element_type=jnp.float32)
        ds_t = (w_t * (dp_t - stats[1:2, :])).astype(jnp.bfloat16)
        dk_sc[...] += jnp.dot(ds_t, q, preferred_element_type=jnp.float32)
        dv_sc[...] += jnp.dot(w_t.astype(jnp.bfloat16), g, preferred_element_type=jnp.float32)

    @pl.when(i == pl.num_programs(0) - 1)
    def _():
        dk_ref[...] = (scale * dk_sc[...]).astype(jnp.bfloat16)
        dv_ref[...] = dv_sc[...].astype(jnp.bfloat16)


def block_call(kernel, rng, fixed, streamed, outs, scratch, nblocks, per):
    def fixed_map(nd):
        return lambda j, r: (0,) * nd

    def clamp(j, r):
        return jnp.minimum(r[0] + j, r[1])

    def stream_map(nd):
        def index(j, r):
            b = clamp(j, r)
            return (b // per,) + (0,) * (nd - 2) + (b % per,)
        return index

    in_specs = [pl.BlockSpec(a.shape, fixed_map(a.ndim)) for a in fixed]
    for a, blk in streamed:
        in_specs.append(pl.BlockSpec(blk, stream_map(a.ndim)))
    return pl.pallas_call(
        kernel,
        grid_spec=pltpu.PrefetchScalarGridSpec(
            num_scalar_prefetch=1,
            grid=(nblocks,),
            in_specs=in_specs,
            out_specs=[pl.BlockSpec(o.shape, fixed_map(len(o.shape))) for o in outs],
            scratch_shapes=scratch,
        ),
        out_shape=outs,
        compiler_params=pltpu.CompilerParams(dimension_semantics=("arbitrary",)),
    )(rng, *fixed, *[a for a, _ in streamed])


def body(queries, keys, values, grad_out, frame_counts):
    n_head = lax.axis_size("head")
    n_tm = lax.axis_size("tm")
    heads_here = HEADS // n_head
    scale = 1.0 / math.sqrt(DH)
    rows_in = queries.shape[0]
    def exchange(arrays):
        packed = jnp.stack([a.reshape(rows_in, HEADS, DH) for a in arrays], axis=2)
        packed = packed.reshape(rows_in, HEADS * len(arrays) * DH)
        got = lax.all_to_all(packed, "head", split_axis=1, concat_axis=0, tiled=True)
        return got.reshape(got.shape[0], heads_here, len(arrays), DH)

    mine_kv = exchange((keys, values))
    mine_qg = exchange((queries, grad_out))
    rows = mine_kv.shape[0]
    per = rows // KBLOCK
    nkeys = rows * n_tm
    nk = nkeys // KBLOCK
    bounds = jnp.cumsum(frame_counts)[:-1].astype(jnp.int32)
    offset = lax.axis_index("tm") * rows
    seg_own = segment_of(offset + jnp.arange(rows, dtype=jnp.int32), bounds)
    seg_keys = segment_of(jnp.arange(nkeys, dtype=jnp.int32), bounds)
    starts = jnp.concatenate([jnp.zeros((1,), jnp.int32), bounds])
    ends = jnp.concatenate([bounds, jnp.full((1,), nkeys, jnp.int32)])
    kstart = starts[seg_own[0]]
    kend = ends[seg_own[rows - 1]]
    rng = jnp.clip(jnp.stack([kstart // KBLOCK, (kend - 1) // KBLOCK]), 0, nk - 1).astype(jnp.int32)
    segq = seg_own.reshape(rows, 1)
    segk = seg_keys.reshape(n_tm, 1, rows)
    f32 = jnp.float32
    bf16 = jnp.bfloat16

    outs_a, outs_b = [], []
    for h in range(heads_here):
        own_k, own_v = mine_kv[:, h, 0, :], mine_kv[:, h, 1, :]
        own_q, own_g = mine_qg[:, h, 0, :], mine_qg[:, h, 1, :]
        kv_t = jnp.stack([own_k.T, own_v.T])[None]
        qg_t = jnp.stack([own_q.T, own_g.T])[None]
        all_kv = lax.all_gather(kv_t, "tm", axis=0, tiled=True)
        all_qg = lax.all_gather(qg_t, "tm", axis=0, tiled=True)
        att, lse, delta = block_call(
            lambda *refs: fwd_kernel(*refs, scale=scale), rng,
            [segq, own_q, own_g],
            [(all_kv, (None, 2, DH, KBLOCK)), (segk, (None, 1, KBLOCK))],
            [jax.ShapeDtypeStruct((rows, DH), bf16), jax.ShapeDtypeStruct((rows, 1), f32),
             jax.ShapeDtypeStruct((rows, 1), f32)],
            [pltpu.VMEM((rows, 1), f32), pltpu.VMEM((rows, 1), f32), pltpu.VMEM((rows, DH), f32),
             pltpu.VMEM((KBLOCK, DH), bf16), pltpu.VMEM((KBLOCK, DH), bf16)],
            nk, per,
        )
        (dq,) = block_call(
            lambda *refs: dq_kernel(*refs, scale=scale), rng,
            [segq, own_q, own_g, lse, delta],
            [(all_kv, (None, 2, DH, KBLOCK)), (segk, (None, 1, KBLOCK))],
            [jax.ShapeDtypeStruct((rows, DH), bf16)],
            [pltpu.VMEM((rows, DH), f32), pltpu.VMEM((KBLOCK, DH), bf16), pltpu.VMEM((KBLOCK, DH), bf16)],
            nk, per,
        )
        stats = jnp.stack([lse.reshape(rows), delta.reshape(rows)])
        hi_part = lax.reduce_precision(stats, exponent_bits=8, mantissa_bits=7)
        rest = stats - hi_part
        mid_part = lax.reduce_precision(rest, exponent_bits=8, mantissa_bits=7)
        lo_part = rest - mid_part
        split = jnp.pad(jnp.concatenate([hi_part, mid_part, lo_part]), ((0, STAT_ROWS - 6), (0, 0))).astype(bf16)[None]
        all_stats = lax.all_gather(split, "tm", axis=0, tiled=True)
        dk, dv = block_call(
            lambda *refs: dkv_kernel(*refs, scale=scale), rng,
            [segq, own_k, own_v],
            [(all_qg, (None, 2, DH, KBLOCK)), (all_stats, (None, STAT_ROWS, KBLOCK)),
             (segk, (None, 1, KBLOCK))],
            [jax.ShapeDtypeStruct((rows, DH), bf16), jax.ShapeDtypeStruct((rows, DH), bf16)],
            [pltpu.VMEM((rows, DH), f32), pltpu.VMEM((rows, DH), f32), pltpu.VMEM((KBLOCK, DH), bf16), pltpu.VMEM((KBLOCK, DH), bf16)],
            nk, per,
        )
        outs_a.append(jnp.stack([att, dq], axis=1))
        outs_b.append(jnp.stack([dk, dv], axis=1))

    def send_back(parts):
        packed = jnp.stack(parts, axis=1).reshape(rows, heads_here * 2 * DH)
        back = lax.all_to_all(packed, "head", split_axis=0, concat_axis=1, tiled=True)
        back = back.reshape(rows_in, HEADS, 2, DH)
        return back[:, :, 0, :].reshape(rows_in, HEADS * DH), back[:, :, 1, :].reshape(rows_in, HEADS * DH)

    attended, grad_q = send_back(outs_a)
    grad_k, grad_v = send_back(outs_b)
    return attended, grad_q, grad_k, grad_v


def solution(mesh):
    placed = (
        P(("tm", "head"), None),
        P(("tm", "head"), None),
        P(("tm", "head"), None),
        P(("tm", "head"), None),
        P(),
    )
    return jax.shard_map(
        body,
        mesh=mesh,
        in_specs=placed,
        out_specs=(
            P(("tm", "head"), None),
            P(("tm", "head"), None),
            P(("tm", "head"), None),
            P(("tm", "head"), None),
        ),
        check_vma=False,
    )
```

```python
import math

import jax
import jax.numpy as jnp
from jax import lax
from jax.experimental import pallas as pl
from jax.experimental.pallas import tpu as pltpu
from jax.sharding import PartitionSpec as P

HEADS = 8
DH = 96
KBLOCK = 512
TQ = 256
NEG = -1e30
STAT_ROWS = 48
NT = (((1,), (1,)), ((), ()))


def segment_of(index, bounds):
    return jnp.sum((index[:, None] >= bounds[None, :]).astype(jnp.int32), axis=1)


def fwd_kernel(rng_ref, segq_ref, q_ref, g_ref, kv_ref, segk_ref,
               att_ref, lse_ref, delta_ref, m_sc, l_sc, acc_sc, k_sc, v_sc, *, scale):
    t = pl.program_id(0)
    j = pl.program_id(1)
    lo = rng_ref[t]
    hi = rng_ref[pl.num_programs(0) + t]

    @pl.when(j == 0)
    def _():
        m_sc[...] = jnp.full(m_sc.shape, NEG, jnp.float32)
        l_sc[...] = jnp.zeros(l_sc.shape, jnp.float32)
        acc_sc[...] = jnp.zeros(acc_sc.shape, jnp.float32)

    @pl.when(lo + j <= hi)
    def _():
        k_sc[...] = kv_ref[0].T
        v_sc[...] = kv_ref[1].T
        k = k_sc[...]
        v = v_sc[...]
        s = lax.dot_general(q_ref[...], k, NT, preferred_element_type=jnp.float32) * scale
        vis = segq_ref[...] == segk_ref[...]
        m_prev = m_sc[...]
        m_new = jnp.maximum(m_prev, jnp.max(jnp.where(vis, s, NEG), axis=1, keepdims=True))
        alpha = jnp.exp(m_prev - m_new)
        p = jnp.where(vis, jnp.exp(s - m_new), 0.0)
        l_sc[...] = l_sc[...] * alpha + jnp.sum(p, axis=1, keepdims=True)
        acc_sc[...] = acc_sc[...] * alpha + jnp.dot(
            p.astype(jnp.bfloat16), v, preferred_element_type=jnp.float32)
        m_sc[...] = m_new

    @pl.when(j == pl.num_programs(1) - 1)
    def _():
        total = l_sc[...]
        att = (acc_sc[...] / total).astype(jnp.bfloat16)
        att_ref[...] = att
        lse_ref[...] = m_sc[...] + jnp.log(total)
        delta_ref[...] = jnp.sum(g_ref[...].astype(jnp.float32) * att.astype(jnp.float32),
                                 axis=1, keepdims=True)


def dq_kernel(rng_ref, segq_ref, q_ref, g_ref, lse_ref, delta_ref, kv_ref, segk_ref,
              dq_ref, dq_sc, k_sc, v_sc, *, scale):
    t = pl.program_id(0)
    j = pl.program_id(1)
    lo = rng_ref[t]
    hi = rng_ref[pl.num_programs(0) + t]

    @pl.when(j == 0)
    def _():
        dq_sc[...] = jnp.zeros(dq_sc.shape, jnp.float32)

    @pl.when(lo + j <= hi)
    def _():
        k_sc[...] = kv_ref[0].T
        v_sc[...] = kv_ref[1].T
        k = k_sc[...]
        v = v_sc[...]
        s = lax.dot_general(q_ref[...], k, NT, preferred_element_type=jnp.float32) * scale
        vis = segq_ref[...] == segk_ref[...]
        w = jnp.where(vis, jnp.exp(s - lse_ref[...]), 0.0)
        dp = lax.dot_general(g_ref[...], v, NT, preferred_element_type=jnp.float32)
        ds = (w * (dp - delta_ref[...])).astype(jnp.bfloat16)
        dq_sc[...] += jnp.dot(ds, k, preferred_element_type=jnp.float32)

    @pl.when(j == pl.num_programs(1) - 1)
    def _():
        dq_ref[...] = (scale * dq_sc[...]).astype(jnp.bfloat16)


def dkv_kernel(rng_ref, segown_ref, k_ref, v_ref, qg_ref, st_ref, segk_ref,
               dk_ref, dv_ref, dk_sc, dv_sc, q_sc, g_sc, *, scale):
    t = pl.program_id(0)
    i = pl.program_id(1)
    lo = rng_ref[t]
    hi = rng_ref[pl.num_programs(0) + t]

    @pl.when(i == 0)
    def _():
        dk_sc[...] = jnp.zeros(dk_sc.shape, jnp.float32)
        dv_sc[...] = jnp.zeros(dv_sc.shape, jnp.float32)

    @pl.when(lo + i <= hi)
    def _():
        q_sc[...] = qg_ref[0].T
        g_sc[...] = qg_ref[1].T
        q = q_sc[...]
        g = g_sc[...]
        parts = st_ref[...].astype(jnp.float32)
        stats = (parts[0:2, :] + parts[2:4, :]) + parts[4:6, :]
        s_t = lax.dot_general(k_ref[...], q, NT, preferred_element_type=jnp.float32) * scale
        vis = segown_ref[...] == segk_ref[...]
        w_t = jnp.where(vis, jnp.exp(s_t - stats[0:1, :]), 0.0)
        dp_t = lax.dot_general(v_ref[...], g, NT, preferred_element_type=jnp.float32)
        ds_t = (w_t * (dp_t - stats[1:2, :])).astype(jnp.bfloat16)
        dk_sc[...] += jnp.dot(ds_t, q, preferred_element_type=jnp.float32)
        dv_sc[...] += jnp.dot(w_t.astype(jnp.bfloat16), g, preferred_element_type=jnp.float32)

    @pl.when(i == pl.num_programs(1) - 1)
    def _():
        dk_ref[...] = (scale * dk_sc[...]).astype(jnp.bfloat16)
        dv_ref[...] = dv_sc[...].astype(jnp.bfloat16)


def block_call(kernel, rng, tiled, streamed, outs, scratch, ntiles, nblocks, per):
    def tile_map(i, j, r):
        return (i, 0)

    def stream_map(nd):
        def index(i, j, r):
            b = jnp.minimum(r[i] + j, r[ntiles + i])
            return (b // per,) + (0,) * (nd - 2) + (b % per,)
        return index

    in_specs = [pl.BlockSpec((TQ,) + a.shape[1:], tile_map) for a in tiled]
    for a, blk in streamed:
        in_specs.append(pl.BlockSpec(blk, stream_map(a.ndim)))
    return pl.pallas_call(
        kernel,
        grid_spec=pltpu.PrefetchScalarGridSpec(
            num_scalar_prefetch=1,
            grid=(ntiles, nblocks),
            in_specs=in_specs,
            out_specs=[pl.BlockSpec((TQ,) + tuple(o.shape[1:]), tile_map) for o in outs],
            scratch_shapes=scratch,
        ),
        out_shape=outs,
        compiler_params=pltpu.CompilerParams(dimension_semantics=("arbitrary", "arbitrary")),
    )(rng, *tiled, *[a for a, _ in streamed])


def body(queries, keys, values, grad_out, frame_counts):
    n_head = lax.axis_size("head")
    n_tm = lax.axis_size("tm")
    heads_here = HEADS // n_head
    scale = 1.0 / math.sqrt(DH)
    rows_in = queries.shape[0]
    def exchange(arrays):
        packed = jnp.stack([a.reshape(rows_in, HEADS, DH) for a in arrays], axis=2)
        packed = packed.reshape(rows_in, HEADS * len(arrays) * DH)
        got = lax.all_to_all(packed, "head", split_axis=1, concat_axis=0, tiled=True)
        return got.reshape(got.shape[0], heads_here, len(arrays), DH)

    mine_kv = exchange((keys, values))
    mine_qg = exchange((queries, grad_out))
    rows = mine_kv.shape[0]
    per = rows // KBLOCK
    nkeys = rows * n_tm
    nk = nkeys // KBLOCK
    bounds = jnp.cumsum(frame_counts)[:-1].astype(jnp.int32)
    offset = lax.axis_index("tm") * rows
    seg_own = segment_of(offset + jnp.arange(rows, dtype=jnp.int32), bounds)
    seg_keys = segment_of(jnp.arange(nkeys, dtype=jnp.int32), bounds)
    starts = jnp.concatenate([jnp.zeros((1,), jnp.int32), bounds])
    ends = jnp.concatenate([bounds, jnp.full((1,), nkeys, jnp.int32)])
    ntiles = rows // TQ
    kstart = starts[seg_own[0::TQ]]
    kend = ends[seg_own[TQ - 1::TQ]]
    rng = jnp.clip(jnp.concatenate([kstart // KBLOCK, (kend - 1) // KBLOCK]), 0, nk - 1).astype(jnp.int32)
    segq = seg_own.reshape(rows, 1)
    segk = seg_keys.reshape(n_tm, 1, rows)
    f32 = jnp.float32
    bf16 = jnp.bfloat16

    outs_a, outs_b = [], []
    for h in range(heads_here):
        own_k, own_v = mine_kv[:, h, 0, :], mine_kv[:, h, 1, :]
        own_q, own_g = mine_qg[:, h, 0, :], mine_qg[:, h, 1, :]
        kv_t = jnp.stack([own_k.T, own_v.T])[None]
        qg_t = jnp.stack([own_q.T, own_g.T])[None]
        all_kv = lax.all_gather(kv_t, "tm", axis=0, tiled=True)
        all_qg = lax.all_gather(qg_t, "tm", axis=0, tiled=True)
        att, lse, delta = block_call(
            lambda *refs: fwd_kernel(*refs, scale=scale), rng,
            [segq, own_q, own_g],
            [(all_kv, (None, 2, DH, KBLOCK)), (segk, (None, 1, KBLOCK))],
            [jax.ShapeDtypeStruct((rows, DH), bf16), jax.ShapeDtypeStruct((rows, 1), f32),
             jax.ShapeDtypeStruct((rows, 1), f32)],
            [pltpu.VMEM((TQ, 1), f32), pltpu.VMEM((TQ, 1), f32), pltpu.VMEM((TQ, DH), f32),
             pltpu.VMEM((KBLOCK, DH), bf16), pltpu.VMEM((KBLOCK, DH), bf16)],
            ntiles, nk, per,
        )
        (dq,) = block_call(
            lambda *refs: dq_kernel(*refs, scale=scale), rng,
            [segq, own_q, own_g, lse, delta],
            [(all_kv, (None, 2, DH, KBLOCK)), (segk, (None, 1, KBLOCK))],
            [jax.ShapeDtypeStruct((rows, DH), bf16)],
            [pltpu.VMEM((TQ, DH), f32), pltpu.VMEM((KBLOCK, DH), bf16), pltpu.VMEM((KBLOCK, DH), bf16)],
            ntiles, nk, per,
        )
        stats = jnp.stack([lse.reshape(rows), delta.reshape(rows)])
        hi_part = lax.reduce_precision(stats, exponent_bits=8, mantissa_bits=7)
        rest = stats - hi_part
        mid_part = lax.reduce_precision(rest, exponent_bits=8, mantissa_bits=7)
        lo_part = rest - mid_part
        split = jnp.pad(jnp.concatenate([hi_part, mid_part, lo_part]), ((0, STAT_ROWS - 6), (0, 0))).astype(bf16)[None]
        all_stats = lax.all_gather(split, "tm", axis=0, tiled=True)
        dk, dv = block_call(
            lambda *refs: dkv_kernel(*refs, scale=scale), rng,
            [segq, own_k, own_v],
            [(all_qg, (None, 2, DH, KBLOCK)), (all_stats, (None, STAT_ROWS, KBLOCK)),
             (segk, (None, 1, KBLOCK))],
            [jax.ShapeDtypeStruct((rows, DH), bf16), jax.ShapeDtypeStruct((rows, DH), bf16)],
            [pltpu.VMEM((TQ, DH), f32), pltpu.VMEM((TQ, DH), f32), pltpu.VMEM((KBLOCK, DH), bf16), pltpu.VMEM((KBLOCK, DH), bf16)],
            ntiles, nk, per,
        )
        outs_a.append(jnp.stack([att, dq], axis=1))
        outs_b.append(jnp.stack([dk, dv], axis=1))

    def send_back(parts):
        packed = jnp.stack(parts, axis=1).reshape(rows, heads_here * 2 * DH)
        back = lax.all_to_all(packed, "head", split_axis=0, concat_axis=1, tiled=True)
        back = back.reshape(rows_in, HEADS, 2, DH)
        return back[:, :, 0, :].reshape(rows_in, HEADS * DH), back[:, :, 1, :].reshape(rows_in, HEADS * DH)

    attended, grad_q = send_back(outs_a)
    grad_k, grad_v = send_back(outs_b)
    return attended, grad_q, grad_k, grad_v


def solution(mesh):
    placed = (
        P(("tm", "head"), None),
        P(("tm", "head"), None),
        P(("tm", "head"), None),
        P(("tm", "head"), None),
        P(),
    )
    return jax.shard_map(
        body,
        mesh=mesh,
        in_specs=placed,
        out_specs=(
            P(("tm", "head"), None),
            P(("tm", "head"), None),
            P(("tm", "head"), None),
            P(("tm", "head"), None),
        ),
        check_vma=False,
    )
```

```python
import functools
import math

import jax
import jax.numpy as jnp
from jax import lax
from jax.experimental import pallas as pl
from jax.experimental.pallas import tpu as pltpu
from jax.sharding import PartitionSpec as P

HEADS = 8
DH = 96
KBLOCK = 512
TQ = 256
NEG = -1e30
STAT_ROWS = 48
NT = (((1,), (1,)), ((), ()))


def segment_of(index, bounds):
    return jnp.sum((index[:, None] >= bounds[None, :]).astype(jnp.int32), axis=1)


def key_segments(rng_ref, b, nskip, nbounds):
    kidx = b * KBLOCK + lax.broadcasted_iota(jnp.int32, (1, KBLOCK), 1)
    seg = jnp.zeros((1, KBLOCK), jnp.int32)
    for u in range(nbounds):
        seg = seg + (kidx >= rng_ref[nskip + u]).astype(jnp.int32)
    return seg


def block_slice(b, per):
    return b // per, pl.ds(pl.multiple_of((b % per) * KBLOCK, KBLOCK), KBLOCK)


def fwd_kernel(rng_ref, segq_ref, q_ref, g_ref, kv_hbm, att_ref, lse_ref, delta_ref,
               buf, sem, m_sc, l_sc, acc_sc, k_sc, v_sc, *, scale, ntiles, nbounds, per):
    def fetch(b, slot):
        dev, cols = block_slice(b, per)
        return pltpu.make_async_copy(kv_hbm.at[dev, :, :, cols], buf.at[slot], sem.at[slot])

    for t in range(ntiles):
        lo = rng_ref[t]
        hi = rng_ref[ntiles + t]
        rows = pl.ds(t * TQ, TQ)
        m_sc[...] = jnp.full(m_sc.shape, NEG, jnp.float32)
        l_sc[...] = jnp.zeros(l_sc.shape, jnp.float32)
        acc_sc[...] = jnp.zeros(acc_sc.shape, jnp.float32)
        fetch(lo, 0).start()

        def step(b, carry):
            slot = (b - lo) % 2

            @pl.when(b < hi)
            def _():
                fetch(b + 1, 1 - slot).start()

            fetch(b, slot).wait()
            k_sc[...] = buf[slot, 0].T
            v_sc[...] = buf[slot, 1].T
            s = lax.dot_general(q_ref[rows, :], k_sc[...], NT,
                                preferred_element_type=jnp.float32) * scale
            vis = segq_ref[rows, :] == key_segments(rng_ref, b, 2 * ntiles, nbounds)
            m_prev = m_sc[...]
            m_new = jnp.maximum(m_prev, jnp.max(jnp.where(vis, s, NEG), axis=1, keepdims=True))
            alpha = jnp.exp(m_prev - m_new)
            p = jnp.where(vis, jnp.exp(s - m_new), 0.0)
            l_sc[...] = l_sc[...] * alpha + jnp.sum(p, axis=1, keepdims=True)
            acc_sc[...] = acc_sc[...] * alpha + jnp.dot(
                p.astype(jnp.bfloat16), v_sc[...], preferred_element_type=jnp.float32)
            m_sc[...] = m_new
            return carry

        lax.fori_loop(lo, hi + 1, step, 0)
        total = l_sc[...]
        att = (acc_sc[...] / total).astype(jnp.bfloat16)
        att_ref[rows, :] = att
        lse_ref[rows, :] = m_sc[...] + jnp.log(total)
        delta_ref[rows, :] = jnp.sum(g_ref[rows, :].astype(jnp.float32) * att.astype(jnp.float32),
                                     axis=1, keepdims=True)


def dq_kernel(rng_ref, segq_ref, q_ref, g_ref, lse_ref, delta_ref, kv_hbm, dq_ref,
              buf, sem, dq_sc, k_sc, v_sc, *, scale, ntiles, nbounds, per):
    def fetch(b, slot):
        dev, cols = block_slice(b, per)
        return pltpu.make_async_copy(kv_hbm.at[dev, :, :, cols], buf.at[slot], sem.at[slot])

    for t in range(ntiles):
        lo = rng_ref[t]
        hi = rng_ref[ntiles + t]
        rows = pl.ds(t * TQ, TQ)
        dq_sc[...] = jnp.zeros(dq_sc.shape, jnp.float32)
        fetch(lo, 0).start()

        def step(b, carry):
            slot = (b - lo) % 2

            @pl.when(b < hi)
            def _():
                fetch(b + 1, 1 - slot).start()

            fetch(b, slot).wait()
            k_sc[...] = buf[slot, 0].T
            v_sc[...] = buf[slot, 1].T
            k = k_sc[...]
            s = lax.dot_general(q_ref[rows, :], k, NT, preferred_element_type=jnp.float32) * scale
            vis = segq_ref[rows, :] == key_segments(rng_ref, b, 2 * ntiles, nbounds)
            w = jnp.where(vis, jnp.exp(s - lse_ref[rows, :]), 0.0)
            dp = lax.dot_general(g_ref[rows, :], v_sc[...], NT, preferred_element_type=jnp.float32)
            ds = (w * (dp - delta_ref[rows, :])).astype(jnp.bfloat16)
            dq_sc[...] += jnp.dot(ds, k, preferred_element_type=jnp.float32)
            return carry

        lax.fori_loop(lo, hi + 1, step, 0)
        dq_ref[rows, :] = (scale * dq_sc[...]).astype(jnp.bfloat16)


def dkv_kernel(rng_ref, segown_ref, k_ref, v_ref, qg_hbm, st_hbm, dk_ref, dv_ref,
               qbuf, sbuf, sem, dk_sc, dv_sc, q_sc, g_sc, *, scale, ntiles, nbounds, per):
    def fetch_q(b, slot):
        dev, cols = block_slice(b, per)
        return pltpu.make_async_copy(qg_hbm.at[dev, :, :, cols], qbuf.at[slot], sem.at[0, slot])

    def fetch_s(b, slot):
        dev, cols = block_slice(b, per)
        return pltpu.make_async_copy(st_hbm.at[dev, :, cols], sbuf.at[slot], sem.at[1, slot])

    for t in range(ntiles):
        lo = rng_ref[t]
        hi = rng_ref[ntiles + t]
        rows = pl.ds(t * TQ, TQ)
        dk_sc[...] = jnp.zeros(dk_sc.shape, jnp.float32)
        dv_sc[...] = jnp.zeros(dv_sc.shape, jnp.float32)
        fetch_q(lo, 0).start()
        fetch_s(lo, 0).start()

        def step(b, carry):
            slot = (b - lo) % 2

            @pl.when(b < hi)
            def _():
                fetch_q(b + 1, 1 - slot).start()
                fetch_s(b + 1, 1 - slot).start()

            fetch_q(b, slot).wait()
            fetch_s(b, slot).wait()
            q_sc[...] = qbuf[slot, 0].T
            g_sc[...] = qbuf[slot, 1].T
            q = q_sc[...]
            g = g_sc[...]
            parts = sbuf[slot].astype(jnp.float32)
            stats = (parts[0:2, :] + parts[2:4, :]) + parts[4:6, :]
            s_t = lax.dot_general(k_ref[rows, :], q, NT, preferred_element_type=jnp.float32) * scale
            vis = segown_ref[rows, :] == key_segments(rng_ref, b, 2 * ntiles, nbounds)
            w_t = jnp.where(vis, jnp.exp(s_t - stats[0:1, :]), 0.0)
            dp_t = lax.dot_general(v_ref[rows, :], g, NT, preferred_element_type=jnp.float32)
            ds_t = (w_t * (dp_t - stats[1:2, :])).astype(jnp.bfloat16)
            dk_sc[...] += jnp.dot(ds_t, q, preferred_element_type=jnp.float32)
            dv_sc[...] += jnp.dot(w_t.astype(jnp.bfloat16), g, preferred_element_type=jnp.float32)
            return carry

        lax.fori_loop(lo, hi + 1, step, 0)
        dk_ref[rows, :] = (scale * dk_sc[...]).astype(jnp.bfloat16)
        dv_ref[rows, :] = dv_sc[...].astype(jnp.bfloat16)


def loop_call(kernel, rng, local, remote, outs, scratch):
    whole = lambda i, r: (0,) * 2
    in_specs = [pl.BlockSpec(a.shape, lambda i, r, nd=a.ndim: (0,) * nd) for a in local]
    in_specs += [pl.BlockSpec(memory_space=pl.ANY) for _ in remote]
    return pl.pallas_call(
        kernel,
        grid_spec=pltpu.PrefetchScalarGridSpec(
            num_scalar_prefetch=1,
            grid=(1,),
            in_specs=in_specs,
            out_specs=[pl.BlockSpec(o.shape, whole) for o in outs],
            scratch_shapes=scratch,
        ),
        out_shape=outs,
        compiler_params=pltpu.CompilerParams(dimension_semantics=("arbitrary",)),
    )(rng, *local, *remote)


def body(queries, keys, values, grad_out, frame_counts):
    n_head = lax.axis_size("head")
    n_tm = lax.axis_size("tm")
    heads_here = HEADS // n_head
    scale = 1.0 / math.sqrt(DH)
    rows_in = queries.shape[0]
    def exchange(arrays):
        packed = jnp.stack([a.reshape(rows_in, HEADS, DH) for a in arrays], axis=2)
        packed = packed.reshape(rows_in, HEADS * len(arrays) * DH)
        got = lax.all_to_all(packed, "head", split_axis=1, concat_axis=0, tiled=True)
        return got.reshape(got.shape[0], heads_here, len(arrays), DH)

    mine_kv = exchange((keys, values))
    mine_qg = exchange((queries, grad_out))
    rows = mine_kv.shape[0]
    per = rows // KBLOCK
    nkeys = rows * n_tm
    nk = nkeys // KBLOCK
    bounds = jnp.cumsum(frame_counts)[:-1].astype(jnp.int32)
    offset = lax.axis_index("tm") * rows
    seg_own = segment_of(offset + jnp.arange(rows, dtype=jnp.int32), bounds)
    seg_keys = segment_of(jnp.arange(nkeys, dtype=jnp.int32), bounds)
    starts = jnp.concatenate([jnp.zeros((1,), jnp.int32), bounds])
    ends = jnp.concatenate([bounds, jnp.full((1,), nkeys, jnp.int32)])
    ntiles = rows // TQ
    kstart = starts[seg_own[0::TQ]]
    kend = ends[seg_own[TQ - 1::TQ]]
    lohi = jnp.clip(jnp.concatenate([kstart // KBLOCK, (kend - 1) // KBLOCK]), 0, nk - 1)
    rng = jnp.concatenate([lohi, bounds]).astype(jnp.int32)
    kw = dict(scale=scale, ntiles=ntiles, nbounds=bounds.shape[0], per=per)
    segq = seg_own.reshape(rows, 1)
    segk = seg_keys.reshape(n_tm, 1, rows)
    f32 = jnp.float32
    bf16 = jnp.bfloat16

    outs_a, outs_b = [], []
    for h in range(heads_here):
        own_k, own_v = mine_kv[:, h, 0, :], mine_kv[:, h, 1, :]
        own_q, own_g = mine_qg[:, h, 0, :], mine_qg[:, h, 1, :]
        kv_t = jnp.stack([own_k.T, own_v.T])[None]
        qg_t = jnp.stack([own_q.T, own_g.T])[None]
        all_kv = lax.all_gather(kv_t, "tm", axis=0, tiled=True)
        all_qg = lax.all_gather(qg_t, "tm", axis=0, tiled=True)
        att, lse, delta = loop_call(
            functools.partial(fwd_kernel, **kw), rng,
            [segq, own_q, own_g], [all_kv],
            [jax.ShapeDtypeStruct((rows, DH), bf16), jax.ShapeDtypeStruct((rows, 1), f32),
             jax.ShapeDtypeStruct((rows, 1), f32)],
            [pltpu.VMEM((2, 2, DH, KBLOCK), bf16), pltpu.SemaphoreType.DMA((2,)),
             pltpu.VMEM((TQ, 1), f32), pltpu.VMEM((TQ, 1), f32), pltpu.VMEM((TQ, DH), f32),
             pltpu.VMEM((KBLOCK, DH), bf16), pltpu.VMEM((KBLOCK, DH), bf16)],
        )
        (dq,) = loop_call(
            functools.partial(dq_kernel, **kw), rng,
            [segq, own_q, own_g, lse, delta], [all_kv],
            [jax.ShapeDtypeStruct((rows, DH), bf16)],
            [pltpu.VMEM((2, 2, DH, KBLOCK), bf16), pltpu.SemaphoreType.DMA((2,)),
             pltpu.VMEM((TQ, DH), f32), pltpu.VMEM((KBLOCK, DH), bf16), pltpu.VMEM((KBLOCK, DH), bf16)],
        )
        stats = jnp.stack([lse.reshape(rows), delta.reshape(rows)])
        hi_part = lax.reduce_precision(stats, exponent_bits=8, mantissa_bits=7)
        rest = stats - hi_part
        mid_part = lax.reduce_precision(rest, exponent_bits=8, mantissa_bits=7)
        lo_part = rest - mid_part
        split = jnp.pad(jnp.concatenate([hi_part, mid_part, lo_part]),
                        ((0, STAT_ROWS - 6), (0, 0))).astype(bf16)[None]
        all_stats = lax.all_gather(split, "tm", axis=0, tiled=True)
        dk, dv = loop_call(
            functools.partial(dkv_kernel, **kw), rng,
            [segq, own_k, own_v], [all_qg, all_stats],
            [jax.ShapeDtypeStruct((rows, DH), bf16), jax.ShapeDtypeStruct((rows, DH), bf16)],
            [pltpu.VMEM((2, 2, DH, KBLOCK), bf16), pltpu.VMEM((2, STAT_ROWS, KBLOCK), bf16),
             pltpu.SemaphoreType.DMA((2, 2)),
             pltpu.VMEM((TQ, DH), f32), pltpu.VMEM((TQ, DH), f32),
             pltpu.VMEM((KBLOCK, DH), bf16), pltpu.VMEM((KBLOCK, DH), bf16)],
        )
        outs_a.append(jnp.stack([att, dq], axis=1))
        outs_b.append(jnp.stack([dk, dv], axis=1))

    def send_back(parts):
        packed = jnp.stack(parts, axis=1).reshape(rows, heads_here * 2 * DH)
        back = lax.all_to_all(packed, "head", split_axis=0, concat_axis=1, tiled=True)
        back = back.reshape(rows_in, HEADS, 2, DH)
        return back[:, :, 0, :].reshape(rows_in, HEADS * DH), back[:, :, 1, :].reshape(rows_in, HEADS * DH)

    attended, grad_q = send_back(outs_a)
    grad_k, grad_v = send_back(outs_b)
    return attended, grad_q, grad_k, grad_v


def solution(mesh):
    placed = (
        P(("tm", "head"), None),
        P(("tm", "head"), None),
        P(("tm", "head"), None),
        P(("tm", "head"), None),
        P(),
    )
    return jax.shard_map(
        body,
        mesh=mesh,
        in_specs=placed,
        out_specs=(
            P(("tm", "head"), None),
            P(("tm", "head"), None),
            P(("tm", "head"), None),
            P(("tm", "head"), None),
        ),
        check_vma=False,
    )
```

```python
import math

import jax
import jax.numpy as jnp
from jax import lax
from jax.experimental import pallas as pl
from jax.experimental.pallas import tpu as pltpu
from jax.sharding import PartitionSpec as P

HEADS = 8
DH = 96
KBLOCK = 1024
TQ = 512
NEG = -1e30
STAT_ROWS = 48
NT = (((1,), (1,)), ((), ()))


def segment_of(index, bounds):
    return jnp.sum((index[:, None] >= bounds[None, :]).astype(jnp.int32), axis=1)


def fwd_kernel(rng_ref, segq_ref, q_ref, g_ref, kv_ref, segk_ref,
               att_ref, lse_ref, delta_ref, m_sc, l_sc, acc_sc, k_sc, v_sc, *, scale):
    t = pl.program_id(0)
    j = pl.program_id(1)
    lo = rng_ref[t]
    hi = rng_ref[pl.num_programs(0) + t]

    @pl.when(j == 0)
    def _():
        m_sc[...] = jnp.full(m_sc.shape, NEG, jnp.float32)
        l_sc[...] = jnp.zeros(l_sc.shape, jnp.float32)
        acc_sc[...] = jnp.zeros(acc_sc.shape, jnp.float32)

    @pl.when(lo + j <= hi)
    def _():
        k_sc[...] = kv_ref[0].T
        v_sc[...] = kv_ref[1].T
        k = k_sc[...]
        v = v_sc[...]
        s = lax.dot_general(q_ref[...], k, NT, preferred_element_type=jnp.float32) * scale
        vis = segq_ref[...] == segk_ref[...]
        m_prev = m_sc[...]
        m_new = jnp.maximum(m_prev, jnp.max(jnp.where(vis, s, NEG), axis=1, keepdims=True))
        alpha = jnp.exp(m_prev - m_new)
        p = jnp.where(vis, jnp.exp(s - m_new), 0.0)
        l_sc[...] = l_sc[...] * alpha + jnp.sum(p, axis=1, keepdims=True)
        acc_sc[...] = acc_sc[...] * alpha + jnp.dot(
            p.astype(jnp.bfloat16), v, preferred_element_type=jnp.float32)
        m_sc[...] = m_new

    @pl.when(j == pl.num_programs(1) - 1)
    def _():
        total = l_sc[...]
        att = (acc_sc[...] / total).astype(jnp.bfloat16)
        att_ref[...] = att
        lse_ref[...] = m_sc[...] + jnp.log(total)
        delta_ref[...] = jnp.sum(g_ref[...].astype(jnp.float32) * att.astype(jnp.float32),
                                 axis=1, keepdims=True)


def dq_kernel(rng_ref, segq_ref, q_ref, g_ref, lse_ref, delta_ref, kv_ref, segk_ref,
              dq_ref, dq_sc, k_sc, v_sc, *, scale):
    t = pl.program_id(0)
    j = pl.program_id(1)
    lo = rng_ref[t]
    hi = rng_ref[pl.num_programs(0) + t]

    @pl.when(j == 0)
    def _():
        dq_sc[...] = jnp.zeros(dq_sc.shape, jnp.float32)

    @pl.when(lo + j <= hi)
    def _():
        k_sc[...] = kv_ref[0].T
        v_sc[...] = kv_ref[1].T
        k = k_sc[...]
        v = v_sc[...]
        s = lax.dot_general(q_ref[...], k, NT, preferred_element_type=jnp.float32) * scale
        vis = segq_ref[...] == segk_ref[...]
        w = jnp.where(vis, jnp.exp(s - lse_ref[...]), 0.0)
        dp = lax.dot_general(g_ref[...], v, NT, preferred_element_type=jnp.float32)
        ds = (w * (dp - delta_ref[...])).astype(jnp.bfloat16)
        dq_sc[...] += jnp.dot(ds, k, preferred_element_type=jnp.float32)

    @pl.when(j == pl.num_programs(1) - 1)
    def _():
        dq_ref[...] = (scale * dq_sc[...]).astype(jnp.bfloat16)


def dkv_kernel(rng_ref, segown_ref, k_ref, v_ref, qg_ref, st_ref, segk_ref,
               dk_ref, dv_ref, dk_sc, dv_sc, q_sc, g_sc, *, scale):
    t = pl.program_id(0)
    i = pl.program_id(1)
    lo = rng_ref[t]
    hi = rng_ref[pl.num_programs(0) + t]

    @pl.when(i == 0)
    def _():
        dk_sc[...] = jnp.zeros(dk_sc.shape, jnp.float32)
        dv_sc[...] = jnp.zeros(dv_sc.shape, jnp.float32)

    @pl.when(lo + i <= hi)
    def _():
        q_sc[...] = qg_ref[0].T
        g_sc[...] = qg_ref[1].T
        q = q_sc[...]
        g = g_sc[...]
        parts = st_ref[...].astype(jnp.float32)
        stats = (parts[0:2, :] + parts[2:4, :]) + parts[4:6, :]
        s_t = lax.dot_general(k_ref[...], q, NT, preferred_element_type=jnp.float32) * scale
        vis = segown_ref[...] == segk_ref[...]
        w_t = jnp.where(vis, jnp.exp(s_t - stats[0:1, :]), 0.0)
        dp_t = lax.dot_general(v_ref[...], g, NT, preferred_element_type=jnp.float32)
        ds_t = (w_t * (dp_t - stats[1:2, :])).astype(jnp.bfloat16)
        dk_sc[...] += jnp.dot(ds_t, q, preferred_element_type=jnp.float32)
        dv_sc[...] += jnp.dot(w_t.astype(jnp.bfloat16), g, preferred_element_type=jnp.float32)

    @pl.when(i == pl.num_programs(1) - 1)
    def _():
        dk_ref[...] = (scale * dk_sc[...]).astype(jnp.bfloat16)
        dv_ref[...] = dv_sc[...].astype(jnp.bfloat16)


def block_call(kernel, rng, tiled, streamed, outs, scratch, ntiles, nblocks, per):
    def tile_map(i, j, r):
        return (i, 0)

    def stream_map(nd):
        def index(i, j, r):
            b = jnp.minimum(r[i] + j, r[ntiles + i])
            return (b // per,) + (0,) * (nd - 2) + (b % per,)
        return index

    in_specs = [pl.BlockSpec((TQ,) + a.shape[1:], tile_map) for a in tiled]
    for a, blk in streamed:
        in_specs.append(pl.BlockSpec(blk, stream_map(a.ndim)))
    return pl.pallas_call(
        kernel,
        grid_spec=pltpu.PrefetchScalarGridSpec(
            num_scalar_prefetch=1,
            grid=(ntiles, nblocks),
            in_specs=in_specs,
            out_specs=[pl.BlockSpec((TQ,) + tuple(o.shape[1:]), tile_map) for o in outs],
            scratch_shapes=scratch,
        ),
        out_shape=outs,
        compiler_params=pltpu.CompilerParams(dimension_semantics=("arbitrary", "arbitrary")),
    )(rng, *tiled, *[a for a, _ in streamed])


def body(queries, keys, values, grad_out, frame_counts):
    n_head = lax.axis_size("head")
    n_tm = lax.axis_size("tm")
    heads_here = HEADS // n_head
    scale = 1.0 / math.sqrt(DH)
    rows_in = queries.shape[0]
    def exchange(arrays):
        packed = jnp.stack([a.reshape(rows_in, HEADS, DH) for a in arrays], axis=2)
        packed = packed.reshape(rows_in, HEADS * len(arrays) * DH)
        got = lax.all_to_all(packed, "head", split_axis=1, concat_axis=0, tiled=True)
        return got.reshape(got.shape[0], heads_here, len(arrays), DH)

    mine_kv = exchange((keys, values))
    mine_qg = exchange((queries, grad_out))
    rows = mine_kv.shape[0]
    per = rows // KBLOCK
    nkeys = rows * n_tm
    nk = nkeys // KBLOCK
    bounds = jnp.cumsum(frame_counts)[:-1].astype(jnp.int32)
    offset = lax.axis_index("tm") * rows
    seg_own = segment_of(offset + jnp.arange(rows, dtype=jnp.int32), bounds)
    seg_keys = segment_of(jnp.arange(nkeys, dtype=jnp.int32), bounds)
    starts = jnp.concatenate([jnp.zeros((1,), jnp.int32), bounds])
    ends = jnp.concatenate([bounds, jnp.full((1,), nkeys, jnp.int32)])
    ntiles = rows // TQ
    kstart = starts[seg_own[0::TQ]]
    kend = ends[seg_own[TQ - 1::TQ]]
    rng = jnp.clip(jnp.concatenate([kstart // KBLOCK, (kend - 1) // KBLOCK]), 0, nk - 1).astype(jnp.int32)
    segq = seg_own.reshape(rows, 1)
    segk = seg_keys.reshape(n_tm, 1, rows)
    f32 = jnp.float32
    bf16 = jnp.bfloat16

    outs_a, outs_b = [], []
    for h in range(heads_here):
        own_k, own_v = mine_kv[:, h, 0, :], mine_kv[:, h, 1, :]
        own_q, own_g = mine_qg[:, h, 0, :], mine_qg[:, h, 1, :]
        kv_t = jnp.stack([own_k.T, own_v.T])[None]
        qg_t = jnp.stack([own_q.T, own_g.T])[None]
        all_kv = lax.all_gather(kv_t, "tm", axis=0, tiled=True)
        all_qg = lax.all_gather(qg_t, "tm", axis=0, tiled=True)
        att, lse, delta = block_call(
            lambda *refs: fwd_kernel(*refs, scale=scale), rng,
            [segq, own_q, own_g],
            [(all_kv, (None, 2, DH, KBLOCK)), (segk, (None, 1, KBLOCK))],
            [jax.ShapeDtypeStruct((rows, DH), bf16), jax.ShapeDtypeStruct((rows, 1), f32),
             jax.ShapeDtypeStruct((rows, 1), f32)],
            [pltpu.VMEM((TQ, 1), f32), pltpu.VMEM((TQ, 1), f32), pltpu.VMEM((TQ, DH), f32),
             pltpu.VMEM((KBLOCK, DH), bf16), pltpu.VMEM((KBLOCK, DH), bf16)],
            ntiles, nk, per,
        )
        (dq,) = block_call(
            lambda *refs: dq_kernel(*refs, scale=scale), rng,
            [segq, own_q, own_g, lse, delta],
            [(all_kv, (None, 2, DH, KBLOCK)), (segk, (None, 1, KBLOCK))],
            [jax.ShapeDtypeStruct((rows, DH), bf16)],
            [pltpu.VMEM((TQ, DH), f32), pltpu.VMEM((KBLOCK, DH), bf16), pltpu.VMEM((KBLOCK, DH), bf16)],
            ntiles, nk, per,
        )
        stats = jnp.stack([lse.reshape(rows), delta.reshape(rows)])
        hi_part = lax.reduce_precision(stats, exponent_bits=8, mantissa_bits=7)
        rest = stats - hi_part
        mid_part = lax.reduce_precision(rest, exponent_bits=8, mantissa_bits=7)
        lo_part = rest - mid_part
        split = jnp.pad(jnp.concatenate([hi_part, mid_part, lo_part]), ((0, STAT_ROWS - 6), (0, 0))).astype(bf16)[None]
        all_stats = lax.all_gather(split, "tm", axis=0, tiled=True)
        dk, dv = block_call(
            lambda *refs: dkv_kernel(*refs, scale=scale), rng,
            [segq, own_k, own_v],
            [(all_qg, (None, 2, DH, KBLOCK)), (all_stats, (None, STAT_ROWS, KBLOCK)),
             (segk, (None, 1, KBLOCK))],
            [jax.ShapeDtypeStruct((rows, DH), bf16), jax.ShapeDtypeStruct((rows, DH), bf16)],
            [pltpu.VMEM((TQ, DH), f32), pltpu.VMEM((TQ, DH), f32), pltpu.VMEM((KBLOCK, DH), bf16), pltpu.VMEM((KBLOCK, DH), bf16)],
            ntiles, nk, per,
        )
        outs_a.append(jnp.stack([att, dq], axis=1))
        outs_b.append(jnp.stack([dk, dv], axis=1))

    def send_back(parts):
        packed = jnp.stack(parts, axis=1).reshape(rows, heads_here * 2 * DH)
        back = lax.all_to_all(packed, "head", split_axis=0, concat_axis=1, tiled=True)
        back = back.reshape(rows_in, HEADS, 2, DH)
        return back[:, :, 0, :].reshape(rows_in, HEADS * DH), back[:, :, 1, :].reshape(rows_in, HEADS * DH)

    attended, grad_q = send_back(outs_a)
    grad_k, grad_v = send_back(outs_b)
    return attended, grad_q, grad_k, grad_v


def solution(mesh):
    placed = (
        P(("tm", "head"), None),
        P(("tm", "head"), None),
        P(("tm", "head"), None),
        P(("tm", "head"), None),
        P(),
    )
    return jax.shard_map(
        body,
        mesh=mesh,
        in_specs=placed,
        out_specs=(
            P(("tm", "head"), None),
            P(("tm", "head"), None),
            P(("tm", "head"), None),
            P(("tm", "head"), None),
        ),
        check_vma=False,
    )
```

```python
import math

import jax
import jax.numpy as jnp
from jax import lax
from jax.experimental import pallas as pl
from jax.experimental.pallas import tpu as pltpu
from jax.sharding import PartitionSpec as P

HEADS = 8
DH = 96
KBLOCK = 1024
TQ = 512
NEG = -1e30
STAT_ROWS = 48
NT = (((1,), (1,)), ((), ()))


def segment_of(index, bounds):
    return jnp.sum((index[:, None] >= bounds[None, :]).astype(jnp.int32), axis=1)


def fwd_kernel(rng_ref, segq_ref, q_ref, g_ref, k_ref, v_ref, segk_ref,
               att_ref, lse_ref, delta_ref, m_sc, l_sc, acc_sc, *, scale):
    t = pl.program_id(0)
    j = pl.program_id(1)
    lo = rng_ref[t]
    hi = rng_ref[pl.num_programs(0) + t]

    @pl.when(j == 0)
    def _():
        m_sc[...] = jnp.full(m_sc.shape, NEG, jnp.float32)
        l_sc[...] = jnp.zeros(l_sc.shape, jnp.float32)
        acc_sc[...] = jnp.zeros(acc_sc.shape, jnp.float32)

    @pl.when(lo + j <= hi)
    def _():
        k = k_ref[...]
        v = v_ref[...]
        s = lax.dot_general(q_ref[...], k, NT, preferred_element_type=jnp.float32) * scale
        vis = segq_ref[...] == segk_ref[...]
        m_prev = m_sc[...]
        m_new = jnp.maximum(m_prev, jnp.max(jnp.where(vis, s, NEG), axis=1, keepdims=True))
        alpha = jnp.exp(m_prev - m_new)
        p = jnp.where(vis, jnp.exp(s - m_new), 0.0)
        l_sc[...] = l_sc[...] * alpha + jnp.sum(p, axis=1, keepdims=True)
        acc_sc[...] = acc_sc[...] * alpha + jnp.dot(
            p.astype(jnp.bfloat16), v, preferred_element_type=jnp.float32)
        m_sc[...] = m_new

    @pl.when(j == pl.num_programs(1) - 1)
    def _():
        total = l_sc[...]
        att = (acc_sc[...] / total).astype(jnp.bfloat16)
        att_ref[...] = att
        lse_ref[...] = m_sc[...] + jnp.log(total)
        delta_ref[...] = jnp.sum(g_ref[...].astype(jnp.float32) * att.astype(jnp.float32),
                                 axis=1, keepdims=True)


def dq_kernel(rng_ref, segq_ref, q_ref, g_ref, lse_ref, delta_ref, k_ref, v_ref, segk_ref,
              dq_ref, dq_sc, *, scale):
    t = pl.program_id(0)
    j = pl.program_id(1)
    lo = rng_ref[t]
    hi = rng_ref[pl.num_programs(0) + t]

    @pl.when(j == 0)
    def _():
        dq_sc[...] = jnp.zeros(dq_sc.shape, jnp.float32)

    @pl.when(lo + j <= hi)
    def _():
        k = k_ref[...]
        v = v_ref[...]
        s = lax.dot_general(q_ref[...], k, NT, preferred_element_type=jnp.float32) * scale
        vis = segq_ref[...] == segk_ref[...]
        w = jnp.where(vis, jnp.exp(s - lse_ref[...]), 0.0)
        dp = lax.dot_general(g_ref[...], v, NT, preferred_element_type=jnp.float32)
        ds = (w * (dp - delta_ref[...])).astype(jnp.bfloat16)
        dq_sc[...] += jnp.dot(ds, k, preferred_element_type=jnp.float32)

    @pl.when(j == pl.num_programs(1) - 1)
    def _():
        dq_ref[...] = (scale * dq_sc[...]).astype(jnp.bfloat16)


def dkv_kernel(rng_ref, segown_ref, k_ref, v_ref, q_ref, g_ref, st_ref, segk_ref,
               dk_ref, dv_ref, dk_sc, dv_sc, *, scale):
    t = pl.program_id(0)
    i = pl.program_id(1)
    lo = rng_ref[t]
    hi = rng_ref[pl.num_programs(0) + t]

    @pl.when(i == 0)
    def _():
        dk_sc[...] = jnp.zeros(dk_sc.shape, jnp.float32)
        dv_sc[...] = jnp.zeros(dv_sc.shape, jnp.float32)

    @pl.when(lo + i <= hi)
    def _():
        q = q_ref[...]
        g = g_ref[...]
        parts = st_ref[...].astype(jnp.float32)
        stats = (parts[0:2, :] + parts[2:4, :]) + parts[4:6, :]
        s_t = lax.dot_general(k_ref[...], q, NT, preferred_element_type=jnp.float32) * scale
        vis = segown_ref[...] == segk_ref[...]
        w_t = jnp.where(vis, jnp.exp(s_t - stats[0:1, :]), 0.0)
        dp_t = lax.dot_general(v_ref[...], g, NT, preferred_element_type=jnp.float32)
        ds_t = (w_t * (dp_t - stats[1:2, :])).astype(jnp.bfloat16)
        dk_sc[...] += jnp.dot(ds_t, q, preferred_element_type=jnp.float32)
        dv_sc[...] += jnp.dot(w_t.astype(jnp.bfloat16), g, preferred_element_type=jnp.float32)

    @pl.when(i == pl.num_programs(1) - 1)
    def _():
        dk_ref[...] = (scale * dk_sc[...]).astype(jnp.bfloat16)
        dv_ref[...] = dv_sc[...].astype(jnp.bfloat16)


def block_call(kernel, rng, tiled, streamed, outs, scratch, ntiles, nblocks, per):
    def tile_map(i, j, r):
        return (i, 0)

    def stream_map(nd):
        def index(i, j, r):
            b = jnp.minimum(r[i] + j, r[ntiles + i])
            if nd == 2:
                return (b, 0)
            return (b // per,) + (0,) * (nd - 2) + (b % per,)
        return index

    in_specs = [pl.BlockSpec((TQ,) + a.shape[1:], tile_map) for a in tiled]
    for a, blk in streamed:
        in_specs.append(pl.BlockSpec(blk, stream_map(a.ndim)))
    return pl.pallas_call(
        kernel,
        grid_spec=pltpu.PrefetchScalarGridSpec(
            num_scalar_prefetch=1,
            grid=(ntiles, nblocks),
            in_specs=in_specs,
            out_specs=[pl.BlockSpec((TQ,) + tuple(o.shape[1:]), tile_map) for o in outs],
            scratch_shapes=scratch,
        ),
        out_shape=outs,
        compiler_params=pltpu.CompilerParams(dimension_semantics=("arbitrary", "arbitrary")),
    )(rng, *tiled, *[a for a, _ in streamed])


def body(queries, keys, values, grad_out, frame_counts):
    n_head = lax.axis_size("head")
    n_tm = lax.axis_size("tm")
    heads_here = HEADS // n_head
    scale = 1.0 / math.sqrt(DH)
    rows_in = queries.shape[0]
    def exchange(arrays):
        packed = jnp.stack([a.reshape(rows_in, HEADS, DH) for a in arrays], axis=2)
        packed = packed.reshape(rows_in, HEADS * len(arrays) * DH)
        got = lax.all_to_all(packed, "head", split_axis=1, concat_axis=0, tiled=True)
        return got.reshape(got.shape[0], heads_here, len(arrays), DH)

    mine_kv = exchange((keys, values))
    mine_qg = exchange((queries, grad_out))
    rows = mine_kv.shape[0]
    per = rows // KBLOCK
    nkeys = rows * n_tm
    nk = nkeys // KBLOCK
    bounds = jnp.cumsum(frame_counts)[:-1].astype(jnp.int32)
    offset = lax.axis_index("tm") * rows
    seg_own = segment_of(offset + jnp.arange(rows, dtype=jnp.int32), bounds)
    seg_keys = segment_of(jnp.arange(nkeys, dtype=jnp.int32), bounds)
    starts = jnp.concatenate([jnp.zeros((1,), jnp.int32), bounds])
    ends = jnp.concatenate([bounds, jnp.full((1,), nkeys, jnp.int32)])
    ntiles = rows // TQ
    kstart = starts[seg_own[0::TQ]]
    kend = ends[seg_own[TQ - 1::TQ]]
    rng = jnp.clip(jnp.concatenate([kstart // KBLOCK, (kend - 1) // KBLOCK]), 0, nk - 1).astype(jnp.int32)
    segq = seg_own.reshape(rows, 1)
    segk = seg_keys.reshape(n_tm, 1, rows)
    f32 = jnp.float32
    bf16 = jnp.bfloat16

    outs_a, outs_b = [], []
    for h in range(heads_here):
        own_k, own_v = mine_kv[:, h, 0, :], mine_kv[:, h, 1, :]
        own_q, own_g = mine_qg[:, h, 0, :], mine_qg[:, h, 1, :]
        kv_t = jnp.stack([own_k.T, own_v.T])[None]
        qg_t = jnp.stack([own_q.T, own_g.T])[None]
        all_kv = lax.all_gather(kv_t, "tm", axis=0, tiled=True)
        all_qg = lax.all_gather(qg_t, "tm", axis=0, tiled=True)
        all_k, all_v = jnp.transpose(all_kv, (1, 0, 3, 2)).reshape(2, nkeys, DH)
        all_q, all_g = jnp.transpose(all_qg, (1, 0, 3, 2)).reshape(2, nkeys, DH)
        att, lse, delta = block_call(
            lambda *refs: fwd_kernel(*refs, scale=scale), rng,
            [segq, own_q, own_g],
            [(all_k, (KBLOCK, DH)), (all_v, (KBLOCK, DH)), (segk, (None, 1, KBLOCK))],
            [jax.ShapeDtypeStruct((rows, DH), bf16), jax.ShapeDtypeStruct((rows, 1), f32),
             jax.ShapeDtypeStruct((rows, 1), f32)],
            [pltpu.VMEM((TQ, 1), f32), pltpu.VMEM((TQ, 1), f32), pltpu.VMEM((TQ, DH), f32)],
            ntiles, nk, per,
        )
        (dq,) = block_call(
            lambda *refs: dq_kernel(*refs, scale=scale), rng,
            [segq, own_q, own_g, lse, delta],
            [(all_k, (KBLOCK, DH)), (all_v, (KBLOCK, DH)), (segk, (None, 1, KBLOCK))],
            [jax.ShapeDtypeStruct((rows, DH), bf16)],
            [pltpu.VMEM((TQ, DH), f32)],
            ntiles, nk, per,
        )
        stats = jnp.stack([lse.reshape(rows), delta.reshape(rows)])
        hi_part = lax.reduce_precision(stats, exponent_bits=8, mantissa_bits=7)
        rest = stats - hi_part
        mid_part = lax.reduce_precision(rest, exponent_bits=8, mantissa_bits=7)
        lo_part = rest - mid_part
        split = jnp.pad(jnp.concatenate([hi_part, mid_part, lo_part]), ((0, STAT_ROWS - 6), (0, 0))).astype(bf16)[None]
        all_stats = lax.all_gather(split, "tm", axis=0, tiled=True)
        dk, dv = block_call(
            lambda *refs: dkv_kernel(*refs, scale=scale), rng,
            [segq, own_k, own_v],
            [(all_q, (KBLOCK, DH)), (all_g, (KBLOCK, DH)), (all_stats, (None, STAT_ROWS, KBLOCK)),
             (segk, (None, 1, KBLOCK))],
            [jax.ShapeDtypeStruct((rows, DH), bf16), jax.ShapeDtypeStruct((rows, DH), bf16)],
            [pltpu.VMEM((TQ, DH), f32), pltpu.VMEM((TQ, DH), f32)],
            ntiles, nk, per,
        )
        outs_a.append(jnp.stack([att, dq], axis=1))
        outs_b.append(jnp.stack([dk, dv], axis=1))

    def send_back(parts):
        packed = jnp.stack(parts, axis=1).reshape(rows, heads_here * 2 * DH)
        back = lax.all_to_all(packed, "head", split_axis=0, concat_axis=1, tiled=True)
        back = back.reshape(rows_in, HEADS, 2, DH)
        return back[:, :, 0, :].reshape(rows_in, HEADS * DH), back[:, :, 1, :].reshape(rows_in, HEADS * DH)

    attended, grad_q = send_back(outs_a)
    grad_k, grad_v = send_back(outs_b)
    return attended, grad_q, grad_k, grad_v


def solution(mesh):
    placed = (
        P(("tm", "head"), None),
        P(("tm", "head"), None),
        P(("tm", "head"), None),
        P(("tm", "head"), None),
        P(),
    )
    return jax.shard_map(
        body,
        mesh=mesh,
        in_specs=placed,
        out_specs=(
            P(("tm", "head"), None),
            P(("tm", "head"), None),
            P(("tm", "head"), None),
            P(("tm", "head"), None),
        ),
        check_vma=False,
    )
```

```python
import functools
import math

import jax
import jax.numpy as jnp
from jax import lax
from jax.experimental import pallas as pl
from jax.experimental.pallas import tpu as pltpu
from jax.sharding import PartitionSpec as P

HEADS = 8
DH = 96
KBLOCK = 1024
TQ = 512
NEG = -1e30
STAT_ROWS = 48
NT = (((1,), (1,)), ((), ()))


def segment_of(index, bounds):
    return jnp.sum((index[:, None] >= bounds[None, :]).astype(jnp.int32), axis=1)


def tile_state(rng_ref, ntiles):
    j = pl.program_id(0)
    t = pl.program_id(1)
    b = rng_ref[0] + j
    live = b <= rng_ref[1]
    mine = jnp.logical_and(live, jnp.logical_and(b >= rng_ref[2 + t], b <= rng_ref[2 + ntiles + t]))
    rows = pl.ds(pl.multiple_of(t * TQ, TQ), TQ)
    return j, t, live, mine, rows


def fwd_kernel(rng_ref, segq_ref, q_ref, g_ref, kv_ref, segk_ref,
               att_ref, lse_ref, delta_ref, m_sc, l_sc, acc_sc, k_sc, v_sc, *, scale, ntiles):
    j, t, live, mine, rows = tile_state(rng_ref, ntiles)

    @pl.when(j == 0)
    def _():
        m_sc[rows, :] = jnp.full((TQ, 1), NEG, jnp.float32)
        l_sc[rows, :] = jnp.zeros((TQ, 1), jnp.float32)
        acc_sc[rows, :] = jnp.zeros((TQ, DH), jnp.float32)

    @pl.when(jnp.logical_and(live, t == 0))
    def _():
        k_sc[...] = kv_ref[0].T
        v_sc[...] = kv_ref[1].T

    @pl.when(mine)
    def _():
        s = lax.dot_general(q_ref[rows, :], k_sc[...], NT, preferred_element_type=jnp.float32) * scale
        vis = segq_ref[rows, :] == segk_ref[...]
        m_prev = m_sc[rows, :]
        m_new = jnp.maximum(m_prev, jnp.max(jnp.where(vis, s, NEG), axis=1, keepdims=True))
        alpha = jnp.exp(m_prev - m_new)
        p = jnp.where(vis, jnp.exp(s - m_new), 0.0)
        l_sc[rows, :] = l_sc[rows, :] * alpha + jnp.sum(p, axis=1, keepdims=True)
        acc_sc[rows, :] = acc_sc[rows, :] * alpha + jnp.dot(
            p.astype(jnp.bfloat16), v_sc[...], preferred_element_type=jnp.float32)
        m_sc[rows, :] = m_new

    @pl.when(j == pl.num_programs(0) - 1)
    def _():
        total = l_sc[rows, :]
        att = (acc_sc[rows, :] / total).astype(jnp.bfloat16)
        att_ref[rows, :] = att
        lse_ref[rows, :] = m_sc[rows, :] + jnp.log(total)
        delta_ref[rows, :] = jnp.sum(g_ref[rows, :].astype(jnp.float32) * att.astype(jnp.float32),
                                     axis=1, keepdims=True)


def dq_kernel(rng_ref, segq_ref, q_ref, g_ref, lse_ref, delta_ref, kv_ref, segk_ref,
              dq_ref, dq_sc, k_sc, v_sc, *, scale, ntiles):
    j, t, live, mine, rows = tile_state(rng_ref, ntiles)

    @pl.when(j == 0)
    def _():
        dq_sc[rows, :] = jnp.zeros((TQ, DH), jnp.float32)

    @pl.when(jnp.logical_and(live, t == 0))
    def _():
        k_sc[...] = kv_ref[0].T
        v_sc[...] = kv_ref[1].T

    @pl.when(mine)
    def _():
        k = k_sc[...]
        s = lax.dot_general(q_ref[rows, :], k, NT, preferred_element_type=jnp.float32) * scale
        vis = segq_ref[rows, :] == segk_ref[...]
        w = jnp.where(vis, jnp.exp(s - lse_ref[rows, :]), 0.0)
        dp = lax.dot_general(g_ref[rows, :], v_sc[...], NT, preferred_element_type=jnp.float32)
        ds = (w * (dp - delta_ref[rows, :])).astype(jnp.bfloat16)
        dq_sc[rows, :] += jnp.dot(ds, k, preferred_element_type=jnp.float32)

    @pl.when(j == pl.num_programs(0) - 1)
    def _():
        dq_ref[rows, :] = (scale * dq_sc[rows, :]).astype(jnp.bfloat16)


def dkv_kernel(rng_ref, segown_ref, k_ref, v_ref, qg_ref, st_ref, segk_ref,
               dk_ref, dv_ref, dk_sc, dv_sc, q_sc, g_sc, *, scale, ntiles):
    j, t, live, mine, rows = tile_state(rng_ref, ntiles)

    @pl.when(j == 0)
    def _():
        dk_sc[rows, :] = jnp.zeros((TQ, DH), jnp.float32)
        dv_sc[rows, :] = jnp.zeros((TQ, DH), jnp.float32)

    @pl.when(jnp.logical_and(live, t == 0))
    def _():
        q_sc[...] = qg_ref[0].T
        g_sc[...] = qg_ref[1].T

    @pl.when(mine)
    def _():
        q = q_sc[...]
        g = g_sc[...]
        parts = st_ref[...].astype(jnp.float32)
        stats = (parts[0:2, :] + parts[2:4, :]) + parts[4:6, :]
        s_t = lax.dot_general(k_ref[rows, :], q, NT, preferred_element_type=jnp.float32) * scale
        vis = segown_ref[rows, :] == segk_ref[...]
        w_t = jnp.where(vis, jnp.exp(s_t - stats[0:1, :]), 0.0)
        dp_t = lax.dot_general(v_ref[rows, :], g, NT, preferred_element_type=jnp.float32)
        ds_t = (w_t * (dp_t - stats[1:2, :])).astype(jnp.bfloat16)
        dk_sc[rows, :] += jnp.dot(ds_t, q, preferred_element_type=jnp.float32)
        dv_sc[rows, :] += jnp.dot(w_t.astype(jnp.bfloat16), g, preferred_element_type=jnp.float32)

    @pl.when(j == pl.num_programs(0) - 1)
    def _():
        dk_ref[rows, :] = (scale * dk_sc[rows, :]).astype(jnp.bfloat16)
        dv_ref[rows, :] = dv_sc[rows, :].astype(jnp.bfloat16)


def block_call(kernel, rng, fixed, streamed, outs, scratch, nblocks, per, ntiles):
    def fixed_map(nd):
        return lambda j, t, r: (0,) * nd

    def stream_map(nd):
        def index(j, t, r):
            b = jnp.minimum(r[0] + j, r[1])
            return (b // per,) + (0,) * (nd - 2) + (b % per,)
        return index

    in_specs = [pl.BlockSpec(a.shape, fixed_map(a.ndim)) for a in fixed]
    for a, blk in streamed:
        in_specs.append(pl.BlockSpec(blk, stream_map(a.ndim)))
    return pl.pallas_call(
        kernel,
        grid_spec=pltpu.PrefetchScalarGridSpec(
            num_scalar_prefetch=1,
            grid=(nblocks, ntiles),
            in_specs=in_specs,
            out_specs=[pl.BlockSpec(o.shape, fixed_map(len(o.shape))) for o in outs],
            scratch_shapes=scratch,
        ),
        out_shape=outs,
        compiler_params=pltpu.CompilerParams(dimension_semantics=("arbitrary", "arbitrary")),
    )(rng, *fixed, *[a for a, _ in streamed])


def body(queries, keys, values, grad_out, frame_counts):
    n_head = lax.axis_size("head")
    n_tm = lax.axis_size("tm")
    heads_here = HEADS // n_head
    scale = 1.0 / math.sqrt(DH)
    rows_in = queries.shape[0]
    def exchange(arrays):
        packed = jnp.stack([a.reshape(rows_in, HEADS, DH) for a in arrays], axis=2)
        packed = packed.reshape(rows_in, HEADS * len(arrays) * DH)
        got = lax.all_to_all(packed, "head", split_axis=1, concat_axis=0, tiled=True)
        return got.reshape(got.shape[0], heads_here, len(arrays), DH)

    mine_kv = exchange((keys, values))
    mine_qg = exchange((queries, grad_out))
    rows = mine_kv.shape[0]
    per = rows // KBLOCK
    nkeys = rows * n_tm
    nk = nkeys // KBLOCK
    bounds = jnp.cumsum(frame_counts)[:-1].astype(jnp.int32)
    offset = lax.axis_index("tm") * rows
    seg_own = segment_of(offset + jnp.arange(rows, dtype=jnp.int32), bounds)
    seg_keys = segment_of(jnp.arange(nkeys, dtype=jnp.int32), bounds)
    starts = jnp.concatenate([jnp.zeros((1,), jnp.int32), bounds])
    ends = jnp.concatenate([bounds, jnp.full((1,), nkeys, jnp.int32)])
    ntiles = rows // TQ
    tstart = starts[seg_own[0::TQ]]
    tend = ends[seg_own[TQ - 1::TQ]]
    rng = jnp.clip(jnp.concatenate([tstart[:1] // KBLOCK, (tend[-1:] - 1) // KBLOCK,
                                    tstart // KBLOCK, (tend - 1) // KBLOCK]), 0, nk - 1).astype(jnp.int32)
    segq = seg_own.reshape(rows, 1)
    segk = seg_keys.reshape(n_tm, 1, rows)
    f32 = jnp.float32
    bf16 = jnp.bfloat16

    outs_a, outs_b = [], []
    for h in range(heads_here):
        own_k, own_v = mine_kv[:, h, 0, :], mine_kv[:, h, 1, :]
        own_q, own_g = mine_qg[:, h, 0, :], mine_qg[:, h, 1, :]
        kv_t = jnp.stack([own_k.T, own_v.T])[None]
        qg_t = jnp.stack([own_q.T, own_g.T])[None]
        all_kv = lax.all_gather(kv_t, "tm", axis=0, tiled=True)
        all_qg = lax.all_gather(qg_t, "tm", axis=0, tiled=True)
        att, lse, delta = block_call(
            lambda *refs: fwd_kernel(*refs, scale=scale, ntiles=ntiles), rng,
            [segq, own_q, own_g],
            [(all_kv, (None, 2, DH, KBLOCK)), (segk, (None, 1, KBLOCK))],
            [jax.ShapeDtypeStruct((rows, DH), bf16), jax.ShapeDtypeStruct((rows, 1), f32),
             jax.ShapeDtypeStruct((rows, 1), f32)],
            [pltpu.VMEM((rows, 1), f32), pltpu.VMEM((rows, 1), f32), pltpu.VMEM((rows, DH), f32),
             pltpu.VMEM((KBLOCK, DH), bf16), pltpu.VMEM((KBLOCK, DH), bf16)],
            nk, per, ntiles,
        )
        (dq,) = block_call(
            lambda *refs: dq_kernel(*refs, scale=scale, ntiles=ntiles), rng,
            [segq, own_q, own_g, lse, delta],
            [(all_kv, (None, 2, DH, KBLOCK)), (segk, (None, 1, KBLOCK))],
            [jax.ShapeDtypeStruct((rows, DH), bf16)],
            [pltpu.VMEM((rows, DH), f32), pltpu.VMEM((KBLOCK, DH), bf16), pltpu.VMEM((KBLOCK, DH), bf16)],
            nk, per, ntiles,
        )
        stats = jnp.stack([lse.reshape(rows), delta.reshape(rows)])
        hi_part = lax.reduce_precision(stats, exponent_bits=8, mantissa_bits=7)
        rest = stats - hi_part
        mid_part = lax.reduce_precision(rest, exponent_bits=8, mantissa_bits=7)
        lo_part = rest - mid_part
        split = jnp.pad(jnp.concatenate([hi_part, mid_part, lo_part]), ((0, STAT_ROWS - 6), (0, 0))).astype(bf16)[None]
        all_stats = lax.all_gather(split, "tm", axis=0, tiled=True)
        dk, dv = block_call(
            lambda *refs: dkv_kernel(*refs, scale=scale, ntiles=ntiles), rng,
            [segq, own_k, own_v],
            [(all_qg, (None, 2, DH, KBLOCK)), (all_stats, (None, STAT_ROWS, KBLOCK)),
             (segk, (None, 1, KBLOCK))],
            [jax.ShapeDtypeStruct((rows, DH), bf16), jax.ShapeDtypeStruct((rows, DH), bf16)],
            [pltpu.VMEM((rows, DH), f32), pltpu.VMEM((rows, DH), f32), pltpu.VMEM((KBLOCK, DH), bf16), pltpu.VMEM((KBLOCK, DH), bf16)],
            nk, per, ntiles,
        )
        outs_a.append(jnp.stack([att, dq], axis=1))
        outs_b.append(jnp.stack([dk, dv], axis=1))

    def send_back(parts):
        packed = jnp.stack(parts, axis=1).reshape(rows, heads_here * 2 * DH)
        back = lax.all_to_all(packed, "head", split_axis=0, concat_axis=1, tiled=True)
        back = back.reshape(rows_in, HEADS, 2, DH)
        return back[:, :, 0, :].reshape(rows_in, HEADS * DH), back[:, :, 1, :].reshape(rows_in, HEADS * DH)

    attended, grad_q = send_back(outs_a)
    grad_k, grad_v = send_back(outs_b)
    return attended, grad_q, grad_k, grad_v


def solution(mesh):
    placed = (
        P(("tm", "head"), None),
        P(("tm", "head"), None),
        P(("tm", "head"), None),
        P(("tm", "head"), None),
        P(),
    )
    return jax.shard_map(
        body,
        mesh=mesh,
        in_specs=placed,
        out_specs=(
            P(("tm", "head"), None),
            P(("tm", "head"), None),
            P(("tm", "head"), None),
            P(("tm", "head"), None),
        ),
        check_vma=False,
    )
```

```python
import functools
import math

import jax
import jax.numpy as jnp
from jax import lax
from jax.experimental import pallas as pl
from jax.experimental.pallas import tpu as pltpu
from jax.sharding import PartitionSpec as P

HEADS = 8
DH = 96
KBLOCK = 1024
TQ = 512
NEG = -1e30
STAT_ROWS = 48
NT = (((1,), (1,)), ((), ()))


def segment_of(index, bounds):
    return jnp.sum((index[:, None] >= bounds[None, :]).astype(jnp.int32), axis=1)


def tile_state(rng_ref, ntiles):
    j = pl.program_id(0)
    t = pl.program_id(1)
    b = rng_ref[0] + j
    live = b <= rng_ref[1]
    mine = jnp.logical_and(live, jnp.logical_and(b >= rng_ref[2 + t], b <= rng_ref[2 + ntiles + t]))
    rows = pl.ds(pl.multiple_of(t * TQ, TQ), TQ)
    return j, t, live, mine, rows


def fwd_kernel(rng_ref, segq_ref, q_ref, g_ref, kv_ref, segk_ref,
               att_ref, lse_ref, delta_ref, m_sc, l_sc, acc_sc, k_sc, v_sc, *, scale, ntiles):
    j, t, live, mine, rows = tile_state(rng_ref, ntiles)

    @pl.when(j == 0)
    def _():
        m_sc[rows, :] = jnp.full((TQ, 1), NEG, jnp.float32)
        l_sc[rows, :] = jnp.zeros((TQ, 1), jnp.float32)
        acc_sc[rows, :] = jnp.zeros((TQ, DH), jnp.float32)

    @pl.when(jnp.logical_and(live, t == 0))
    def _():
        k_sc[...] = kv_ref[0].T
        v_sc[...] = kv_ref[1].T

    @pl.when(mine)
    def _():
        s = lax.dot_general(q_ref[rows, :], k_sc[...], NT, preferred_element_type=jnp.float32) * scale
        vis = segq_ref[rows, :] == segk_ref[...]
        m_prev = m_sc[rows, :]
        m_new = jnp.maximum(m_prev, jnp.max(jnp.where(vis, s, NEG), axis=1, keepdims=True))
        alpha = jnp.exp(m_prev - m_new)
        p = jnp.where(vis, jnp.exp(s - m_new), 0.0)
        l_sc[rows, :] = l_sc[rows, :] * alpha + jnp.sum(p, axis=1, keepdims=True)
        acc_sc[rows, :] = acc_sc[rows, :] * alpha + jnp.dot(
            p.astype(jnp.bfloat16), v_sc[...], preferred_element_type=jnp.float32)
        m_sc[rows, :] = m_new

    @pl.when(j == pl.num_programs(0) - 1)
    def _():
        total = l_sc[rows, :]
        att = (acc_sc[rows, :] / total).astype(jnp.bfloat16)
        att_ref[rows, :] = att
        lse_ref[rows, :] = m_sc[rows, :] + jnp.log(total)
        delta_ref[rows, :] = jnp.sum(g_ref[rows, :].astype(jnp.float32) * att.astype(jnp.float32),
                                     axis=1, keepdims=True)


def dq_kernel(rng_ref, segq_ref, q_ref, g_ref, lse_ref, delta_ref, kv_ref, segk_ref,
              dq_ref, dq_sc, k_sc, v_sc, *, scale, ntiles):
    j, t, live, mine, rows = tile_state(rng_ref, ntiles)

    @pl.when(j == 0)
    def _():
        dq_sc[rows, :] = jnp.zeros((TQ, DH), jnp.float32)

    @pl.when(jnp.logical_and(live, t == 0))
    def _():
        k_sc[...] = kv_ref[0].T
        v_sc[...] = kv_ref[1].T

    @pl.when(mine)
    def _():
        k = k_sc[...]
        s = lax.dot_general(q_ref[rows, :], k, NT, preferred_element_type=jnp.float32) * scale
        vis = segq_ref[rows, :] == segk_ref[...]
        w = jnp.where(vis, jnp.exp(s - lse_ref[rows, :]), 0.0)
        dp = lax.dot_general(g_ref[rows, :], v_sc[...], NT, preferred_element_type=jnp.float32)
        ds = (w * (dp - delta_ref[rows, :])).astype(jnp.bfloat16)
        dq_sc[rows, :] += jnp.dot(ds, k, preferred_element_type=jnp.float32)

    @pl.when(j == pl.num_programs(0) - 1)
    def _():
        dq_ref[rows, :] = (scale * dq_sc[rows, :]).astype(jnp.bfloat16)


def dkv_kernel(rng_ref, segown_ref, k_ref, v_ref, qg_ref, segk_ref,
               dk_ref, dv_ref, dk_sc, dv_sc, q_sc, g_sc, *, scale, ntiles):
    j, t, live, mine, rows = tile_state(rng_ref, ntiles)

    @pl.when(j == 0)
    def _():
        dk_sc[rows, :] = jnp.zeros((TQ, DH), jnp.float32)
        dv_sc[rows, :] = jnp.zeros((TQ, DH), jnp.float32)

    @pl.when(jnp.logical_and(live, t == 0))
    def _():
        q_sc[...] = qg_ref[0:DH, :].T
        g_sc[...] = qg_ref[DH:2 * DH, :].T

    @pl.when(mine)
    def _():
        q = q_sc[...]
        g = g_sc[...]
        parts = qg_ref[2 * DH:2 * DH + 6, :].astype(jnp.float32)
        stats = (parts[0:2, :] + parts[2:4, :]) + parts[4:6, :]
        s_t = lax.dot_general(k_ref[rows, :], q, NT, preferred_element_type=jnp.float32) * scale
        vis = segown_ref[rows, :] == segk_ref[...]
        w_t = jnp.where(vis, jnp.exp(s_t - stats[0:1, :]), 0.0)
        dp_t = lax.dot_general(v_ref[rows, :], g, NT, preferred_element_type=jnp.float32)
        ds_t = (w_t * (dp_t - stats[1:2, :])).astype(jnp.bfloat16)
        dk_sc[rows, :] += jnp.dot(ds_t, q, preferred_element_type=jnp.float32)
        dv_sc[rows, :] += jnp.dot(w_t.astype(jnp.bfloat16), g, preferred_element_type=jnp.float32)

    @pl.when(j == pl.num_programs(0) - 1)
    def _():
        dk_ref[rows, :] = (scale * dk_sc[rows, :]).astype(jnp.bfloat16)
        dv_ref[rows, :] = dv_sc[rows, :].astype(jnp.bfloat16)


def block_call(kernel, rng, fixed, streamed, outs, scratch, nblocks, per, ntiles):
    def fixed_map(nd):
        return lambda j, t, r: (0,) * nd

    def stream_map(nd):
        def index(j, t, r):
            b = jnp.minimum(r[0] + j, r[1])
            return (b // per,) + (0,) * (nd - 2) + (b % per,)
        return index

    in_specs = [pl.BlockSpec(a.shape, fixed_map(a.ndim)) for a in fixed]
    for a, blk in streamed:
        in_specs.append(pl.BlockSpec(blk, stream_map(a.ndim)))
    return pl.pallas_call(
        kernel,
        grid_spec=pltpu.PrefetchScalarGridSpec(
            num_scalar_prefetch=1,
            grid=(nblocks, ntiles),
            in_specs=in_specs,
            out_specs=[pl.BlockSpec(o.shape, fixed_map(len(o.shape))) for o in outs],
            scratch_shapes=scratch,
        ),
        out_shape=outs,
        compiler_params=pltpu.CompilerParams(dimension_semantics=("arbitrary", "arbitrary")),
    )(rng, *fixed, *[a for a, _ in streamed])


def body(queries, keys, values, grad_out, frame_counts):
    n_head = lax.axis_size("head")
    n_tm = lax.axis_size("tm")
    heads_here = HEADS // n_head
    scale = 1.0 / math.sqrt(DH)
    rows_in = queries.shape[0]
    def exchange(arrays):
        packed = jnp.stack([a.reshape(rows_in, HEADS, DH) for a in arrays], axis=2)
        packed = packed.reshape(rows_in, HEADS * len(arrays) * DH)
        got = lax.all_to_all(packed, "head", split_axis=1, concat_axis=0, tiled=True)
        return got.reshape(got.shape[0], heads_here, len(arrays), DH)

    mine_kv = exchange((keys, values))
    mine_qg = exchange((queries, grad_out))
    rows = mine_kv.shape[0]
    per = rows // KBLOCK
    nkeys = rows * n_tm
    nk = nkeys // KBLOCK
    bounds = jnp.cumsum(frame_counts)[:-1].astype(jnp.int32)
    offset = lax.axis_index("tm") * rows
    seg_own = segment_of(offset + jnp.arange(rows, dtype=jnp.int32), bounds)
    seg_keys = segment_of(jnp.arange(nkeys, dtype=jnp.int32), bounds)
    starts = jnp.concatenate([jnp.zeros((1,), jnp.int32), bounds])
    ends = jnp.concatenate([bounds, jnp.full((1,), nkeys, jnp.int32)])
    ntiles = rows // TQ
    tstart = starts[seg_own[0::TQ]]
    tend = ends[seg_own[TQ - 1::TQ]]
    rng = jnp.clip(jnp.concatenate([tstart[:1] // KBLOCK, (tend[-1:] - 1) // KBLOCK,
                                    tstart // KBLOCK, (tend - 1) // KBLOCK]), 0, nk - 1).astype(jnp.int32)
    segq = seg_own.reshape(rows, 1)
    segk = seg_keys.reshape(n_tm, 1, rows)
    f32 = jnp.float32
    bf16 = jnp.bfloat16

    outs_a, outs_b = [], []
    for h in range(heads_here):
        own_k, own_v = mine_kv[:, h, 0, :], mine_kv[:, h, 1, :]
        own_q, own_g = mine_qg[:, h, 0, :], mine_qg[:, h, 1, :]
        kv_t = jnp.stack([own_k.T, own_v.T])[None]
        qg_t = jnp.stack([own_q.T, own_g.T])[None]
        all_kv = lax.all_gather(kv_t, "tm", axis=0, tiled=True)
        att, lse, delta = block_call(
            lambda *refs: fwd_kernel(*refs, scale=scale, ntiles=ntiles), rng,
            [segq, own_q, own_g],
            [(all_kv, (None, 2, DH, KBLOCK)), (segk, (None, 1, KBLOCK))],
            [jax.ShapeDtypeStruct((rows, DH), bf16), jax.ShapeDtypeStruct((rows, 1), f32),
             jax.ShapeDtypeStruct((rows, 1), f32)],
            [pltpu.VMEM((rows, 1), f32), pltpu.VMEM((rows, 1), f32), pltpu.VMEM((rows, DH), f32),
             pltpu.VMEM((KBLOCK, DH), bf16), pltpu.VMEM((KBLOCK, DH), bf16)],
            nk, per, ntiles,
        )
        (dq,) = block_call(
            lambda *refs: dq_kernel(*refs, scale=scale, ntiles=ntiles), rng,
            [segq, own_q, own_g, lse, delta],
            [(all_kv, (None, 2, DH, KBLOCK)), (segk, (None, 1, KBLOCK))],
            [jax.ShapeDtypeStruct((rows, DH), bf16)],
            [pltpu.VMEM((rows, DH), f32), pltpu.VMEM((KBLOCK, DH), bf16), pltpu.VMEM((KBLOCK, DH), bf16)],
            nk, per, ntiles,
        )
        stats = jnp.stack([lse.reshape(rows), delta.reshape(rows)])
        hi_part = lax.reduce_precision(stats, exponent_bits=8, mantissa_bits=7)
        rest = stats - hi_part
        mid_part = lax.reduce_precision(rest, exponent_bits=8, mantissa_bits=7)
        lo_part = rest - mid_part
        split = jnp.pad(jnp.concatenate([hi_part, mid_part, lo_part]), ((0, STAT_ROWS - 6), (0, 0))).astype(bf16)[None]
        qgs = jnp.concatenate([qg_t.reshape(1, 2 * DH, rows), split], axis=1)
        all_qgs = lax.all_gather(qgs, "tm", axis=0, tiled=True)
        dk, dv = block_call(
            lambda *refs: dkv_kernel(*refs, scale=scale, ntiles=ntiles), rng,
            [segq, own_k, own_v],
            [(all_qgs, (None, 2 * DH + STAT_ROWS, KBLOCK)),
             (segk, (None, 1, KBLOCK))],
            [jax.ShapeDtypeStruct((rows, DH), bf16), jax.ShapeDtypeStruct((rows, DH), bf16)],
            [pltpu.VMEM((rows, DH), f32), pltpu.VMEM((rows, DH), f32), pltpu.VMEM((KBLOCK, DH), bf16), pltpu.VMEM((KBLOCK, DH), bf16)],
            nk, per, ntiles,
        )
        outs_a.append(jnp.stack([att, dq], axis=1))
        outs_b.append(jnp.stack([dk, dv], axis=1))

    def send_back(parts):
        packed = jnp.stack(parts, axis=1).reshape(rows, heads_here * 2 * DH)
        back = lax.all_to_all(packed, "head", split_axis=0, concat_axis=1, tiled=True)
        back = back.reshape(rows_in, HEADS, 2, DH)
        return back[:, :, 0, :].reshape(rows_in, HEADS * DH), back[:, :, 1, :].reshape(rows_in, HEADS * DH)

    attended, grad_q = send_back(outs_a)
    grad_k, grad_v = send_back(outs_b)
    return attended, grad_q, grad_k, grad_v


def solution(mesh):
    placed = (
        P(("tm", "head"), None),
        P(("tm", "head"), None),
        P(("tm", "head"), None),
        P(("tm", "head"), None),
        P(),
    )
    return jax.shard_map(
        body,
        mesh=mesh,
        in_specs=placed,
        out_specs=(
            P(("tm", "head"), None),
            P(("tm", "head"), None),
            P(("tm", "head"), None),
            P(("tm", "head"), None),
        ),
        check_vma=False,
    )
```

```python
import functools
import math

import jax
import jax.numpy as jnp
from jax import lax
from jax.experimental import pallas as pl
from jax.experimental.pallas import tpu as pltpu
from jax.sharding import PartitionSpec as P

HEADS = 8
DH = 96
KBLOCK = 512
TQ = 512
NEG = -1e30
STAT_ROWS = 48
NT = (((1,), (1,)), ((), ()))


def segment_of(index, bounds):
    return jnp.sum((index[:, None] >= bounds[None, :]).astype(jnp.int32), axis=1)


def tile_state(rng_ref, ntiles):
    j = pl.program_id(0)
    t = pl.program_id(1)
    b = rng_ref[0] + j
    live = b <= rng_ref[1]
    mine = jnp.logical_and(live, jnp.logical_and(b >= rng_ref[2 + t], b <= rng_ref[2 + ntiles + t]))
    rows = pl.ds(pl.multiple_of(t * TQ, TQ), TQ)
    return j, t, live, mine, rows


def fwd_kernel(rng_ref, segq_ref, q_ref, g_ref, kv_ref, segk_ref,
               att_ref, lse_ref, delta_ref, m_sc, l_sc, acc_sc, k_sc, v_sc, *, scale, ntiles):
    j, t, live, mine, rows = tile_state(rng_ref, ntiles)

    @pl.when(j == 0)
    def _():
        m_sc[rows, :] = jnp.full((TQ, 1), NEG, jnp.float32)
        l_sc[rows, :] = jnp.zeros((TQ, 1), jnp.float32)
        acc_sc[rows, :] = jnp.zeros((TQ, DH), jnp.float32)

    @pl.when(jnp.logical_and(live, t == 0))
    def _():
        k_sc[...] = kv_ref[0].T
        v_sc[...] = kv_ref[1].T

    @pl.when(mine)
    def _():
        s = lax.dot_general(q_ref[rows, :], k_sc[...], NT, preferred_element_type=jnp.float32) * scale
        vis = segq_ref[rows, :] == segk_ref[...]
        m_prev = m_sc[rows, :]
        m_new = jnp.maximum(m_prev, jnp.max(jnp.where(vis, s, NEG), axis=1, keepdims=True))
        alpha = jnp.exp(m_prev - m_new)
        p = jnp.where(vis, jnp.exp(s - m_new), 0.0)
        l_sc[rows, :] = l_sc[rows, :] * alpha + jnp.sum(p, axis=1, keepdims=True)
        acc_sc[rows, :] = acc_sc[rows, :] * alpha + jnp.dot(
            p.astype(jnp.bfloat16), v_sc[...], preferred_element_type=jnp.float32)
        m_sc[rows, :] = m_new

    @pl.when(j == pl.num_programs(0) - 1)
    def _():
        total = l_sc[rows, :]
        att = (acc_sc[rows, :] / total).astype(jnp.bfloat16)
        att_ref[rows, :] = att
        lse_ref[rows, :] = m_sc[rows, :] + jnp.log(total)
        delta_ref[rows, :] = jnp.sum(g_ref[rows, :].astype(jnp.float32) * att.astype(jnp.float32),
                                     axis=1, keepdims=True)


def dq_kernel(rng_ref, segq_ref, q_ref, g_ref, lse_ref, delta_ref, kv_ref, segk_ref,
              dq_ref, dq_sc, k_sc, v_sc, *, scale, ntiles):
    j, t, live, mine, rows = tile_state(rng_ref, ntiles)

    @pl.when(j == 0)
    def _():
        dq_sc[rows, :] = jnp.zeros((TQ, DH), jnp.float32)

    @pl.when(jnp.logical_and(live, t == 0))
    def _():
        k_sc[...] = kv_ref[0].T
        v_sc[...] = kv_ref[1].T

    @pl.when(mine)
    def _():
        k = k_sc[...]
        s = lax.dot_general(q_ref[rows, :], k, NT, preferred_element_type=jnp.float32) * scale
        vis = segq_ref[rows, :] == segk_ref[...]
        w = jnp.where(vis, jnp.exp(s - lse_ref[rows, :]), 0.0)
        dp = lax.dot_general(g_ref[rows, :], v_sc[...], NT, preferred_element_type=jnp.float32)
        ds = (w * (dp - delta_ref[rows, :])).astype(jnp.bfloat16)
        dq_sc[rows, :] += jnp.dot(ds, k, preferred_element_type=jnp.float32)

    @pl.when(j == pl.num_programs(0) - 1)
    def _():
        dq_ref[rows, :] = (scale * dq_sc[rows, :]).astype(jnp.bfloat16)


def dkv_kernel(rng_ref, segown_ref, k_ref, v_ref, qg_ref, st_ref, segk_ref,
               dk_ref, dv_ref, dk_sc, dv_sc, q_sc, g_sc, *, scale, ntiles):
    j, t, live, mine, rows = tile_state(rng_ref, ntiles)

    @pl.when(j == 0)
    def _():
        dk_sc[rows, :] = jnp.zeros((TQ, DH), jnp.float32)
        dv_sc[rows, :] = jnp.zeros((TQ, DH), jnp.float32)

    @pl.when(jnp.logical_and(live, t == 0))
    def _():
        q_sc[...] = qg_ref[0].T
        g_sc[...] = qg_ref[1].T

    @pl.when(mine)
    def _():
        q = q_sc[...]
        g = g_sc[...]
        parts = st_ref[...].astype(jnp.float32)
        stats = (parts[0:2, :] + parts[2:4, :]) + parts[4:6, :]
        s_t = lax.dot_general(k_ref[rows, :], q, NT, preferred_element_type=jnp.float32) * scale
        vis = segown_ref[rows, :] == segk_ref[...]
        w_t = jnp.where(vis, jnp.exp(s_t - stats[0:1, :]), 0.0)
        dp_t = lax.dot_general(v_ref[rows, :], g, NT, preferred_element_type=jnp.float32)
        ds_t = (w_t * (dp_t - stats[1:2, :])).astype(jnp.bfloat16)
        dk_sc[rows, :] += jnp.dot(ds_t, q, preferred_element_type=jnp.float32)
        dv_sc[rows, :] += jnp.dot(w_t.astype(jnp.bfloat16), g, preferred_element_type=jnp.float32)

    @pl.when(j == pl.num_programs(0) - 1)
    def _():
        dk_ref[rows, :] = (scale * dk_sc[rows, :]).astype(jnp.bfloat16)
        dv_ref[rows, :] = dv_sc[rows, :].astype(jnp.bfloat16)


def block_call(kernel, rng, fixed, streamed, outs, scratch, nblocks, per, ntiles):
    def fixed_map(nd):
        return lambda j, t, r: (0,) * nd

    def stream_map(nd):
        def index(j, t, r):
            b = jnp.minimum(r[0] + j, r[1])
            return (b // per,) + (0,) * (nd - 2) + (b % per,)
        return index

    in_specs = [pl.BlockSpec(a.shape, fixed_map(a.ndim)) for a in fixed]
    for a, blk in streamed:
        in_specs.append(pl.BlockSpec(blk, stream_map(a.ndim)))
    return pl.pallas_call(
        kernel,
        grid_spec=pltpu.PrefetchScalarGridSpec(
            num_scalar_prefetch=1,
            grid=(nblocks, ntiles),
            in_specs=in_specs,
            out_specs=[pl.BlockSpec(o.shape, fixed_map(len(o.shape))) for o in outs],
            scratch_shapes=scratch,
        ),
        out_shape=outs,
        compiler_params=pltpu.CompilerParams(dimension_semantics=("arbitrary", "arbitrary")),
    )(rng, *fixed, *[a for a, _ in streamed])


def body(queries, keys, values, grad_out, frame_counts):
    n_head = lax.axis_size("head")
    n_tm = lax.axis_size("tm")
    heads_here = HEADS // n_head
    scale = 1.0 / math.sqrt(DH)
    rows_in = queries.shape[0]
    def exchange(arrays):
        packed = jnp.stack([a.reshape(rows_in, HEADS, DH) for a in arrays], axis=2)
        packed = packed.reshape(rows_in, HEADS * len(arrays) * DH)
        got = lax.all_to_all(packed, "head", split_axis=1, concat_axis=0, tiled=True)
        return got.reshape(got.shape[0], heads_here, len(arrays), DH)

    mine_kv = exchange((keys, values))
    mine_qg = exchange((queries, grad_out))
    rows = mine_kv.shape[0]
    per = rows // KBLOCK
    nkeys = rows * n_tm
    nk = nkeys // KBLOCK
    bounds = jnp.cumsum(frame_counts)[:-1].astype(jnp.int32)
    offset = lax.axis_index("tm") * rows
    seg_own = segment_of(offset + jnp.arange(rows, dtype=jnp.int32), bounds)
    seg_keys = segment_of(jnp.arange(nkeys, dtype=jnp.int32), bounds)
    starts = jnp.concatenate([jnp.zeros((1,), jnp.int32), bounds])
    ends = jnp.concatenate([bounds, jnp.full((1,), nkeys, jnp.int32)])
    ntiles = rows // TQ
    tstart = starts[seg_own[0::TQ]]
    tend = ends[seg_own[TQ - 1::TQ]]
    rng = jnp.clip(jnp.concatenate([tstart[:1] // KBLOCK, (tend[-1:] - 1) // KBLOCK,
                                    tstart // KBLOCK, (tend - 1) // KBLOCK]), 0, nk - 1).astype(jnp.int32)
    segq = seg_own.reshape(rows, 1)
    segk = seg_keys.reshape(n_tm, 1, rows)
    f32 = jnp.float32
    bf16 = jnp.bfloat16

    outs_a, outs_b = [], []
    for h in range(heads_here):
        own_k, own_v = mine_kv[:, h, 0, :], mine_kv[:, h, 1, :]
        own_q, own_g = mine_qg[:, h, 0, :], mine_qg[:, h, 1, :]
        kv_t = jnp.stack([own_k.T, own_v.T])[None]
        qg_t = jnp.stack([own_q.T, own_g.T])[None]
        all_kv = lax.all_gather(kv_t, "tm", axis=0, tiled=True)
        all_qg = lax.all_gather(qg_t, "tm", axis=0, tiled=True)
        att, lse, delta = block_call(
            lambda *refs: fwd_kernel(*refs, scale=scale, ntiles=ntiles), rng,
            [segq, own_q, own_g],
            [(all_kv, (None, 2, DH, KBLOCK)), (segk, (None, 1, KBLOCK))],
            [jax.ShapeDtypeStruct((rows, DH), bf16), jax.ShapeDtypeStruct((rows, 1), f32),
             jax.ShapeDtypeStruct((rows, 1), f32)],
            [pltpu.VMEM((rows, 1), f32), pltpu.VMEM((rows, 1), f32), pltpu.VMEM((rows, DH), f32),
             pltpu.VMEM((KBLOCK, DH), bf16), pltpu.VMEM((KBLOCK, DH), bf16)],
            nk, per, ntiles,
        )
        (dq,) = block_call(
            lambda *refs: dq_kernel(*refs, scale=scale, ntiles=ntiles), rng,
            [segq, own_q, own_g, lse, delta],
            [(all_kv, (None, 2, DH, KBLOCK)), (segk, (None, 1, KBLOCK))],
            [jax.ShapeDtypeStruct((rows, DH), bf16)],
            [pltpu.VMEM((rows, DH), f32), pltpu.VMEM((KBLOCK, DH), bf16), pltpu.VMEM((KBLOCK, DH), bf16)],
            nk, per, ntiles,
        )
        stats = jnp.stack([lse.reshape(rows), delta.reshape(rows)])
        hi_part = lax.reduce_precision(stats, exponent_bits=8, mantissa_bits=7)
        rest = stats - hi_part
        mid_part = lax.reduce_precision(rest, exponent_bits=8, mantissa_bits=7)
        lo_part = rest - mid_part
        split = jnp.pad(jnp.concatenate([hi_part, mid_part, lo_part]), ((0, STAT_ROWS - 6), (0, 0))).astype(bf16)[None]
        all_stats = lax.all_gather(split, "tm", axis=0, tiled=True)
        dk, dv = block_call(
            lambda *refs: dkv_kernel(*refs, scale=scale, ntiles=ntiles), rng,
            [segq, own_k, own_v],
            [(all_qg, (None, 2, DH, KBLOCK)), (all_stats, (None, STAT_ROWS, KBLOCK)),
             (segk, (None, 1, KBLOCK))],
            [jax.ShapeDtypeStruct((rows, DH), bf16), jax.ShapeDtypeStruct((rows, DH), bf16)],
            [pltpu.VMEM((rows, DH), f32), pltpu.VMEM((rows, DH), f32), pltpu.VMEM((KBLOCK, DH), bf16), pltpu.VMEM((KBLOCK, DH), bf16)],
            nk, per, ntiles,
        )
        outs_a.append(jnp.stack([att, dq], axis=1))
        outs_b.append(jnp.stack([dk, dv], axis=1))

    def send_back(parts):
        packed = jnp.stack(parts, axis=1).reshape(rows, heads_here * 2 * DH)
        back = lax.all_to_all(packed, "head", split_axis=0, concat_axis=1, tiled=True)
        back = back.reshape(rows_in, HEADS, 2, DH)
        return back[:, :, 0, :].reshape(rows_in, HEADS * DH), back[:, :, 1, :].reshape(rows_in, HEADS * DH)

    attended, grad_q = send_back(outs_a)
    grad_k, grad_v = send_back(outs_b)
    return attended, grad_q, grad_k, grad_v


def solution(mesh):
    placed = (
        P(("tm", "head"), None),
        P(("tm", "head"), None),
        P(("tm", "head"), None),
        P(("tm", "head"), None),
        P(),
    )
    return jax.shard_map(
        body,
        mesh=mesh,
        in_specs=placed,
        out_specs=(
            P(("tm", "head"), None),
            P(("tm", "head"), None),
            P(("tm", "head"), None),
            P(("tm", "head"), None),
        ),
        check_vma=False,
    )
```

```python
import functools
import math

import jax
import jax.numpy as jnp
from jax import lax
from jax.experimental import pallas as pl
from jax.experimental.pallas import tpu as pltpu
from jax.sharding import PartitionSpec as P

HEADS = 8
DH = 96
KBLOCK = 1024
TQ = 512
NEG = -1e30
STAT_ROWS = 48
NT = (((1,), (1,)), ((), ()))


def segment_of(index, bounds):
    return jnp.sum((index[:, None] >= bounds[None, :]).astype(jnp.int32), axis=1)


def tile_state(rng_ref, ntiles):
    j = pl.program_id(0)
    t = pl.program_id(1)
    b = rng_ref[0] + j
    live = b <= rng_ref[1]
    mine = jnp.logical_and(live, jnp.logical_and(b >= rng_ref[2 + t], b <= rng_ref[2 + ntiles + t]))
    rows = pl.ds(pl.multiple_of(t * TQ, TQ), TQ)
    return j, t, live, mine, rows


def fwd_kernel(rng_ref, segq_ref, q_ref, g_ref, kv_ref, segk_ref,
               att_ref, lse_ref, delta_ref, m_sc, l_sc, acc_sc, k_sc, v_sc, *, scale, ntiles):
    j, t, live, mine, rows = tile_state(rng_ref, ntiles)

    @pl.when(j == 0)
    def _():
        m_sc[rows, :] = jnp.full((TQ, 1), NEG, jnp.float32)
        l_sc[rows, :] = jnp.zeros((TQ, 1), jnp.float32)
        acc_sc[rows, :] = jnp.zeros((TQ, DH), jnp.float32)

    @pl.when(jnp.logical_and(live, t == 0))
    def _():
        k_sc[...] = kv_ref[0].T
        v_sc[...] = kv_ref[1].T

    @pl.when(mine)
    def _():
        s = lax.dot_general(q_ref[rows, :], k_sc[...], NT, preferred_element_type=jnp.float32) * scale
        vis = segq_ref[rows, :] == segk_ref[...]
        m_prev = m_sc[rows, :]
        s_vis = jnp.where(vis, s, NEG)
        m_new = jnp.maximum(m_prev, jnp.max(s_vis, axis=1, keepdims=True))
        alpha = jnp.exp(m_prev - m_new)
        p = jnp.exp(s_vis - m_new)
        l_sc[rows, :] = l_sc[rows, :] * alpha + jnp.sum(p, axis=1, keepdims=True)
        acc_sc[rows, :] = acc_sc[rows, :] * alpha + jnp.dot(
            p.astype(jnp.bfloat16), v_sc[...], preferred_element_type=jnp.float32)
        m_sc[rows, :] = m_new

    @pl.when(j == pl.num_programs(0) - 1)
    def _():
        total = l_sc[rows, :]
        att = (acc_sc[rows, :] / total).astype(jnp.bfloat16)
        att_ref[rows, :] = att
        lse_ref[rows, :] = m_sc[rows, :] + jnp.log(total)
        delta_ref[rows, :] = jnp.sum(g_ref[rows, :].astype(jnp.float32) * att.astype(jnp.float32),
                                     axis=1, keepdims=True)


def dq_kernel(rng_ref, segq_ref, q_ref, g_ref, lse_ref, delta_ref, kv_ref, segk_ref,
              dq_ref, dq_sc, k_sc, v_sc, *, scale, ntiles):
    j, t, live, mine, rows = tile_state(rng_ref, ntiles)

    @pl.when(j == 0)
    def _():
        dq_sc[rows, :] = jnp.zeros((TQ, DH), jnp.float32)

    @pl.when(jnp.logical_and(live, t == 0))
    def _():
        k_sc[...] = kv_ref[0].T
        v_sc[...] = kv_ref[1].T

    @pl.when(mine)
    def _():
        k = k_sc[...]
        s = lax.dot_general(q_ref[rows, :], k, NT, preferred_element_type=jnp.float32) * scale
        vis = segq_ref[rows, :] == segk_ref[...]
        w = jnp.where(vis, jnp.exp(s - lse_ref[rows, :]), 0.0)
        dp = lax.dot_general(g_ref[rows, :], v_sc[...], NT, preferred_element_type=jnp.float32)
        ds = (w * (dp - delta_ref[rows, :])).astype(jnp.bfloat16)
        dq_sc[rows, :] += jnp.dot(ds, k, preferred_element_type=jnp.float32)

    @pl.when(j == pl.num_programs(0) - 1)
    def _():
        dq_ref[rows, :] = (scale * dq_sc[rows, :]).astype(jnp.bfloat16)


def dkv_kernel(rng_ref, segown_ref, k_ref, v_ref, qg_ref, st_ref, segk_ref,
               dk_ref, dv_ref, dk_sc, dv_sc, q_sc, g_sc, *, scale, ntiles):
    j, t, live, mine, rows = tile_state(rng_ref, ntiles)

    @pl.when(j == 0)
    def _():
        dk_sc[rows, :] = jnp.zeros((TQ, DH), jnp.float32)
        dv_sc[rows, :] = jnp.zeros((TQ, DH), jnp.float32)

    @pl.when(jnp.logical_and(live, t == 0))
    def _():
        q_sc[...] = qg_ref[0].T
        g_sc[...] = qg_ref[1].T

    @pl.when(mine)
    def _():
        q = q_sc[...]
        g = g_sc[...]
        parts = st_ref[...].astype(jnp.float32)
        stats = (parts[0:2, :] + parts[2:4, :]) + parts[4:6, :]
        s_t = lax.dot_general(k_ref[rows, :], q, NT, preferred_element_type=jnp.float32) * scale
        vis = segown_ref[rows, :] == segk_ref[...]
        w_t = jnp.where(vis, jnp.exp(s_t - stats[0:1, :]), 0.0)
        dp_t = lax.dot_general(v_ref[rows, :], g, NT, preferred_element_type=jnp.float32)
        ds_t = (w_t * (dp_t - stats[1:2, :])).astype(jnp.bfloat16)
        dk_sc[rows, :] += jnp.dot(ds_t, q, preferred_element_type=jnp.float32)
        dv_sc[rows, :] += jnp.dot(w_t.astype(jnp.bfloat16), g, preferred_element_type=jnp.float32)

    @pl.when(j == pl.num_programs(0) - 1)
    def _():
        dk_ref[rows, :] = (scale * dk_sc[rows, :]).astype(jnp.bfloat16)
        dv_ref[rows, :] = dv_sc[rows, :].astype(jnp.bfloat16)


def block_call(kernel, rng, fixed, streamed, outs, scratch, nblocks, per, ntiles):
    def fixed_map(nd):
        return lambda j, t, r: (0,) * nd

    def stream_map(nd):
        def index(j, t, r):
            b = jnp.minimum(r[0] + j, r[1])
            return (b // per,) + (0,) * (nd - 2) + (b % per,)
        return index

    in_specs = [pl.BlockSpec(a.shape, fixed_map(a.ndim)) for a in fixed]
    for a, blk in streamed:
        in_specs.append(pl.BlockSpec(blk, stream_map(a.ndim)))
    return pl.pallas_call(
        kernel,
        grid_spec=pltpu.PrefetchScalarGridSpec(
            num_scalar_prefetch=1,
            grid=(nblocks, ntiles),
            in_specs=in_specs,
            out_specs=[pl.BlockSpec(o.shape, fixed_map(len(o.shape))) for o in outs],
            scratch_shapes=scratch,
        ),
        out_shape=outs,
        compiler_params=pltpu.CompilerParams(dimension_semantics=("arbitrary", "arbitrary")),
    )(rng, *fixed, *[a for a, _ in streamed])


def body(queries, keys, values, grad_out, frame_counts):
    n_head = lax.axis_size("head")
    n_tm = lax.axis_size("tm")
    heads_here = HEADS // n_head
    scale = 1.0 / math.sqrt(DH)
    rows_in = queries.shape[0]
    def exchange(arrays):
        packed = jnp.stack([a.reshape(rows_in, HEADS, DH) for a in arrays], axis=2)
        packed = packed.reshape(rows_in, HEADS * len(arrays) * DH)
        got = lax.all_to_all(packed, "head", split_axis=1, concat_axis=0, tiled=True)
        return got.reshape(got.shape[0], heads_here, len(arrays), DH)

    mine_kv = exchange((keys, values))
    mine_qg = exchange((queries, grad_out))
    rows = mine_kv.shape[0]
    per = rows // KBLOCK
    nkeys = rows * n_tm
    nk = nkeys // KBLOCK
    bounds = jnp.cumsum(frame_counts)[:-1].astype(jnp.int32)
    offset = lax.axis_index("tm") * rows
    seg_own = segment_of(offset + jnp.arange(rows, dtype=jnp.int32), bounds)
    seg_keys = segment_of(jnp.arange(nkeys, dtype=jnp.int32), bounds)
    starts = jnp.concatenate([jnp.zeros((1,), jnp.int32), bounds])
    ends = jnp.concatenate([bounds, jnp.full((1,), nkeys, jnp.int32)])
    ntiles = rows // TQ
    tstart = starts[seg_own[0::TQ]]
    tend = ends[seg_own[TQ - 1::TQ]]
    rng = jnp.clip(jnp.concatenate([tstart[:1] // KBLOCK, (tend[-1:] - 1) // KBLOCK,
                                    tstart // KBLOCK, (tend - 1) // KBLOCK]), 0, nk - 1).astype(jnp.int32)
    segq = seg_own.reshape(rows, 1)
    segk = seg_keys.reshape(n_tm, 1, rows)
    f32 = jnp.float32
    bf16 = jnp.bfloat16

    outs_a, outs_b = [], []
    for h in range(heads_here):
        own_k, own_v = mine_kv[:, h, 0, :], mine_kv[:, h, 1, :]
        own_q, own_g = mine_qg[:, h, 0, :], mine_qg[:, h, 1, :]
        kv_t = jnp.stack([own_k.T, own_v.T])[None]
        qg_t = jnp.stack([own_q.T, own_g.T])[None]
        all_kv = lax.all_gather(kv_t, "tm", axis=0, tiled=True)
        all_qg = lax.all_gather(qg_t, "tm", axis=0, tiled=True)
        att, lse, delta = block_call(
            lambda *refs: fwd_kernel(*refs, scale=scale, ntiles=ntiles), rng,
            [segq, own_q, own_g],
            [(all_kv, (None, 2, DH, KBLOCK)), (segk, (None, 1, KBLOCK))],
            [jax.ShapeDtypeStruct((rows, DH), bf16), jax.ShapeDtypeStruct((rows, 1), f32),
             jax.ShapeDtypeStruct((rows, 1), f32)],
            [pltpu.VMEM((rows, 1), f32), pltpu.VMEM((rows, 1), f32), pltpu.VMEM((rows, DH), f32),
             pltpu.VMEM((KBLOCK, DH), bf16), pltpu.VMEM((KBLOCK, DH), bf16)],
            nk, per, ntiles,
        )
        (dq,) = block_call(
            lambda *refs: dq_kernel(*refs, scale=scale, ntiles=ntiles), rng,
            [segq, own_q, own_g, lse, delta],
            [(all_kv, (None, 2, DH, KBLOCK)), (segk, (None, 1, KBLOCK))],
            [jax.ShapeDtypeStruct((rows, DH), bf16)],
            [pltpu.VMEM((rows, DH), f32), pltpu.VMEM((KBLOCK, DH), bf16), pltpu.VMEM((KBLOCK, DH), bf16)],
            nk, per, ntiles,
        )
        stats = jnp.stack([lse.reshape(rows), delta.reshape(rows)])
        hi_part = lax.reduce_precision(stats, exponent_bits=8, mantissa_bits=7)
        rest = stats - hi_part
        mid_part = lax.reduce_precision(rest, exponent_bits=8, mantissa_bits=7)
        lo_part = rest - mid_part
        split = jnp.pad(jnp.concatenate([hi_part, mid_part, lo_part]), ((0, STAT_ROWS - 6), (0, 0))).astype(bf16)[None]
        all_stats = lax.all_gather(split, "tm", axis=0, tiled=True)
        dk, dv = block_call(
            lambda *refs: dkv_kernel(*refs, scale=scale, ntiles=ntiles), rng,
            [segq, own_k, own_v],
            [(all_qg, (None, 2, DH, KBLOCK)), (all_stats, (None, STAT_ROWS, KBLOCK)),
             (segk, (None, 1, KBLOCK))],
            [jax.ShapeDtypeStruct((rows, DH), bf16), jax.ShapeDtypeStruct((rows, DH), bf16)],
            [pltpu.VMEM((rows, DH), f32), pltpu.VMEM((rows, DH), f32), pltpu.VMEM((KBLOCK, DH), bf16), pltpu.VMEM((KBLOCK, DH), bf16)],
            nk, per, ntiles,
        )
        outs_a.append(jnp.stack([att, dq], axis=1))
        outs_b.append(jnp.stack([dk, dv], axis=1))

    def send_back(parts):
        packed = jnp.stack(parts, axis=1).reshape(rows, heads_here * 2 * DH)
        back = lax.all_to_all(packed, "head", split_axis=0, concat_axis=1, tiled=True)
        back = back.reshape(rows_in, HEADS, 2, DH)
        return back[:, :, 0, :].reshape(rows_in, HEADS * DH), back[:, :, 1, :].reshape(rows_in, HEADS * DH)

    attended, grad_q = send_back(outs_a)
    grad_k, grad_v = send_back(outs_b)
    return attended, grad_q, grad_k, grad_v


def solution(mesh):
    placed = (
        P(("tm", "head"), None),
        P(("tm", "head"), None),
        P(("tm", "head"), None),
        P(("tm", "head"), None),
        P(),
    )
    return jax.shard_map(
        body,
        mesh=mesh,
        in_specs=placed,
        out_specs=(
            P(("tm", "head"), None),
            P(("tm", "head"), None),
            P(("tm", "head"), None),
            P(("tm", "head"), None),
        ),
        check_vma=False,
    )
```

```python
import functools
import math

import jax
import jax.numpy as jnp
from jax import lax
from jax.experimental import pallas as pl
from jax.experimental.pallas import tpu as pltpu
from jax.sharding import PartitionSpec as P

HEADS = 8
DH = 96
KBLOCK = 1024
TQ = 512
NEG = -1e30
STAT_ROWS = 48
NT = (((1,), (1,)), ((), ()))


def segment_of(index, bounds):
    return jnp.sum((index[:, None] >= bounds[None, :]).astype(jnp.int32), axis=1)


def tile_state(rng_ref, ntiles):
    j = pl.program_id(0)
    t = pl.program_id(1)
    b = rng_ref[0] + j
    live = b <= rng_ref[1]
    mine = jnp.logical_and(live, jnp.logical_and(b >= rng_ref[2 + t], b <= rng_ref[2 + ntiles + t]))
    rows = pl.ds(pl.multiple_of(t * TQ, TQ), TQ)
    return j, t, live, mine, rows


def fwd_kernel(rng_ref, segq_ref, q_ref, g_ref, kv_ref, segk_ref,
               att_ref, lse_ref, delta_ref, m_sc, l_sc, acc_sc, k_sc, v_sc, *, scale, ntiles):
    j, t, live, mine, rows = tile_state(rng_ref, ntiles)

    @pl.when(j == 0)
    def _():
        m_sc[rows, :] = jnp.full((TQ, 1), NEG, jnp.float32)
        l_sc[rows, :] = jnp.zeros((TQ, 1), jnp.float32)
        acc_sc[rows, :] = jnp.zeros((TQ, DH), jnp.float32)

    @pl.when(jnp.logical_and(live, t == 0))
    def _():
        k_sc[...] = kv_ref[0].T
        v_sc[...] = kv_ref[1].T

    @pl.when(mine)
    def _():
        s = lax.dot_general(q_ref[rows, :], k_sc[...], NT, preferred_element_type=jnp.float32) * scale
        vis = segq_ref[rows, :] == segk_ref[...]
        m_prev = m_sc[rows, :]
        s_vis = jnp.where(vis, s, NEG)
        m_new = jnp.maximum(m_prev, jnp.max(s_vis, axis=1, keepdims=True))
        alpha = jnp.exp(m_prev - m_new)
        p = jnp.exp(s_vis - m_new)
        l_sc[rows, :] = l_sc[rows, :] * alpha + jnp.sum(p, axis=1, keepdims=True)
        acc_sc[rows, :] = acc_sc[rows, :] * alpha + jnp.dot(
            p.astype(jnp.bfloat16), v_sc[...], preferred_element_type=jnp.float32)
        m_sc[rows, :] = m_new

    @pl.when(j == pl.num_programs(0) - 1)
    def _():
        total = l_sc[rows, :]
        att = (acc_sc[rows, :] / total).astype(jnp.bfloat16)
        att_ref[rows, :] = att
        lse_ref[rows, :] = m_sc[rows, :] + jnp.log(total)
        delta_ref[rows, :] = jnp.sum(g_ref[rows, :].astype(jnp.float32) * att.astype(jnp.float32),
                                     axis=1, keepdims=True)


def dq_kernel(rng_ref, segq_ref, q_ref, g_ref, lse_ref, delta_ref, kv_ref, segk_ref,
              dq_ref, dq_sc, k_sc, v_sc, *, scale, ntiles):
    j, t, live, mine, rows = tile_state(rng_ref, ntiles)

    @pl.when(j == 0)
    def _():
        dq_sc[rows, :] = jnp.zeros((TQ, DH), jnp.float32)

    @pl.when(jnp.logical_and(live, t == 0))
    def _():
        k_sc[...] = kv_ref[0].T
        v_sc[...] = kv_ref[1].T

    @pl.when(mine)
    def _():
        k = k_sc[...]
        s = lax.dot_general(q_ref[rows, :], k, NT, preferred_element_type=jnp.float32) * scale
        vis = segq_ref[rows, :] == segk_ref[...]
        w = jnp.where(vis, jnp.exp(s - lse_ref[rows, :]), 0.0)
        dp = lax.dot_general(g_ref[rows, :], v_sc[...], NT, preferred_element_type=jnp.float32)
        ds = (w * (dp - delta_ref[rows, :])).astype(jnp.bfloat16)
        dq_sc[rows, :] += jnp.dot(ds, k, preferred_element_type=jnp.float32)

    @pl.when(j == pl.num_programs(0) - 1)
    def _():
        dq_ref[rows, :] = (scale * dq_sc[rows, :]).astype(jnp.bfloat16)


def dkv_kernel(rng_ref, segown_ref, k_ref, v_ref, qg_ref, st_ref, segk_ref,
               dk_ref, dv_ref, dk_sc, dv_sc, q_sc, g_sc, *, scale, ntiles):
    j, t, live, mine, rows = tile_state(rng_ref, ntiles)

    @pl.when(j == 0)
    def _():
        dk_sc[rows, :] = jnp.zeros((TQ, DH), jnp.float32)
        dv_sc[rows, :] = jnp.zeros((TQ, DH), jnp.float32)

    @pl.when(jnp.logical_and(live, t == 0))
    def _():
        q_sc[...] = qg_ref[0].T
        g_sc[...] = qg_ref[1].T

    @pl.when(mine)
    def _():
        q = q_sc[...]
        g = g_sc[...]
        parts = st_ref[...].astype(jnp.float32)
        stats = (parts[0:2, :] + parts[2:4, :]) + parts[4:6, :]
        s_t = lax.dot_general(k_ref[rows, :], q, NT, preferred_element_type=jnp.float32) * scale
        vis = segown_ref[rows, :] == segk_ref[...]
        w_t = jnp.where(vis, jnp.exp(s_t - stats[0:1, :]), 0.0)
        dp_t = lax.dot_general(v_ref[rows, :], g, NT, preferred_element_type=jnp.float32)
        ds_t = (w_t * (dp_t - stats[1:2, :])).astype(jnp.bfloat16)
        dk_sc[rows, :] += jnp.dot(ds_t, q, preferred_element_type=jnp.float32)
        dv_sc[rows, :] += jnp.dot(w_t.astype(jnp.bfloat16), g, preferred_element_type=jnp.float32)

    @pl.when(j == pl.num_programs(0) - 1)
    def _():
        dk_ref[rows, :] = (scale * dk_sc[rows, :]).astype(jnp.bfloat16)
        dv_ref[rows, :] = dv_sc[rows, :].astype(jnp.bfloat16)


def block_call(kernel, rng, fixed, streamed, outs, scratch, nblocks, per, ntiles, flags=None):
    def fixed_map(nd):
        return lambda j, t, r: (0,) * nd

    def stream_map(nd):
        def index(j, t, r):
            b = jnp.minimum(r[0] + j, r[1])
            return (b // per,) + (0,) * (nd - 2) + (b % per,)
        return index

    in_specs = [pl.BlockSpec(a.shape, fixed_map(a.ndim)) for a in fixed]
    for a, blk in streamed:
        in_specs.append(pl.BlockSpec(blk, stream_map(a.ndim)))
    return pl.pallas_call(
        kernel,
        grid_spec=pltpu.PrefetchScalarGridSpec(
            num_scalar_prefetch=1,
            grid=(nblocks, ntiles),
            in_specs=in_specs,
            out_specs=[pl.BlockSpec(o.shape, fixed_map(len(o.shape))) for o in outs],
            scratch_shapes=scratch,
        ),
        out_shape=outs,
        compiler_params=pltpu.CompilerParams(dimension_semantics=("arbitrary", "arbitrary"), flags=flags),
    )(rng, *fixed, *[a for a, _ in streamed])


def body(queries, keys, values, grad_out, frame_counts):
    n_head = lax.axis_size("head")
    n_tm = lax.axis_size("tm")
    heads_here = HEADS // n_head
    scale = 1.0 / math.sqrt(DH)
    rows_in = queries.shape[0]
    def exchange(arrays):
        packed = jnp.stack([a.reshape(rows_in, HEADS, DH) for a in arrays], axis=2)
        packed = packed.reshape(rows_in, HEADS * len(arrays) * DH)
        got = lax.all_to_all(packed, "head", split_axis=1, concat_axis=0, tiled=True)
        return got.reshape(got.shape[0], heads_here, len(arrays), DH)

    mine_kv = exchange((keys, values))
    mine_qg = exchange((queries, grad_out))
    rows = mine_kv.shape[0]
    per = rows // KBLOCK
    nkeys = rows * n_tm
    nk = nkeys // KBLOCK
    bounds = jnp.cumsum(frame_counts)[:-1].astype(jnp.int32)
    offset = lax.axis_index("tm") * rows
    seg_own = segment_of(offset + jnp.arange(rows, dtype=jnp.int32), bounds)
    seg_keys = segment_of(jnp.arange(nkeys, dtype=jnp.int32), bounds)
    starts = jnp.concatenate([jnp.zeros((1,), jnp.int32), bounds])
    ends = jnp.concatenate([bounds, jnp.full((1,), nkeys, jnp.int32)])
    ntiles = rows // TQ
    tstart = starts[seg_own[0::TQ]]
    tend = ends[seg_own[TQ - 1::TQ]]
    rng = jnp.clip(jnp.concatenate([tstart[:1] // KBLOCK, (tend[-1:] - 1) // KBLOCK,
                                    tstart // KBLOCK, (tend - 1) // KBLOCK]), 0, nk - 1).astype(jnp.int32)
    segq = seg_own.reshape(rows, 1)
    segk = seg_keys.reshape(n_tm, 1, rows)
    f32 = jnp.float32
    bf16 = jnp.bfloat16

    outs_a, outs_b = [], []
    for h in range(heads_here):
        own_k, own_v = mine_kv[:, h, 0, :], mine_kv[:, h, 1, :]
        own_q, own_g = mine_qg[:, h, 0, :], mine_qg[:, h, 1, :]
        kv_t = jnp.stack([own_k.T, own_v.T])[None]
        qg_t = jnp.stack([own_q.T, own_g.T])[None]
        all_kv = lax.all_gather(kv_t, "tm", axis=0, tiled=True)
        all_qg = lax.all_gather(qg_t, "tm", axis=0, tiled=True)
        att, lse, delta = block_call(
            lambda *refs: fwd_kernel(*refs, scale=scale, ntiles=ntiles), rng,
            [segq, own_q, own_g],
            [(all_kv, (None, 2, DH, KBLOCK)), (segk, (None, 1, KBLOCK))],
            [jax.ShapeDtypeStruct((rows, DH), bf16), jax.ShapeDtypeStruct((rows, 1), f32),
             jax.ShapeDtypeStruct((rows, 1), f32)],
            [pltpu.VMEM((rows, 1), f32), pltpu.VMEM((rows, 1), f32), pltpu.VMEM((rows, DH), f32),
             pltpu.VMEM((KBLOCK, DH), bf16), pltpu.VMEM((KBLOCK, DH), bf16)],
            nk, per, ntiles,
        )
        (dq,) = block_call(
            lambda *refs: dq_kernel(*refs, scale=scale, ntiles=ntiles), rng,
            [segq, own_q, own_g, lse, delta],
            [(all_kv, (None, 2, DH, KBLOCK)), (segk, (None, 1, KBLOCK))],
            [jax.ShapeDtypeStruct((rows, DH), bf16)],
            [pltpu.VMEM((rows, DH), f32), pltpu.VMEM((KBLOCK, DH), bf16), pltpu.VMEM((KBLOCK, DH), bf16)],
            nk, per, ntiles,
        )
        stats = jnp.stack([lse.reshape(rows), delta.reshape(rows)])
        hi_part = lax.reduce_precision(stats, exponent_bits=8, mantissa_bits=7)
        rest = stats - hi_part
        mid_part = lax.reduce_precision(rest, exponent_bits=8, mantissa_bits=7)
        lo_part = rest - mid_part
        split = jnp.pad(jnp.concatenate([hi_part, mid_part, lo_part]), ((0, STAT_ROWS - 6), (0, 0))).astype(bf16)[None]
        all_stats = lax.all_gather(split, "tm", axis=0, tiled=True)
        dk, dv = block_call(
            lambda *refs: dkv_kernel(*refs, scale=scale, ntiles=ntiles), rng,
            [segq, own_k, own_v],
            [(all_qg, (None, 2, DH, KBLOCK)), (all_stats, (None, STAT_ROWS, KBLOCK)),
             (segk, (None, 1, KBLOCK))],
            [jax.ShapeDtypeStruct((rows, DH), bf16), jax.ShapeDtypeStruct((rows, DH), bf16)],
            [pltpu.VMEM((rows, DH), f32), pltpu.VMEM((rows, DH), f32), pltpu.VMEM((KBLOCK, DH), bf16), pltpu.VMEM((KBLOCK, DH), bf16)],
            nk, per, ntiles,
        )
        outs_a.append(jnp.stack([att, dq], axis=1))
        outs_b.append(jnp.stack([dk, dv], axis=1))

    def send_back(parts):
        packed = jnp.stack(parts, axis=1).reshape(rows, heads_here * 2 * DH)
        back = lax.all_to_all(packed, "head", split_axis=0, concat_axis=1, tiled=True)
        back = back.reshape(rows_in, HEADS, 2, DH)
        return back[:, :, 0, :].reshape(rows_in, HEADS * DH), back[:, :, 1, :].reshape(rows_in, HEADS * DH)

    attended, grad_q = send_back(outs_a)
    grad_k, grad_v = send_back(outs_b)
    return attended, grad_q, grad_k, grad_v


def solution(mesh):
    placed = (
        P(("tm", "head"), None),
        P(("tm", "head"), None),
        P(("tm", "head"), None),
        P(("tm", "head"), None),
        P(),
    )
    return jax.shard_map(
        body,
        mesh=mesh,
        in_specs=placed,
        out_specs=(
            P(("tm", "head"), None),
            P(("tm", "head"), None),
            P(("tm", "head"), None),
            P(("tm", "head"), None),
        ),
        check_vma=False,
    )
```
